32 devices in a mesh: dp: 4 (over z), context: 8 (over y, x, core).
Axes of the slice: x: 2, y: 2, z: 4, core: 2. Of those that a mesh axis runs over, the one named last changes fastest.
Arguments:
- queries: bfloat16 [4, 1024, 4096], P('dp', 'context'), may hold values from -12 to 12
- key_rows: bfloat16 [4, 1024, 4096], P('dp', 'context'), may hold values from -12 to 12
- value_rows: bfloat16 [4, 1024, 4096], P('dp', 'context'), may hold values from -6 to 6
- cotangent: bfloat16 [4, 1024, 2048], P('dp', 'context'), may hold values from -6 to 6
- out_weight: bfloat16 [4096, 2048], P(('dp', 'context')), may hold values from -0.09375 to 0.09375
- random_blocks: int32 [4, 14, 3], P('dp'), may hold values from 1 to 14, as said below
Outputs:
- query_grad: bfloat16 [4, 1024, 4096], P('dp', 'context')
- key_grad: bfloat16 [4, 1024, 4096], P('dp', 'context')
- value_grad: bfloat16 [4, 1024, 4096], P('dp', 'context')
The draws below stay inside these ranges and needn't reach their ends.
Inputs may be any that keep to these rules, and one draw needn't show every extreme that they name: `random_blocks`: row j of a document holds three distinct block numbers, none of them j, j + 1 or j + 2.
All inputs are finite; a program needn't handle non-finite values.
Results may differ from the reference program's by a relative error of at most 0.012.
The reference program's roundings to bfloat16 on the way count: a program that leaves them out, or rounds other values in their place, can miss the bound.
Values may be sent and summed in bfloat16 or wider, within the bound.
No kernel may reach another device: no remote copies, remote signals or barrier semaphores. Data moves between devices by JAX's collectives and lax.ppermute only.
A program may use at most 192 MiB of HBM per device.

```python
import math
import jax
import jax.numpy as jnp
from jax import lax

D = 2048
HEADS = 32
HD = 128
BLOCK = 64
RAND = 3
DOCS = 4
SEQ = 1024
MID = 14


def attention_pair(key):
    shape = (DOCS, SEQ, HEADS * HD)
    first, second = jax.random.split(jax.random.fold_in(key, 17))
    drawn_q = jax.random.truncated_normal(first, -6.0, 6.0, shape, jnp.float32)
    drawn_k = jax.random.truncated_normal(second, -6.0, 6.0, shape, jnp.float32)
    return (drawn_q, drawn_k)


def draw_queries(key, part):
    return attention_pair(key)[0].astype(jnp.bfloat16)


def draw_key_rows(key, part):
    return attention_pair(key)[1].astype(jnp.bfloat16)


def draw_random_blocks(key, part):
    choices_count = MID - 3
    scores = jax.random.randint(jax.random.fold_in(key, 5), (DOCS, MID, choices_count), 0, 2 ** 20, jnp.int32) * choices_count + jnp.arange(choices_count, dtype=jnp.int32)
    picks = lax.top_k(scores, RAND)[1].astype(jnp.int32)
    row_ids = jnp.arange(MID, dtype=jnp.int32)[None, :, None]
    return (1 + (row_ids + 2 + picks) % MID).astype(jnp.int32)


def block_levels(rng, extent, pieces, low, largest):
    loudness, own = 1.0, jax.random.fold_in(rng, 6)
    for dim, shards_of in pieces:
        heights = jnp.exp(jax.random.uniform(jax.random.fold_in(own, dim), (shards_of,), jnp.float32, low / len(pieces), largest / len(pieces)))
        loudness = loudness * jnp.repeat(heights, extent[dim] // shards_of).reshape([-1 if axis == dim else 1 for axis in range(len(extent))])
    return loudness


def centred(stream_key, shape, scale, most, cuts=(), kind=jnp.bfloat16):
    values = jax.random.normal(stream_key, shape, jnp.float32) * scale
    if len(cuts) > 0:
        values = block_levels(stream_key, shape, cuts, -0.22, 0.18) * values
    return jnp.clip(values, min=-most, max=most).astype(kind)


def setup_inputs(seed: int = 0) -> dict:
    streams_of = jax.random.split(jax.random.key(seed), 7)
    queries = draw_queries(jax.random.fold_in(streams_of[6], 71), 0)
    key_rows = draw_key_rows(jax.random.fold_in(streams_of[6], 71), 0)
    value_rows = centred(streams_of[2], (DOCS, SEQ, HEADS * HD), 1.0, 6.0, ((0, 4), (1, 8)))
    cotangent = centred(streams_of[3], (DOCS, SEQ, D), 1.0, 6.0, ((0, 4), (1, 8)))
    out_weight = centred(streams_of[4], (HEADS * HD, D), (HEADS * HD) ** -0.5, 0.09375, ((0, 32),))
    random_blocks = draw_random_blocks(jax.random.fold_in(streams_of[6], 71), 0)
    return dict(queries=queries, key_rows=key_rows, value_rows=value_rows, cotangent=cotangent, out_weight=out_weight, random_blocks=random_blocks)


def head_grads(queries, key_rows, value_rows, upstream, random_ids):
    length, width = queries.shape
    count = length // BLOCK
    middle = count - 2
    factor = 1.0 / math.sqrt(width)
    query_f = queries.astype(jnp.float32)
    key_f = key_rows.astype(jnp.float32)
    value_f = value_rows.astype(jnp.float32)
    upstream_f = upstream.astype(jnp.float32)
    query_blocks = query_f.reshape(count, BLOCK, width)
    key_blocks = key_f.reshape(count, BLOCK, width)
    value_blocks = value_f.reshape(count, BLOCK, width)
    upstream_blocks = upstream_f.reshape(count, BLOCK, width)
    row_ids = jnp.arange(1, count - 1, dtype=jnp.int32)
    lower = row_ids - 1
    upper = row_ids + 1
    key_index = jnp.concatenate([jnp.zeros((middle, 1), jnp.int32), jnp.full((middle, 1), count - 1, jnp.int32), lower[:, None], row_ids[:, None], upper[:, None], random_ids.astype(jnp.int32)], axis=1)
    usable = jnp.concatenate([jnp.ones((middle, 2), jnp.bool_), (lower >= 1)[:, None], jnp.ones((middle, 1), jnp.bool_), (upper <= count - 2)[:, None], jnp.ones((middle, RAND), jnp.bool_)], axis=1)
    key_index = jnp.where(usable, key_index, row_ids[:, None])
    gathered_keys = key_blocks[key_index]
    gathered_values = value_blocks[key_index]
    mid_queries = query_blocks[1:count - 1]
    mid_upstream = upstream_blocks[1:count - 1]
    highest = lax.Precision.HIGHEST
    scores_mid = jnp.einsum('mqd,mjkd->mqjk', mid_queries, gathered_keys, precision=highest) * factor
    scores_mid = jnp.where(usable[:, None, :, None], scores_mid, -1e+30)
    top_mid = lax.optimization_barrier(jnp.max(scores_mid, axis=(2, 3), keepdims=True))
    expo_mid = jnp.exp(scores_mid - top_mid)
    weights_mid = expo_mid / lax.optimization_barrier(jnp.sum(expo_mid, axis=(2, 3), keepdims=True))
    rounded_mid = lax.optimization_barrier(weights_mid.astype(jnp.bfloat16)).astype(jnp.float32)
    attended = jnp.einsum('mqjk,mjkd->mqd', rounded_mid, gathered_values, precision=highest)
    row_term = lax.optimization_barrier(jnp.sum(mid_upstream * attended, axis=-1))
    grad_probs = jnp.einsum('mqd,mjkd->mqjk', mid_upstream, gathered_values, precision=highest)
    grad_scores = weights_mid * (grad_probs - row_term[:, :, None, None]) * factor
    grad_round = lax.optimization_barrier(grad_scores.astype(jnp.bfloat16)).astype(jnp.float32)
    mid_query_grad = jnp.einsum('mqjk,mjkd->mqd', grad_round, gathered_keys, precision=highest)
    key_terms = jnp.einsum('mqjk,mqd->mjkd', grad_round, mid_queries, precision=highest)
    value_terms = jnp.einsum('mqjk,mqd->mjkd', rounded_mid, mid_upstream, precision=highest)
    key_grad = jnp.zeros((count, BLOCK, width), jnp.float32).at[key_index].add(key_terms)
    value_grad = jnp.zeros((count, BLOCK, width), jnp.float32).at[key_index].add(value_terms)
    global_queries = jnp.concatenate([queries[:BLOCK], queries[length - BLOCK:]], axis=0)
    global_upstream = jnp.concatenate([upstream[:BLOCK], upstream[length - BLOCK:]], axis=0)
    scores_top = jnp.dot(global_queries, key_rows.T, preferred_element_type=jnp.float32) * factor
    top_top = lax.optimization_barrier(jnp.max(scores_top, axis=1, keepdims=True))
    expo_top = jnp.exp(scores_top - top_top)
    weights_top = expo_top / lax.optimization_barrier(jnp.sum(expo_top, axis=1, keepdims=True))
    rounded_top = weights_top.astype(jnp.bfloat16)
    attended_top = jnp.dot(rounded_top, value_rows, preferred_element_type=jnp.float32)
    row_top = lax.optimization_barrier(jnp.sum(global_upstream.astype(jnp.float32) * attended_top, axis=1))
    grad_top = jnp.dot(global_upstream, value_rows.T, preferred_element_type=jnp.float32)
    scores_grad_top = (weights_top * (grad_top - row_top[:, None]) * factor).astype(jnp.bfloat16)
    top_query_grad = jnp.dot(scores_grad_top, key_rows, preferred_element_type=jnp.float32)
    key_total = key_grad.reshape(length, width) + jnp.dot(scores_grad_top.T, global_queries, preferred_element_type=jnp.float32)
    value_total = value_grad.reshape(length, width) + jnp.dot(rounded_top.T, global_upstream, preferred_element_type=jnp.float32)
    query_total = jnp.concatenate([top_query_grad[:BLOCK], mid_query_grad.reshape(middle * BLOCK, width), top_query_grad[BLOCK:]], axis=0)
    return (query_total.astype(jnp.bfloat16), key_total.astype(jnp.bfloat16), value_total.astype(jnp.bfloat16))

def reference(queries, key_rows, value_rows, cotangent, out_weight, random_blocks):

    def one_document(items):
        doc_queries, doc_keys, doc_values, doc_cotangent, doc_random = items
        upstream = jnp.dot(doc_cotangent, out_weight.T, preferred_element_type=jnp.float32).astype(jnp.bfloat16)

        def one_head(head_id):
            start = head_id * HD

            def columns(array):
                return lax.dynamic_slice_in_dim(array, start, HD, 1)
            return head_grads(columns(doc_queries), columns(doc_keys), columns(doc_values), columns(upstream), doc_random)
        first, second, third = lax.map(one_head, jnp.arange(HEADS, dtype=jnp.int32))
        return (jnp.transpose(first, (1, 0, 2)).reshape(SEQ, HEADS * HD), jnp.transpose(second, (1, 0, 2)).reshape(SEQ, HEADS * HD), jnp.transpose(third, (1, 0, 2)).reshape(SEQ, HEADS * HD))
    query_grad, key_grad, value_grad = lax.map(one_document, (queries, key_rows, value_rows, cotangent, random_blocks))
    return (query_grad, key_grad, value_grad)
```

```python
import functools
import math

import jax
import jax.numpy as jnp
from jax import lax
from jax.experimental import pallas as pl
from jax.experimental.pallas import tpu as pltpu
from jax.sharding import PartitionSpec as P

HD = 128
BLOCK = 64
RAND = 3
SLOTS = 5 + RAND


def _nt(a, b):
    return lax.dot_general(a, b, (((1,), (1,)), ((), ())), preferred_element_type=jnp.float32)


def _tn(a, b):
    return lax.dot_general(a, b, (((0,), (0,)), ((), ())), preferred_element_type=jnp.float32)


def _nn(a, b):
    return lax.dot_general(a, b, (((1,), (0,)), ((), ())), preferred_element_type=jnp.float32)


def _attention_kernel(rb_ref, q_ref, k_ref, v_ref, u_ref, dq_ref, dk_ref, dv_ref,
                      dk_acc, dv_acc, kg_ref, vg_ref, *, length):
    count = length // BLOCK
    factor = 1.0 / math.sqrt(HD)

    def softmax_grads(qb, ub, keys, values, mask):
        scores = _nt(qb, keys) * factor
        if mask is not None:
            scores = jnp.where(mask, -1e30, scores)
        top = jnp.max(scores, axis=1, keepdims=True)
        expo = jnp.exp(scores - top)
        weights = expo * (1.0 / jnp.sum(expo, axis=1, keepdims=True))
        rounded = weights.astype(jnp.bfloat16)
        attended = _nn(rounded, values)
        row = jnp.sum(ub.astype(jnp.float32) * attended, axis=1, keepdims=True)
        grad_probs = _nt(ub, values)
        grad_scores = (weights * (grad_probs - row) * factor).astype(jnp.bfloat16)
        query_grad = _nn(grad_scores, keys)
        key_grad = _tn(grad_scores, qb)
        value_grad = _tn(rounded, ub)
        return query_grad, key_grad, value_grad

    keys_all = k_ref[...]
    values_all = v_ref[...]
    for index, start in enumerate((0, length - BLOCK)):
        qb = q_ref[start:start + BLOCK, :]
        ub = u_ref[start:start + BLOCK, :]
        query_grad, key_grad, value_grad = softmax_grads(qb, ub, keys_all, values_all, None)
        dq_ref[start:start + BLOCK, :] = query_grad.astype(jnp.bfloat16)
        if index == 0:
            dk_acc[...] = key_grad
            dv_acc[...] = value_grad
        else:
            dk_acc[...] += key_grad
            dv_acc[...] += value_grad

    columns = lax.broadcasted_iota(jnp.int32, (BLOCK, SLOTS * BLOCK), 1) // BLOCK

    def mid_step(m, carry):
        base = (m - 1) * RAND
        lower = jnp.where(m - 1 >= 1, m - 1, m)
        upper = jnp.where(m + 1 <= count - 2, m + 1, m)
        ids = [0, count - 1, lower, m, upper] + [rb_ref[base + r] for r in range(RAND)]
        for slot, block in enumerate(ids):
            row = pl.multiple_of(block * BLOCK, BLOCK)
            kg_ref[slot * BLOCK:(slot + 1) * BLOCK, :] = k_ref[pl.ds(row, BLOCK), :]
            vg_ref[slot * BLOCK:(slot + 1) * BLOCK, :] = v_ref[pl.ds(row, BLOCK), :]
        start = pl.multiple_of(m * BLOCK, BLOCK)
        qb = q_ref[pl.ds(start, BLOCK), :]
        ub = u_ref[pl.ds(start, BLOCK), :]
        mask = ((columns == 2) & (m == 1)) | ((columns == 4) & (m == count - 2))
        query_grad, key_grad, value_grad = softmax_grads(qb, ub, kg_ref[...], vg_ref[...], mask)
        dq_ref[pl.ds(start, BLOCK), :] = query_grad.astype(jnp.bfloat16)
        for slot, block in enumerate(ids):
            row = pl.multiple_of(block * BLOCK, BLOCK)
            dk_acc[pl.ds(row, BLOCK), :] += key_grad[slot * BLOCK:(slot + 1) * BLOCK, :]
            dv_acc[pl.ds(row, BLOCK), :] += value_grad[slot * BLOCK:(slot + 1) * BLOCK, :]
        return carry

    lax.fori_loop(1, count - 1, mid_step, 0)
    dk_ref[...] = dk_acc[...].astype(jnp.bfloat16)
    dv_ref[...] = dv_acc[...].astype(jnp.bfloat16)


def attention_grads(queries, key_rows, value_rows, upstream, random_ids):
    length, width = queries.shape
    heads = width // HD
    spec = pl.BlockSpec((length, HD), lambda h, rb: (0, h))
    out = jax.ShapeDtypeStruct((length, width), jnp.bfloat16)
    return pl.pallas_call(
        functools.partial(_attention_kernel, length=length),
        out_shape=(out, out, out),
        grid_spec=pltpu.PrefetchScalarGridSpec(
            num_scalar_prefetch=1,
            grid=(heads,),
            in_specs=[spec, spec, spec, spec],
            out_specs=[spec, spec, spec],
            scratch_shapes=[
                pltpu.VMEM((length, HD), jnp.float32),
                pltpu.VMEM((length, HD), jnp.float32),
                pltpu.VMEM((SLOTS * BLOCK, HD), jnp.bfloat16),
                pltpu.VMEM((SLOTS * BLOCK, HD), jnp.bfloat16),
            ],
        ),
        compiler_params=pltpu.CompilerParams(dimension_semantics=("arbitrary",)),
    )(random_ids.reshape(-1), queries, key_rows, value_rows, upstream)


def body(queries, key_rows, value_rows, cotangent, out_weight, random_blocks):
    dp = lax.axis_size("dp")
    ctx = lax.axis_size("context")
    local_queries = queries[0]
    local_keys = key_rows[0]
    local_values = value_rows[0]
    local_cotangent = cotangent[0]
    tokens, width = local_queries.shape
    total_heads = width // HD
    rows_per_device = out_weight.shape[0]
    strided = rows_per_device == HD and total_heads == dp * ctx

    if strided:
        head_weight = lax.all_gather(out_weight, "dp", axis=0, tiled=True)
        full_cotangent = lax.all_gather(local_cotangent, "context", axis=0, tiled=True)
        upstream = lax.dot_general(
            full_cotangent, head_weight, (((1,), (1,)), ((), ())),
            preferred_element_type=jnp.float32,
        ).astype(jnp.bfloat16)

        def send(array):
            split = array.reshape(tokens, dp, ctx, HD)
            moved = lax.all_to_all(split, "context", split_axis=2, concat_axis=0, tiled=True)
            return moved.reshape(tokens * ctx, dp * HD)

        def back(array):
            split = array.reshape(tokens * ctx, dp, 1, HD)
            moved = lax.all_to_all(split, "context", split_axis=0, concat_axis=2, tiled=True)
            return moved.reshape(tokens, width)

        head_upstream = upstream
    else:
        upstream = lax.dot_general(
            local_cotangent,
            lax.all_gather(out_weight, ("dp", "context"), axis=0, tiled=True),
            (((1,), (1,)), ((), ())),
            preferred_element_type=jnp.float32,
        ).astype(jnp.bfloat16)

        def send(array):
            return lax.all_to_all(array, "context", split_axis=1, concat_axis=0, tiled=True)

        def back(array):
            return lax.all_to_all(array, "context", split_axis=0, concat_axis=1, tiled=True)

        head_upstream = send(upstream)

    grads = attention_grads(
        send(local_queries), send(local_keys), send(local_values), head_upstream,
        random_blocks[0],
    )
    return tuple(back(grad)[None] for grad in grads)


def solution(mesh):
    return jax.shard_map(
        body,
        mesh=mesh,
        in_specs=(
            P("dp", "context", None),
            P("dp", "context", None),
            P("dp", "context", None),
            P("dp", "context", None),
            P(("dp", "context"), None),
            P("dp", None, None),
        ),
        out_specs=(P("dp", "context", None), P("dp", "context", None), P("dp", "context", None)),
        check_vma=False,
    )
```

```python
import functools
import math

import jax
import jax.numpy as jnp
from jax import lax
from jax.experimental import pallas as pl
from jax.experimental.pallas import tpu as pltpu
from jax.sharding import PartitionSpec as P

HD = 128
BLOCK = 64
RAND = 3
SLOTS = 5 + RAND


def _nt(a, b):
    return lax.dot_general(a, b, (((1,), (1,)), ((), ())), preferred_element_type=jnp.float32)


def _tn(a, b):
    return lax.dot_general(a, b, (((0,), (0,)), ((), ())), preferred_element_type=jnp.float32)


def _nn(a, b):
    return lax.dot_general(a, b, (((1,), (0,)), ((), ())), preferred_element_type=jnp.float32)


def _attention_kernel(rb_ref, x_ref, u_ref, o_ref, dk_acc, dv_acc, kg_ref, vg_ref, *, length):
    count = length // BLOCK
    q_ref, k_ref, v_ref = (x_ref.at[:, i * HD:(i + 1) * HD] for i in range(3))
    dq_ref, dk_ref, dv_ref = (o_ref.at[:, i * HD:(i + 1) * HD] for i in range(3))
    factor = 1.0 / math.sqrt(HD)

    def softmax_grads(qb, ub, keys, values, mask):
        scores = _nt(qb, keys) * factor
        if mask is not None:
            scores = jnp.where(mask, -1e30, scores)
        top = jnp.max(scores, axis=1, keepdims=True)
        expo = jnp.exp(scores - top)
        weights = expo * (1.0 / jnp.sum(expo, axis=1, keepdims=True))
        rounded = weights.astype(jnp.bfloat16)
        attended = _nn(rounded, values)
        row = jnp.sum(ub.astype(jnp.float32) * attended, axis=1, keepdims=True)
        grad_probs = _nt(ub, values)
        grad_scores = (weights * (grad_probs - row) * factor).astype(jnp.bfloat16)
        query_grad = _nn(grad_scores, keys)
        key_grad = _tn(grad_scores, qb)
        value_grad = _tn(rounded, ub)
        return query_grad, key_grad, value_grad

    keys_all = k_ref[...]
    values_all = v_ref[...]
    for index, start in enumerate((0, length - BLOCK)):
        qb = q_ref[start:start + BLOCK, :]
        ub = u_ref[start:start + BLOCK, :]
        query_grad, key_grad, value_grad = softmax_grads(qb, ub, keys_all, values_all, None)
        dq_ref[start:start + BLOCK, :] = query_grad.astype(jnp.bfloat16)
        if index == 0:
            dk_acc[...] = key_grad
            dv_acc[...] = value_grad
        else:
            dk_acc[...] += key_grad
            dv_acc[...] += value_grad

    columns = lax.broadcasted_iota(jnp.int32, (BLOCK, SLOTS * BLOCK), 1) // BLOCK

    def mid_step(m, carry):
        base = (m - 1) * RAND
        lower = jnp.where(m - 1 >= 1, m - 1, m)
        upper = jnp.where(m + 1 <= count - 2, m + 1, m)
        ids = [0, count - 1, lower, m, upper] + [rb_ref[base + r] for r in range(RAND)]
        for slot, block in enumerate(ids):
            row = pl.multiple_of(block * BLOCK, BLOCK)
            kg_ref[slot * BLOCK:(slot + 1) * BLOCK, :] = k_ref[pl.ds(row, BLOCK), :]
            vg_ref[slot * BLOCK:(slot + 1) * BLOCK, :] = v_ref[pl.ds(row, BLOCK), :]
        start = pl.multiple_of(m * BLOCK, BLOCK)
        qb = q_ref[pl.ds(start, BLOCK), :]
        ub = u_ref[pl.ds(start, BLOCK), :]
        mask = ((columns == 2) & (m == 1)) | ((columns == 4) & (m == count - 2))
        query_grad, key_grad, value_grad = softmax_grads(qb, ub, kg_ref[...], vg_ref[...], mask)
        dq_ref[pl.ds(start, BLOCK), :] = query_grad.astype(jnp.bfloat16)
        for slot, block in enumerate(ids):
            row = pl.multiple_of(block * BLOCK, BLOCK)
            dk_acc[pl.ds(row, BLOCK), :] += key_grad[slot * BLOCK:(slot + 1) * BLOCK, :]
            dv_acc[pl.ds(row, BLOCK), :] += value_grad[slot * BLOCK:(slot + 1) * BLOCK, :]
        return carry

    lax.fori_loop(1, count - 1, mid_step, 0)
    dk_ref[...] = dk_acc[...].astype(jnp.bfloat16)
    dv_ref[...] = dv_acc[...].astype(jnp.bfloat16)


def attention_grads(stacked, upstream, random_ids):
    length = stacked.shape[0]
    count = length // BLOCK
    spec = pl.BlockSpec((length, HD), lambda h, rb: (0, h))
    whole = pl.BlockSpec((length, 3 * HD), lambda h, rb: (0, 0))
    out = jax.ShapeDtypeStruct((length, 3 * HD), jnp.bfloat16)
    pairs = 2 * BLOCK * length + (count - 2) * BLOCK * SLOTS * BLOCK
    cost = pl.CostEstimate(
        flops=12 * pairs * HD, transcendentals=pairs, bytes_accessed=14 * length * HD
    )
    return pl.pallas_call(
        functools.partial(_attention_kernel, length=length),
        out_shape=out,
        grid_spec=pltpu.PrefetchScalarGridSpec(
            num_scalar_prefetch=1,
            grid=(1,),
            in_specs=[whole, spec],
            out_specs=whole,
            scratch_shapes=[
                pltpu.VMEM((length, HD), jnp.float32),
                pltpu.VMEM((length, HD), jnp.float32),
                pltpu.VMEM((SLOTS * BLOCK, HD), jnp.bfloat16),
                pltpu.VMEM((SLOTS * BLOCK, HD), jnp.bfloat16),
            ],
        ),
        compiler_params=pltpu.CompilerParams(dimension_semantics=("arbitrary",)),
        cost_estimate=cost,
    )(random_ids.reshape(-1), stacked, upstream)


def body(queries, key_rows, value_rows, cotangent, out_weight, random_blocks):
    dp = lax.axis_size("dp")
    ctx = lax.axis_size("context")
    local = (queries[0], key_rows[0], value_rows[0])
    local_cotangent = cotangent[0]
    tokens, width = local[0].shape
    total_heads = width // HD
    local_heads = total_heads // ctx
    rows_per_device = out_weight.shape[0]
    strided = rows_per_device == HD and local_heads == dp

    if strided:
        head_weight = lax.all_gather(out_weight, "dp", axis=0, tiled=True)
        full_cotangent = lax.all_gather(local_cotangent, "context", axis=0, tiled=True)

        def chunk(array, c):
            return array.reshape(tokens, dp, ctx, HD)[:, c]
    else:
        upstream = lax.dot_general(
            local_cotangent,
            lax.all_gather(out_weight, ("dp", "context"), axis=0, tiled=True),
            (((1,), (1,)), ((), ())),
            preferred_element_type=jnp.float32,
        ).astype(jnp.bfloat16)
        local = local + (upstream,)

        def chunk(array, c):
            return array.reshape(tokens, ctx, local_heads, HD)[:, :, c]

    pieces = []
    for c in range(local_heads):
        stacked = jnp.stack([chunk(array, c) for array in local], axis=1)
        moved = lax.all_to_all(stacked, "context", split_axis=2, concat_axis=0, tiled=True)
        moved = moved.reshape(tokens * ctx, len(local) * HD)
        if strided:
            head_upstream = lax.dot_general(
                full_cotangent, head_weight[c * HD:(c + 1) * HD], (((1,), (1,)), ((), ())),
                preferred_element_type=jnp.float32,
            ).astype(jnp.bfloat16)
        else:
            head_upstream = moved[:, 3 * HD:]
        grads = attention_grads(moved[:, :3 * HD], head_upstream, random_blocks[0])
        grads = grads.reshape(tokens * ctx, 3, 1, HD)
        pieces.append(lax.all_to_all(grads, "context", split_axis=0, concat_axis=2, tiled=True))

    outs = []
    for g in range(3):
        parts = [piece[:, g] for piece in pieces]
        joined = jnp.stack(parts, axis=1 if strided else 2)
        outs.append(joined.reshape(1, tokens, width))
    return tuple(outs)


def solution(mesh):
    return jax.shard_map(
        body,
        mesh=mesh,
        in_specs=(
            P("dp", "context", None),
            P("dp", "context", None),
            P("dp", "context", None),
            P("dp", "context", None),
            P(("dp", "context"), None),
            P("dp", None, None),
        ),
        out_specs=(P("dp", "context", None), P("dp", "context", None), P("dp", "context", None)),
        check_vma=False,
    )
```

```python
import functools
import math

import jax
import jax.numpy as jnp
from jax import lax
from jax.experimental import pallas as pl
from jax.experimental.pallas import tpu as pltpu
from jax.sharding import PartitionSpec as P

HD = 128
BLOCK = 64
RAND = 3
SLOTS = 5 + RAND


def _nt(a, b):
    return lax.dot_general(a, b, (((1,), (1,)), ((), ())), preferred_element_type=jnp.float32)


def _tn(a, b):
    return lax.dot_general(a, b, (((0,), (0,)), ((), ())), preferred_element_type=jnp.float32)


def _nn(a, b):
    return lax.dot_general(a, b, (((1,), (0,)), ((), ())), preferred_element_type=jnp.float32)


def _attention_kernel(rb_ref, x_ref, u_ref, o_ref, dk_acc, dv_acc, kg_ref, vg_ref):
    parts, _, tokens, _ = x_ref.shape
    per_part = tokens // BLOCK
    length = parts * tokens
    count = length // BLOCK
    factor = 1.0 / math.sqrt(HD)

    def rows(ref, which, block):
        if isinstance(block, int):
            offset = (block % per_part) * BLOCK
        else:
            offset = pl.multiple_of((block % per_part) * BLOCK, BLOCK)
        return ref.at[block // per_part, which, pl.ds(offset, BLOCK), :]

    def softmax_grads(qb, ub, keys, values, mask):
        scores = _nt(qb, keys) * factor
        if mask is not None:
            scores = jnp.where(mask, -1e30, scores)
        top = jnp.max(scores, axis=1, keepdims=True)
        expo = jnp.exp(scores - top)
        weights = expo * (1.0 / jnp.sum(expo, axis=1, keepdims=True))
        rounded = weights.astype(jnp.bfloat16)
        attended = _nn(rounded, values)
        row = jnp.sum(ub.astype(jnp.float32) * attended, axis=1, keepdims=True)
        grad_probs = _nt(ub, values)
        grad_scores = (weights * (grad_probs - row) * factor).astype(jnp.bfloat16)
        query_grad = _nn(grad_scores, keys)
        key_grad = _tn(grad_scores, qb)
        value_grad = _tn(rounded, ub)
        return query_grad, key_grad, value_grad

    keys_all = x_ref[:, 1, :, :].reshape(length, HD)
    values_all = x_ref[:, 2, :, :].reshape(length, HD)
    for index, block in enumerate((0, count - 1)):
        qb = rows(x_ref, 0, block)[...]
        ub = u_ref[block * BLOCK:(block + 1) * BLOCK, :]
        query_grad, key_grad, value_grad = softmax_grads(qb, ub, keys_all, values_all, None)
        rows(o_ref, 0, block)[...] = query_grad.astype(jnp.bfloat16)
        if index == 0:
            dk_acc[...] = key_grad
            dv_acc[...] = value_grad
        else:
            dk_acc[...] += key_grad
            dv_acc[...] += value_grad

    columns = lax.broadcasted_iota(jnp.int32, (BLOCK, SLOTS * BLOCK), 1) // BLOCK

    def mid_step(m, carry):
        base = (m - 1) * RAND
        lower = jnp.where(m - 1 >= 1, m - 1, m)
        upper = jnp.where(m + 1 <= count - 2, m + 1, m)
        ids = [0, count - 1, lower, m, upper] + [rb_ref[base + r] for r in range(RAND)]
        for slot, block in enumerate(ids):
            kg_ref[slot * BLOCK:(slot + 1) * BLOCK, :] = rows(x_ref, 1, block)[...]
            vg_ref[slot * BLOCK:(slot + 1) * BLOCK, :] = rows(x_ref, 2, block)[...]
        start = pl.multiple_of(m * BLOCK, BLOCK)
        qb = rows(x_ref, 0, m)[...]
        ub = u_ref[pl.ds(start, BLOCK), :]
        mask = ((columns == 2) & (m == 1)) | ((columns == 4) & (m == count - 2))
        query_grad, key_grad, value_grad = softmax_grads(qb, ub, kg_ref[...], vg_ref[...], mask)
        rows(o_ref, 0, m)[...] = query_grad.astype(jnp.bfloat16)
        for slot, block in enumerate(ids):
            row = pl.multiple_of(block * BLOCK, BLOCK)
            dk_acc[pl.ds(row, BLOCK), :] += key_grad[slot * BLOCK:(slot + 1) * BLOCK, :]
            dv_acc[pl.ds(row, BLOCK), :] += value_grad[slot * BLOCK:(slot + 1) * BLOCK, :]
        return carry

    lax.fori_loop(1, count - 1, mid_step, 0)
    o_ref[:, 1, :, :] = dk_acc[...].reshape(parts, tokens, HD).astype(jnp.bfloat16)
    o_ref[:, 2, :, :] = dv_acc[...].reshape(parts, tokens, HD).astype(jnp.bfloat16)


def attention_grads(stacked, upstream, head, random_ids):
    parts, _, tokens, _ = stacked.shape
    length = parts * tokens
    count = length // BLOCK
    whole = pl.BlockSpec((parts, 3, tokens, HD), lambda h, rb: (0, 0, 0, 0))
    spec = pl.BlockSpec((length, HD), lambda h, rb: (0, head))
    out = jax.ShapeDtypeStruct((parts, 3, tokens, HD), jnp.bfloat16)
    pairs = 2 * BLOCK * length + (count - 2) * BLOCK * SLOTS * BLOCK
    cost = pl.CostEstimate(
        flops=12 * pairs * HD, transcendentals=pairs, bytes_accessed=14 * length * HD
    )
    return pl.pallas_call(
        _attention_kernel,
        out_shape=out,
        grid_spec=pltpu.PrefetchScalarGridSpec(
            num_scalar_prefetch=1,
            grid=(1,),
            in_specs=[whole, spec],
            out_specs=whole,
            scratch_shapes=[
                pltpu.VMEM((length, HD), jnp.float32),
                pltpu.VMEM((length, HD), jnp.float32),
                pltpu.VMEM((SLOTS * BLOCK, HD), jnp.bfloat16),
                pltpu.VMEM((SLOTS * BLOCK, HD), jnp.bfloat16),
            ],
        ),
        compiler_params=pltpu.CompilerParams(dimension_semantics=("arbitrary",)),
        cost_estimate=cost,
    )(random_ids.reshape(-1), stacked, upstream)


def body(queries, key_rows, value_rows, cotangent, out_weight, random_blocks):
    dp = lax.axis_size("dp")
    ctx = lax.axis_size("context")
    local = (queries[0], key_rows[0], value_rows[0])
    local_cotangent = cotangent[0]
    tokens, width = local[0].shape
    total_heads = width // HD
    local_heads = total_heads // ctx
    rows_per_device = out_weight.shape[0]
    strided = rows_per_device == HD and local_heads == dp

    if strided:
        head_weight = lax.all_gather(out_weight, "dp", axis=0, tiled=True)
        full_cotangent = lax.all_gather(local_cotangent, "context", axis=0, tiled=True)
        upstream = lax.dot_general(
            full_cotangent, head_weight, (((1,), (1,)), ((), ())),
            preferred_element_type=jnp.float32,
        ).astype(jnp.bfloat16)

        def chunk(array, c):
            return array.reshape(tokens, dp, ctx, HD)[:, c]
    else:
        upstream = lax.dot_general(
            local_cotangent,
            lax.all_gather(out_weight, ("dp", "context"), axis=0, tiled=True),
            (((1,), (1,)), ((), ())),
            preferred_element_type=jnp.float32,
        ).astype(jnp.bfloat16)
        local = local + (upstream,)

        def chunk(array, c):
            return array.reshape(tokens, ctx, local_heads, HD)[:, :, c]

    pieces = []
    for c in range(local_heads):
        stacked = jnp.stack([chunk(array, c).transpose(1, 0, 2) for array in local], axis=1)
        moved = lax.all_to_all(stacked, "context", split_axis=0, concat_axis=0, tiled=True)
        if strided:
            grads = attention_grads(moved, upstream, c, random_blocks[0])
        else:
            head_upstream = moved[:, 3].reshape(tokens * ctx, HD)
            grads = attention_grads(moved[:, :3], head_upstream, 0, random_blocks[0])
        back = lax.all_to_all(grads, "context", split_axis=0, concat_axis=0, tiled=True)
        pieces.append(back.transpose(1, 2, 0, 3))

    outs = []
    for g in range(3):
        joined = jnp.stack([piece[g] for piece in pieces], axis=1 if strided else 2)
        outs.append(joined.reshape(1, tokens, width))
    return tuple(outs)


def solution(mesh):
    return jax.shard_map(
        body,
        mesh=mesh,
        in_specs=(
            P("dp", "context", None),
            P("dp", "context", None),
            P("dp", "context", None),
            P("dp", "context", None),
            P(("dp", "context"), None),
            P("dp", None, None),
        ),
        out_specs=(P("dp", "context", None), P("dp", "context", None), P("dp", "context", None)),
        check_vma=False,
    )
```

```python
import functools
import math

import jax
import jax.numpy as jnp
from jax import lax
from jax.experimental import pallas as pl
from jax.experimental.pallas import tpu as pltpu
from jax.sharding import PartitionSpec as P

HD = 128
BLOCK = 64
RAND = 3
SLOTS = 5 + RAND


def _nt(a, b):
    return lax.dot_general(a, b, (((1,), (1,)), ((), ())), preferred_element_type=jnp.float32)


def _tn(a, b):
    return lax.dot_general(a, b, (((0,), (0,)), ((), ())), preferred_element_type=jnp.float32)


def _nn(a, b):
    return lax.dot_general(a, b, (((1,), (0,)), ((), ())), preferred_element_type=jnp.float32)


def _attention_kernel(rb_ref, x_ref, u_ref, o_ref, dk_acc, dv_acc, kg_ref, vg_ref):
    parts, _, tokens, _ = x_ref.shape
    per_part = tokens // BLOCK
    length = parts * tokens
    count = length // BLOCK
    factor = 1.0 / math.sqrt(HD)

    def rows(ref, which, block):
        if isinstance(block, int):
            offset = (block % per_part) * BLOCK
        else:
            offset = pl.multiple_of((block % per_part) * BLOCK, BLOCK)
        return ref.at[block // per_part, which, pl.ds(offset, BLOCK), :]

    def softmax_grads(qb, ub, keys, values, mask):
        scores = _nt(qb, keys) * factor
        if mask is not None:
            scores = jnp.where(mask, -1e30, scores)
        top = jnp.max(scores, axis=1, keepdims=True)
        expo = jnp.exp(scores - top)
        weights = expo * (1.0 / jnp.sum(expo, axis=1, keepdims=True))
        rounded = weights.astype(jnp.bfloat16)
        attended = _nn(rounded, values)
        row = jnp.sum(ub.astype(jnp.float32) * attended, axis=1, keepdims=True)
        grad_probs = _nt(ub, values)
        grad_scores = (weights * (grad_probs - row) * factor).astype(jnp.bfloat16)
        query_grad = _nn(grad_scores, keys)
        key_grad = _tn(grad_scores, qb)
        value_grad = _tn(rounded, ub)
        return query_grad, key_grad, value_grad

    keys_all = x_ref[:, 1, :, :].reshape(length, HD)
    values_all = x_ref[:, 2, :, :].reshape(length, HD)
    for index, block in enumerate((0, count - 1)):
        qb = rows(x_ref, 0, block)[...]
        ub = u_ref[block * BLOCK:(block + 1) * BLOCK, :]
        query_grad, key_grad, value_grad = softmax_grads(qb, ub, keys_all, values_all, None)
        rows(o_ref, 0, block)[...] = query_grad.astype(jnp.bfloat16)
        if index == 0:
            dk_acc[...] = key_grad
            dv_acc[...] = value_grad
        else:
            dk_acc[...] += key_grad
            dv_acc[...] += value_grad

    columns = lax.broadcasted_iota(jnp.int32, (BLOCK, SLOTS * BLOCK), 1) // BLOCK

    def mid_step(m, carry):
        base = (m - 1) * RAND
        lower = jnp.where(m - 1 >= 1, m - 1, m)
        upper = jnp.where(m + 1 <= count - 2, m + 1, m)
        ids = [0, count - 1, lower, m, upper] + [rb_ref[base + r] for r in range(RAND)]
        for slot, block in enumerate(ids):
            kg_ref[slot * BLOCK:(slot + 1) * BLOCK, :] = rows(x_ref, 1, block)[...]
            vg_ref[slot * BLOCK:(slot + 1) * BLOCK, :] = rows(x_ref, 2, block)[...]
        start = pl.multiple_of(m * BLOCK, BLOCK)
        qb = rows(x_ref, 0, m)[...]
        ub = u_ref[pl.ds(start, BLOCK), :]
        mask = ((columns == 2) & (m == 1)) | ((columns == 4) & (m == count - 2))
        query_grad, key_grad, value_grad = softmax_grads(qb, ub, kg_ref[...], vg_ref[...], mask)
        rows(o_ref, 0, m)[...] = query_grad.astype(jnp.bfloat16)
        for slot, block in enumerate(ids):
            row = pl.multiple_of(block * BLOCK, BLOCK)
            dk_acc[pl.ds(row, BLOCK), :] += key_grad[slot * BLOCK:(slot + 1) * BLOCK, :]
            dv_acc[pl.ds(row, BLOCK), :] += value_grad[slot * BLOCK:(slot + 1) * BLOCK, :]
        return carry

    lax.fori_loop(1, count - 1, mid_step, 0, unroll=2)
    o_ref[:, 1, :, :] = dk_acc[...].reshape(parts, tokens, HD).astype(jnp.bfloat16)
    o_ref[:, 2, :, :] = dv_acc[...].reshape(parts, tokens, HD).astype(jnp.bfloat16)


def attention_grads(stacked, upstream, head, random_ids):
    parts, _, tokens, _ = stacked.shape
    length = parts * tokens
    count = length // BLOCK
    whole = pl.BlockSpec((parts, 3, tokens, HD), lambda h, rb: (0, 0, 0, 0))
    spec = pl.BlockSpec((length, HD), lambda h, rb: (0, head))
    out = jax.ShapeDtypeStruct((parts, 3, tokens, HD), jnp.bfloat16)
    pairs = 2 * BLOCK * length + (count - 2) * BLOCK * SLOTS * BLOCK
    cost = pl.CostEstimate(
        flops=12 * pairs * HD, transcendentals=pairs, bytes_accessed=14 * length * HD
    )
    return pl.pallas_call(
        _attention_kernel,
        out_shape=out,
        grid_spec=pltpu.PrefetchScalarGridSpec(
            num_scalar_prefetch=1,
            grid=(1,),
            in_specs=[whole, spec],
            out_specs=whole,
            scratch_shapes=[
                pltpu.VMEM((length, HD), jnp.float32),
                pltpu.VMEM((length, HD), jnp.float32),
                pltpu.VMEM((SLOTS * BLOCK, HD), jnp.bfloat16),
                pltpu.VMEM((SLOTS * BLOCK, HD), jnp.bfloat16),
            ],
        ),
        compiler_params=pltpu.CompilerParams(dimension_semantics=("arbitrary",)),
        cost_estimate=cost,
    )(random_ids.reshape(-1), stacked, upstream)


def body(queries, key_rows, value_rows, cotangent, out_weight, random_blocks):
    dp = lax.axis_size("dp")
    ctx = lax.axis_size("context")
    local = (queries[0], key_rows[0], value_rows[0])
    local_cotangent = cotangent[0]
    tokens, width = local[0].shape
    total_heads = width // HD
    local_heads = total_heads // ctx
    rows_per_device = out_weight.shape[0]
    strided = rows_per_device == HD and local_heads == dp and ctx % 2 == 0

    if strided:
        me = lax.axis_index("dp")
        got = [out_weight] + [
            lax.ppermute(out_weight, "dp", [(a, (a + s) % dp) for a in range(dp)])
            for s in range(1, dp)
        ]
        order = (me - jnp.arange(dp)) % dp
        head_weight = jnp.take(jnp.stack(got), order, axis=0).reshape(dp * HD, -1)
        j = lax.axis_index("context")
        shifts = list(range(0, ctx, 2))
        mine = jnp.stack([local_cotangent] + [
            lax.ppermute(local_cotangent, "context", [(a, (a + s) % ctx) for a in range(ctx)])
            for s in shifts[1:]
        ])
        other = lax.ppermute(mine, "context", [(a, a ^ 1) for a in range(ctx)])
        gathered = jnp.concatenate([mine, other]).reshape(ctx * tokens, -1)
        upstream = lax.dot_general(
            gathered, head_weight, (((1,), (1,)), ((), ())),
            preferred_element_type=jnp.float32,
        ).astype(jnp.bfloat16)
        source = jnp.arange(ctx)
        same = source % 2 == j % 2
        position = jnp.where(
            same, ((j - source) % ctx) // 2, ctx // 2 + (((j ^ 1) - source) % ctx) // 2
        )
        upstream = jnp.take(upstream.reshape(ctx, tokens, -1), position, axis=0)
        upstream = upstream.reshape(ctx * tokens, -1)

        def chunk(array, c):
            return array.reshape(tokens, dp, ctx, HD)[:, c]
    else:
        upstream = lax.dot_general(
            local_cotangent,
            lax.all_gather(out_weight, ("dp", "context"), axis=0, tiled=True),
            (((1,), (1,)), ((), ())),
            preferred_element_type=jnp.float32,
        ).astype(jnp.bfloat16)
        local = local + (upstream,)

        def chunk(array, c):
            return array.reshape(tokens, ctx, local_heads, HD)[:, :, c]

    pieces = []
    for c in range(local_heads):
        stacked = jnp.stack([chunk(array, c).transpose(1, 0, 2) for array in local], axis=1)
        moved = lax.all_to_all(stacked, "context", split_axis=0, concat_axis=0, tiled=True)
        if strided:
            grads = attention_grads(moved, upstream, c, random_blocks[0])
        else:
            head_upstream = moved[:, 3].reshape(tokens * ctx, HD)
            grads = attention_grads(moved[:, :3], head_upstream, 0, random_blocks[0])
        back = lax.all_to_all(grads, "context", split_axis=0, concat_axis=0, tiled=True)
        pieces.append(back.transpose(1, 2, 0, 3))

    outs = []
    for g in range(3):
        joined = jnp.stack([piece[g] for piece in pieces], axis=1 if strided else 2)
        outs.append(joined.reshape(1, tokens, width))
    return tuple(outs)


def solution(mesh):
    return jax.shard_map(
        body,
        mesh=mesh,
        in_specs=(
            P("dp", "context", None),
            P("dp", "context", None),
            P("dp", "context", None),
            P("dp", "context", None),
            P(("dp", "context"), None),
            P("dp", None, None),
        ),
        out_specs=(P("dp", "context", None), P("dp", "context", None), P("dp", "context", None)),
        check_vma=False,
    )
```

```python
import functools
import math

import jax
import jax.numpy as jnp
from jax import lax
from jax.experimental import pallas as pl
from jax.experimental.pallas import tpu as pltpu
from jax.sharding import PartitionSpec as P

HD = 128
BLOCK = 64
RAND = 3
SLOTS = 5 + RAND


def _nt(a, b):
    return lax.dot_general(a, b, (((1,), (1,)), ((), ())), preferred_element_type=jnp.float32)


def _tn(a, b):
    return lax.dot_general(a, b, (((0,), (0,)), ((), ())), preferred_element_type=jnp.float32)


def _nn(a, b):
    return lax.dot_general(a, b, (((1,), (0,)), ((), ())), preferred_element_type=jnp.float32)


def _attention_kernel(rb_ref, x_ref, u_ref, o_ref, dk_acc, dv_acc, kg_ref, vg_ref):
    parts, _, tokens, _ = x_ref.shape
    per_part = tokens // BLOCK
    length = parts * tokens
    count = length // BLOCK
    factor = 1.0 / math.sqrt(HD)

    def rows(ref, which, block):
        if isinstance(block, int):
            offset = (block % per_part) * BLOCK
        else:
            offset = pl.multiple_of((block % per_part) * BLOCK, BLOCK)
        return ref.at[block // per_part, which, pl.ds(offset, BLOCK), :]

    def softmax_grads(qb, ub, keys, values, mask):
        scores = _nt(qb, keys) * factor
        if mask is not None:
            scores = jnp.where(mask, -1e30, scores)
        top = jnp.max(scores, axis=1, keepdims=True)
        expo = jnp.exp(scores - top)
        weights = expo * (1.0 / jnp.sum(expo, axis=1, keepdims=True))
        rounded = weights.astype(jnp.bfloat16)
        attended = _nn(rounded, values)
        row = jnp.sum(ub.astype(jnp.float32) * attended, axis=1, keepdims=True)
        grad_probs = _nt(ub, values)
        grad_scores = (weights * (grad_probs - row) * factor).astype(jnp.bfloat16)
        query_grad = _nn(grad_scores, keys)
        key_grad = _tn(grad_scores, qb)
        value_grad = _tn(rounded, ub)
        return query_grad, key_grad, value_grad

    keys_all = x_ref[:, 1, :, :].reshape(length, HD)
    values_all = x_ref[:, 2, :, :].reshape(length, HD)
    for index, block in enumerate((0, count - 1)):
        qb = rows(x_ref, 0, block)[...]
        ub = u_ref[block * BLOCK:(block + 1) * BLOCK, :]
        query_grad, key_grad, value_grad = softmax_grads(qb, ub, keys_all, values_all, None)
        rows(o_ref, 0, block)[...] = query_grad.astype(jnp.bfloat16)
        if index == 0:
            dk_acc[...] = key_grad
            dv_acc[...] = value_grad
        else:
            dk_acc[...] += key_grad
            dv_acc[...] += value_grad

    columns = lax.broadcasted_iota(jnp.int32, (BLOCK, SLOTS * BLOCK), 1) // BLOCK

    def mid_step(m, carry):
        base = (m - 1) * RAND
        lower = jnp.where(m - 1 >= 1, m - 1, m)
        upper = jnp.where(m + 1 <= count - 2, m + 1, m)
        ids = [0, count - 1, lower, m, upper] + [rb_ref[base + r] for r in range(RAND)]
        for slot, block in enumerate(ids):
            kg_ref[slot * BLOCK:(slot + 1) * BLOCK, :] = rows(x_ref, 1, block)[...]
            vg_ref[slot * BLOCK:(slot + 1) * BLOCK, :] = rows(x_ref, 2, block)[...]
        start = pl.multiple_of(m * BLOCK, BLOCK)
        qb = rows(x_ref, 0, m)[...]
        ub = u_ref[pl.ds(start, BLOCK), :]
        mask = ((columns == 2) & (m == 1)) | ((columns == 4) & (m == count - 2))
        query_grad, key_grad, value_grad = softmax_grads(qb, ub, kg_ref[...], vg_ref[...], mask)
        rows(o_ref, 0, m)[...] = query_grad.astype(jnp.bfloat16)
        for slot, block in enumerate(ids):
            row = pl.multiple_of(block * BLOCK, BLOCK)
            dk_acc[pl.ds(row, BLOCK), :] += key_grad[slot * BLOCK:(slot + 1) * BLOCK, :]
            dv_acc[pl.ds(row, BLOCK), :] += value_grad[slot * BLOCK:(slot + 1) * BLOCK, :]
        return carry

    lax.fori_loop(1, count - 1, mid_step, 0, unroll=2)
    o_ref[:, 1, :, :] = dk_acc[...].reshape(parts, tokens, HD).astype(jnp.bfloat16)
    o_ref[:, 2, :, :] = dv_acc[...].reshape(parts, tokens, HD).astype(jnp.bfloat16)


def attention_grads(stacked, upstream, head, random_ids):
    parts, _, _, tokens, _ = stacked.shape
    length = parts * tokens
    count = length // BLOCK
    source = pl.BlockSpec((parts, 3, None, tokens, HD), lambda h, rb: (0, 0, head, 0, 0))
    whole = pl.BlockSpec((parts, 3, tokens, HD), lambda h, rb: (0, 0, 0, 0))
    spec = pl.BlockSpec((length, HD), lambda h, rb: (0, head))
    out = jax.ShapeDtypeStruct((parts, 3, tokens, HD), jnp.bfloat16)
    pairs = 2 * BLOCK * length + (count - 2) * BLOCK * SLOTS * BLOCK
    cost = pl.CostEstimate(
        flops=12 * pairs * HD, transcendentals=pairs, bytes_accessed=14 * length * HD
    )
    return pl.pallas_call(
        _attention_kernel,
        out_shape=out,
        grid_spec=pltpu.PrefetchScalarGridSpec(
            num_scalar_prefetch=1,
            grid=(1,),
            in_specs=[source, spec],
            out_specs=whole,
            scratch_shapes=[
                pltpu.VMEM((length, HD), jnp.float32),
                pltpu.VMEM((length, HD), jnp.float32),
                pltpu.VMEM((SLOTS * BLOCK, HD), jnp.bfloat16),
                pltpu.VMEM((SLOTS * BLOCK, HD), jnp.bfloat16),
            ],
        ),
        compiler_params=pltpu.CompilerParams(dimension_semantics=("arbitrary",)),
        cost_estimate=cost,
    )(random_ids.reshape(-1), stacked, upstream)


def body(queries, key_rows, value_rows, cotangent, out_weight, random_blocks):
    dp = lax.axis_size("dp")
    ctx = lax.axis_size("context")
    local = (queries[0], key_rows[0], value_rows[0])
    local_cotangent = cotangent[0]
    tokens, width = local[0].shape
    total_heads = width // HD
    local_heads = total_heads // ctx
    rows_per_device = out_weight.shape[0]
    strided = rows_per_device == HD and local_heads == dp and ctx % 2 == 0

    if strided:
        me = lax.axis_index("dp")
        got = [out_weight] + [
            lax.ppermute(out_weight, "dp", [(a, (a + s) % dp) for a in range(dp)])
            for s in range(1, dp)
        ]
        order = (me - jnp.arange(dp)) % dp
        head_weight = jnp.take(jnp.stack(got), order, axis=0).reshape(dp * HD, -1)
        j = lax.axis_index("context")
        shifts = list(range(0, ctx, 2))
        mine = jnp.stack([local_cotangent] + [
            lax.ppermute(local_cotangent, "context", [(a, (a + s) % ctx) for a in range(ctx)])
            for s in shifts[1:]
        ])
        other = lax.ppermute(mine, "context", [(a, a ^ 1) for a in range(ctx)])
        gathered = jnp.concatenate([mine, other]).reshape(ctx * tokens, -1)
        upstream = lax.dot_general(
            gathered, head_weight, (((1,), (1,)), ((), ())),
            preferred_element_type=jnp.float32,
        ).astype(jnp.bfloat16)
        source = jnp.arange(ctx)
        same = source % 2 == j % 2
        position = jnp.where(
            same, ((j - source) % ctx) // 2, ctx // 2 + (((j ^ 1) - source) % ctx) // 2
        )
        upstream = jnp.take(upstream.reshape(ctx, tokens, -1), position, axis=0)
        upstream = upstream.reshape(ctx * tokens, -1)

        def chunk(array):
            return array.reshape(tokens, dp, ctx, HD).transpose(2, 1, 0, 3)
    else:
        upstream = lax.dot_general(
            local_cotangent,
            lax.all_gather(out_weight, ("dp", "context"), axis=0, tiled=True),
            (((1,), (1,)), ((), ())),
            preferred_element_type=jnp.float32,
        ).astype(jnp.bfloat16)
        local = local + (upstream,)

        def chunk(array):
            return array.reshape(tokens, ctx, local_heads, HD).transpose(1, 2, 0, 3)

    stacked = jnp.stack([chunk(array) for array in local], axis=1)
    moved = lax.all_to_all(stacked, "context", split_axis=0, concat_axis=0, tiled=True)
    if not strided:
        head_upstream = moved[:, 3].transpose(1, 0, 2, 3).reshape(local_heads, tokens * ctx, HD)
        moved = moved[:, :3]
    pieces = []
    for c in range(local_heads):
        if strided:
            grads = attention_grads(moved, upstream, c, random_blocks[0])
        else:
            grads = attention_grads(moved, head_upstream[c], 0, random_blocks[0])
        back = lax.all_to_all(grads, "context", split_axis=0, concat_axis=0, tiled=True)
        pieces.append(back.transpose(1, 2, 0, 3))

    outs = []
    for g in range(3):
        joined = jnp.stack([piece[g] for piece in pieces], axis=1 if strided else 2)
        outs.append(joined.reshape(1, tokens, width))
    return tuple(outs)


def solution(mesh):
    return jax.shard_map(
        body,
        mesh=mesh,
        in_specs=(
            P("dp", "context", None),
            P("dp", "context", None),
            P("dp", "context", None),
            P("dp", "context", None),
            P(("dp", "context"), None),
            P("dp", None, None),
        ),
        out_specs=(P("dp", "context", None), P("dp", "context", None), P("dp", "context", None)),
        check_vma=False,
    )
```

```python
import functools
import math

import jax
import jax.numpy as jnp
from jax import lax
from jax.experimental import pallas as pl
from jax.experimental.pallas import tpu as pltpu
from jax.sharding import PartitionSpec as P

HD = 128
BLOCK = 64
RAND = 3
SLOTS = 5 + RAND


def _nt(a, b):
    return lax.dot_general(a, b, (((1,), (1,)), ((), ())), preferred_element_type=jnp.float32)


def _tn(a, b):
    return lax.dot_general(a, b, (((0,), (0,)), ((), ())), preferred_element_type=jnp.float32)


def _nn(a, b):
    return lax.dot_general(a, b, (((1,), (0,)), ((), ())), preferred_element_type=jnp.float32)


def _attention_kernel(rb_ref, pos_ref, col_ref, x_ref, u_ref, o_ref, dk_acc, dv_acc, kg_ref, vg_ref):
    parts, _, tokens, _ = x_ref.shape
    per_part = tokens // BLOCK
    length = parts * tokens
    count = length // BLOCK
    factor = 1.0 / math.sqrt(HD)

    def rows(ref, which, block):
        if isinstance(block, int):
            offset = (block % per_part) * BLOCK
        else:
            offset = pl.multiple_of((block % per_part) * BLOCK, BLOCK)
        return ref.at[block // per_part, which, pl.ds(offset, BLOCK), :]

    def upstream_rows(block):
        offset = pos_ref[block // per_part] * tokens + (block % per_part) * BLOCK
        return u_ref[pl.ds(pl.multiple_of(offset, BLOCK), BLOCK), :]

    def softmax_grads(qb, ub, keys, values, mask):
        scores = _nt(qb, keys) * factor
        if mask is not None:
            scores = jnp.where(mask, -1e30, scores)
        top = jnp.max(scores, axis=1, keepdims=True)
        expo = jnp.exp(scores - top)
        weights = expo * (1.0 / jnp.sum(expo, axis=1, keepdims=True))
        rounded = weights.astype(jnp.bfloat16)
        attended = _nn(rounded, values)
        row = jnp.sum(ub.astype(jnp.float32) * attended, axis=1, keepdims=True)
        grad_probs = _nt(ub, values)
        grad_scores = (weights * (grad_probs - row) * factor).astype(jnp.bfloat16)
        query_grad = _nn(grad_scores, keys)
        key_grad = _tn(grad_scores, qb)
        value_grad = _tn(rounded, ub)
        return query_grad, key_grad, value_grad

    keys_all = x_ref[:, 1, :, :].reshape(length, HD)
    values_all = x_ref[:, 2, :, :].reshape(length, HD)
    for index, block in enumerate((0, count - 1)):
        qb = rows(x_ref, 0, block)[...]
        ub = upstream_rows(block)
        query_grad, key_grad, value_grad = softmax_grads(qb, ub, keys_all, values_all, None)
        rows(o_ref, 0, block)[...] = query_grad.astype(jnp.bfloat16)
        if index == 0:
            dk_acc[...] = key_grad
            dv_acc[...] = value_grad
        else:
            dk_acc[...] += key_grad
            dv_acc[...] += value_grad

    columns = lax.broadcasted_iota(jnp.int32, (BLOCK, SLOTS * BLOCK), 1) // BLOCK

    def mid_step(m, carry):
        base = (m - 1) * RAND
        lower = jnp.where(m - 1 >= 1, m - 1, m)
        upper = jnp.where(m + 1 <= count - 2, m + 1, m)
        ids = [0, count - 1, lower, m, upper] + [rb_ref[base + r] for r in range(RAND)]
        for slot, block in enumerate(ids):
            kg_ref[slot * BLOCK:(slot + 1) * BLOCK, :] = rows(x_ref, 1, block)[...]
            vg_ref[slot * BLOCK:(slot + 1) * BLOCK, :] = rows(x_ref, 2, block)[...]
        start = pl.multiple_of(m * BLOCK, BLOCK)
        qb = rows(x_ref, 0, m)[...]
        ub = upstream_rows(m)
        mask = ((columns == 2) & (m == 1)) | ((columns == 4) & (m == count - 2))
        query_grad, key_grad, value_grad = softmax_grads(qb, ub, kg_ref[...], vg_ref[...], mask)
        rows(o_ref, 0, m)[...] = query_grad.astype(jnp.bfloat16)
        for slot, block in enumerate(ids):
            row = pl.multiple_of(block * BLOCK, BLOCK)
            dk_acc[pl.ds(row, BLOCK), :] += key_grad[slot * BLOCK:(slot + 1) * BLOCK, :]
            dv_acc[pl.ds(row, BLOCK), :] += value_grad[slot * BLOCK:(slot + 1) * BLOCK, :]
        return carry

    lax.fori_loop(1, count - 1, mid_step, 0, unroll=2)
    o_ref[:, 1, :, :] = dk_acc[...].reshape(parts, tokens, HD).astype(jnp.bfloat16)
    o_ref[:, 2, :, :] = dv_acc[...].reshape(parts, tokens, HD).astype(jnp.bfloat16)


def attention_grads(stacked, upstream, head, column, positions, random_ids):
    parts, _, _, tokens, _ = stacked.shape
    length = parts * tokens
    count = length // BLOCK
    source = pl.BlockSpec((parts, 3, None, tokens, HD), lambda h, rb, ps, cl: (0, 0, head, 0, 0))
    whole = pl.BlockSpec((parts, 3, tokens, HD), lambda h, rb, ps, cl: (0, 0, 0, 0))
    spec = pl.BlockSpec((length, HD), lambda h, rb, ps, cl: (0, cl[0]))
    out = jax.ShapeDtypeStruct((parts, 3, tokens, HD), jnp.bfloat16)
    pairs = 2 * BLOCK * length + (count - 2) * BLOCK * SLOTS * BLOCK
    cost = pl.CostEstimate(
        flops=12 * pairs * HD, transcendentals=pairs, bytes_accessed=14 * length * HD
    )
    return pl.pallas_call(
        _attention_kernel,
        out_shape=out,
        grid_spec=pltpu.PrefetchScalarGridSpec(
            num_scalar_prefetch=3,
            grid=(1,),
            in_specs=[source, spec],
            out_specs=whole,
            scratch_shapes=[
                pltpu.VMEM((length, HD), jnp.float32),
                pltpu.VMEM((length, HD), jnp.float32),
                pltpu.VMEM((SLOTS * BLOCK, HD), jnp.bfloat16),
                pltpu.VMEM((SLOTS * BLOCK, HD), jnp.bfloat16),
            ],
        ),
        compiler_params=pltpu.CompilerParams(dimension_semantics=("arbitrary",)),
        cost_estimate=cost,
    )(random_ids.reshape(-1), positions, column.reshape(1), stacked, upstream)


def body(queries, key_rows, value_rows, cotangent, out_weight, random_blocks):
    dp = lax.axis_size("dp")
    ctx = lax.axis_size("context")
    local = (queries[0], key_rows[0], value_rows[0])
    local_cotangent = cotangent[0]
    tokens, width = local[0].shape
    total_heads = width // HD
    local_heads = total_heads // ctx
    rows_per_device = out_weight.shape[0]
    strided = rows_per_device == HD and local_heads == dp and ctx % 2 == 0

    if strided:
        me = lax.axis_index("dp")
        got = [out_weight] + [
            lax.ppermute(out_weight, "dp", [(a, (a + s) % dp) for a in range(dp)])
            for s in range(1, dp)
        ]
        head_weight = jnp.concatenate(got, axis=0)
        columns = [(me - c) % dp for c in range(local_heads)]
        j = lax.axis_index("context")
        shifts = list(range(0, ctx, 2))
        mine = jnp.stack([local_cotangent] + [
            lax.ppermute(local_cotangent, "context", [(a, (a + s) % ctx) for a in range(ctx)])
            for s in shifts[1:]
        ])
        other = lax.ppermute(mine, "context", [(a, a ^ 1) for a in range(ctx)])

        def project(piece):
            return lax.dot_general(
                piece.reshape(-1, piece.shape[-1]), head_weight, (((1,), (1,)), ((), ())),
                preferred_element_type=jnp.float32,
            ).astype(jnp.bfloat16)

        upstream = jnp.concatenate([project(mine), project(other)], axis=0)
        source = jnp.arange(ctx)
        same = source % 2 == j % 2
        positions = jnp.where(
            same, ((j - source) % ctx) // 2, ctx // 2 + (((j ^ 1) - source) % ctx) // 2
        ).astype(jnp.int32)

        def chunk(array):
            return array.reshape(tokens, dp, ctx, HD).transpose(2, 1, 0, 3)
    else:
        upstream = lax.dot_general(
            local_cotangent,
            lax.all_gather(out_weight, ("dp", "context"), axis=0, tiled=True),
            (((1,), (1,)), ((), ())),
            preferred_element_type=jnp.float32,
        ).astype(jnp.bfloat16)
        local = local + (upstream,)
        positions = jnp.arange(ctx, dtype=jnp.int32)

        def chunk(array):
            return array.reshape(tokens, ctx, local_heads, HD).transpose(1, 2, 0, 3)

    stacked = jnp.stack([chunk(array) for array in local], axis=1)
    moved = lax.all_to_all(stacked, "context", split_axis=0, concat_axis=0, tiled=True)
    if not strided:
        head_upstream = moved[:, 3].transpose(1, 0, 2, 3).reshape(local_heads, tokens * ctx, HD)
        moved = moved[:, :3]
    pieces = []
    for c in range(local_heads):
        if strided:
            grads = attention_grads(
                moved, upstream, c, columns[c].astype(jnp.int32), positions, random_blocks[0]
            )
        else:
            grads = attention_grads(
                moved, head_upstream[c], 0, jnp.zeros((), jnp.int32), positions, random_blocks[0]
            )
        back = lax.all_to_all(grads, "context", split_axis=0, concat_axis=0, tiled=True)
        pieces.append(back.transpose(1, 2, 0, 3))

    outs = []
    for g in range(3):
        joined = jnp.stack([piece[g] for piece in pieces], axis=1 if strided else 2)
        outs.append(joined.reshape(1, tokens, width))
    return tuple(outs)


def solution(mesh):
    return jax.shard_map(
        body,
        mesh=mesh,
        in_specs=(
            P("dp", "context", None),
            P("dp", "context", None),
            P("dp", "context", None),
            P("dp", "context", None),
            P(("dp", "context"), None),
            P("dp", None, None),
        ),
        out_specs=(P("dp", "context", None), P("dp", "context", None), P("dp", "context", None)),
        check_vma=False,
    )
```

```python
import functools
import math

import jax
import jax.numpy as jnp
from jax import lax
from jax.experimental import pallas as pl
from jax.experimental.pallas import tpu as pltpu
from jax.sharding import PartitionSpec as P

HD = 128
BLOCK = 64
RAND = 3
SLOTS = 5 + RAND


def _nt(a, b):
    return lax.dot_general(a, b, (((1,), (1,)), ((), ())), preferred_element_type=jnp.float32)


def _tn(a, b):
    return lax.dot_general(a, b, (((0,), (0,)), ((), ())), preferred_element_type=jnp.float32)


def _nn(a, b):
    return lax.dot_general(a, b, (((1,), (0,)), ((), ())), preferred_element_type=jnp.float32)


def _attention_kernel(rb_ref, pos_ref, col_ref, x_ref, u_ref, o_ref, dk_acc, dv_acc, kg_ref, vg_ref):
    parts, _, tokens, _ = x_ref.shape
    per_part = tokens // BLOCK
    length = parts * tokens
    count = length // BLOCK
    factor = 1.0 / math.sqrt(HD)

    def rows(ref, which, block):
        if isinstance(block, int):
            offset = (block % per_part) * BLOCK
        else:
            offset = pl.multiple_of((block % per_part) * BLOCK, BLOCK)
        return ref.at[block // per_part, which, pl.ds(offset, BLOCK), :]

    def upstream_rows(block):
        offset = pos_ref[block // per_part] * tokens + (block % per_part) * BLOCK
        return u_ref[pl.ds(pl.multiple_of(offset, BLOCK), BLOCK), :]

    def softmax_grads(qb, ub, keys, values, mask):
        scores = _nt(qb, keys) * factor
        if mask is not None:
            scores = jnp.where(mask, -1e30, scores)
        top = jnp.max(scores, axis=1, keepdims=True)
        expo = jnp.exp(scores - top)
        weights = expo * (1.0 / jnp.sum(expo, axis=1, keepdims=True))
        rounded = weights.astype(jnp.bfloat16)
        attended = _nn(rounded, values)
        row = jnp.sum(ub.astype(jnp.float32) * attended, axis=1, keepdims=True)
        grad_probs = _nt(ub, values)
        grad_scores = (weights * (grad_probs - row) * factor).astype(jnp.bfloat16)
        query_grad = _nn(grad_scores, keys)
        key_grad = _tn(grad_scores, qb)
        value_grad = _tn(rounded, ub)
        return query_grad, key_grad, value_grad

    keys_all = x_ref[:, 1, :, :].reshape(length, HD)
    values_all = x_ref[:, 2, :, :].reshape(length, HD)
    for index, block in enumerate((0, count - 1)):
        qb = rows(x_ref, 0, block)[...]
        ub = upstream_rows(block)
        query_grad, key_grad, value_grad = softmax_grads(qb, ub, keys_all, values_all, None)
        rows(o_ref, 0, block)[...] = query_grad.astype(jnp.bfloat16)
        if index == 0:
            dk_acc[...] = key_grad
            dv_acc[...] = value_grad
        else:
            dk_acc[...] += key_grad
            dv_acc[...] += value_grad

    columns = lax.broadcasted_iota(jnp.int32, (BLOCK, SLOTS * BLOCK), 1) // BLOCK

    def mid_step(m, carry):
        base = (m - 1) * RAND
        lower = jnp.where(m - 1 >= 1, m - 1, m)
        upper = jnp.where(m + 1 <= count - 2, m + 1, m)
        ids = [0, count - 1, lower, m, upper] + [rb_ref[base + r] for r in range(RAND)]
        for slot, block in enumerate(ids):
            kg_ref[slot * BLOCK:(slot + 1) * BLOCK, :] = rows(x_ref, 1, block)[...]
            vg_ref[slot * BLOCK:(slot + 1) * BLOCK, :] = rows(x_ref, 2, block)[...]
        start = pl.multiple_of(m * BLOCK, BLOCK)
        qb = rows(x_ref, 0, m)[...]
        ub = upstream_rows(m)
        mask = ((columns == 2) & (m == 1)) | ((columns == 4) & (m == count - 2))
        query_grad, key_grad, value_grad = softmax_grads(qb, ub, kg_ref[...], vg_ref[...], mask)
        rows(o_ref, 0, m)[...] = query_grad.astype(jnp.bfloat16)
        for slot, block in enumerate(ids):
            row = pl.multiple_of(block * BLOCK, BLOCK)
            dk_acc[pl.ds(row, BLOCK), :] += key_grad[slot * BLOCK:(slot + 1) * BLOCK, :]
            dv_acc[pl.ds(row, BLOCK), :] += value_grad[slot * BLOCK:(slot + 1) * BLOCK, :]
        return carry

    lax.fori_loop(1, count - 1, mid_step, 0, unroll=2)
    o_ref[:, 1, :, :] = dk_acc[...].reshape(parts, tokens, HD).astype(jnp.bfloat16)
    o_ref[:, 2, :, :] = dv_acc[...].reshape(parts, tokens, HD).astype(jnp.bfloat16)


def attention_grads(stacked, upstream, head, column, positions, random_ids):
    parts, _, _, tokens, _ = stacked.shape
    length = parts * tokens
    count = length // BLOCK
    source = pl.BlockSpec((parts, 3, None, tokens, HD), lambda h, rb, ps, cl: (0, 0, head, 0, 0))
    whole = pl.BlockSpec((parts, 3, tokens, HD), lambda h, rb, ps, cl: (0, 0, 0, 0))
    spec = pl.BlockSpec((length, HD), lambda h, rb, ps, cl: (0, cl[0]))
    out = jax.ShapeDtypeStruct((parts, 3, tokens, HD), jnp.bfloat16)
    pairs = 2 * BLOCK * length + (count - 2) * BLOCK * SLOTS * BLOCK
    cost = pl.CostEstimate(
        flops=12 * pairs * HD, transcendentals=pairs, bytes_accessed=14 * length * HD
    )
    return pl.pallas_call(
        _attention_kernel,
        out_shape=out,
        grid_spec=pltpu.PrefetchScalarGridSpec(
            num_scalar_prefetch=3,
            grid=(1,),
            in_specs=[source, spec],
            out_specs=whole,
            scratch_shapes=[
                pltpu.VMEM((length, HD), jnp.float32),
                pltpu.VMEM((length, HD), jnp.float32),
                pltpu.VMEM((SLOTS * BLOCK, HD), jnp.bfloat16),
                pltpu.VMEM((SLOTS * BLOCK, HD), jnp.bfloat16),
            ],
        ),
        compiler_params=pltpu.CompilerParams(dimension_semantics=("arbitrary",)),
        cost_estimate=cost,
    )(random_ids.reshape(-1), positions, column.reshape(1), stacked, upstream)


def body(queries, key_rows, value_rows, cotangent, out_weight, random_blocks):
    dp = lax.axis_size("dp")
    ctx = lax.axis_size("context")
    local = (queries[0], key_rows[0], value_rows[0])
    local_cotangent = cotangent[0]
    tokens, width = local[0].shape
    total_heads = width // HD
    local_heads = total_heads // ctx
    rows_per_device = out_weight.shape[0]
    strided = rows_per_device == HD and local_heads == dp and ctx % 2 == 0

    if strided:
        spread = jnp.broadcast_to(out_weight[None], (dp,) + out_weight.shape)
        head_weight = lax.all_to_all(spread, "dp", split_axis=0, concat_axis=0, tiled=True)
        head_weight = head_weight.reshape(dp * HD, -1)
        columns = [jnp.array(c, jnp.int32) for c in range(local_heads)]
        j = lax.axis_index("context")
        shifts = list(range(0, ctx, 2))
        mine = jnp.stack([local_cotangent] + [
            lax.ppermute(local_cotangent, "context", [(a, (a + s) % ctx) for a in range(ctx)])
            for s in shifts[1:]
        ])
        other = lax.ppermute(mine, "context", [(a, a ^ 1) for a in range(ctx)])

        def project(piece):
            return lax.dot_general(
                piece.reshape(-1, piece.shape[-1]), head_weight, (((1,), (1,)), ((), ())),
                preferred_element_type=jnp.float32,
            ).astype(jnp.bfloat16)

        upstream = jnp.concatenate([project(mine), project(other)], axis=0)
        source = jnp.arange(ctx)
        same = source % 2 == j % 2
        positions = jnp.where(
            same, ((j - source) % ctx) // 2, ctx // 2 + (((j ^ 1) - source) % ctx) // 2
        ).astype(jnp.int32)

        def chunk(array):
            return array.reshape(tokens, dp, ctx, HD).transpose(2, 1, 0, 3)
    else:
        upstream = lax.dot_general(
            local_cotangent,
            lax.all_gather(out_weight, ("dp", "context"), axis=0, tiled=True),
            (((1,), (1,)), ((), ())),
            preferred_element_type=jnp.float32,
        ).astype(jnp.bfloat16)
        local = local + (upstream,)
        positions = jnp.arange(ctx, dtype=jnp.int32)

        def chunk(array):
            return array.reshape(tokens, ctx, local_heads, HD).transpose(1, 2, 0, 3)

    stacked = jnp.stack([chunk(array) for array in local], axis=1)
    moved = lax.all_to_all(stacked, "context", split_axis=0, concat_axis=0, tiled=True)
    if not strided:
        head_upstream = moved[:, 3].transpose(1, 0, 2, 3).reshape(local_heads, tokens * ctx, HD)
        moved = moved[:, :3]
    pieces = []
    for c in range(local_heads):
        if strided:
            grads = attention_grads(
                moved, upstream, c, columns[c].astype(jnp.int32), positions, random_blocks[0]
            )
        else:
            grads = attention_grads(
                moved, head_upstream[c], 0, jnp.zeros((), jnp.int32), positions, random_blocks[0]
            )
        back = lax.all_to_all(grads, "context", split_axis=0, concat_axis=0, tiled=True)
        pieces.append(back.transpose(1, 2, 0, 3))

    outs = []
    for g in range(3):
        joined = jnp.stack([piece[g] for piece in pieces], axis=1 if strided else 2)
        outs.append(joined.reshape(1, tokens, width))
    return tuple(outs)


def solution(mesh):
    return jax.shard_map(
        body,
        mesh=mesh,
        in_specs=(
            P("dp", "context", None),
            P("dp", "context", None),
            P("dp", "context", None),
            P("dp", "context", None),
            P(("dp", "context"), None),
            P("dp", None, None),
        ),
        out_specs=(P("dp", "context", None), P("dp", "context", None), P("dp", "context", None)),
        check_vma=False,
    )
```

```python
import functools
import math

import jax
import jax.numpy as jnp
from jax import lax
from jax.experimental import pallas as pl
from jax.experimental.pallas import tpu as pltpu
from jax.sharding import PartitionSpec as P

HD = 128
BLOCK = 64
RAND = 3
SLOTS = 5 + RAND


def _nt(a, b):
    return lax.dot_general(a, b, (((1,), (1,)), ((), ())), preferred_element_type=jnp.float32)


def _tn(a, b):
    return lax.dot_general(a, b, (((0,), (0,)), ((), ())), preferred_element_type=jnp.float32)


def _nn(a, b):
    return lax.dot_general(a, b, (((1,), (0,)), ((), ())), preferred_element_type=jnp.float32)


def _attention_kernel(rb_ref, pos_ref, col_ref, x_ref, u_ref, o_ref, dk_acc, dv_acc, kg_ref, vg_ref):
    parts, _, tokens, _ = x_ref.shape
    per_part = tokens // BLOCK
    length = parts * tokens
    count = length // BLOCK
    factor = 1.0 / math.sqrt(HD)

    def rows(ref, which, block):
        if isinstance(block, int):
            offset = (block % per_part) * BLOCK
        else:
            offset = pl.multiple_of((block % per_part) * BLOCK, BLOCK)
        return ref.at[block // per_part, which, pl.ds(offset, BLOCK), :]

    def upstream_rows(block):
        offset = pos_ref[block // per_part] * tokens + (block % per_part) * BLOCK
        return u_ref[pl.ds(pl.multiple_of(offset, BLOCK), BLOCK), :]

    def softmax_grads(qb, ub, keys, values, mask):
        scores = _nt(qb, keys) * factor
        if mask is not None:
            scores = jnp.where(mask, -1e30, scores)
        top = jnp.max(scores, axis=1, keepdims=True)
        expo = jnp.exp(scores - top)
        weights = expo * (1.0 / jnp.sum(expo, axis=1, keepdims=True))
        rounded = weights.astype(jnp.bfloat16)
        attended = _nn(rounded, values)
        row = jnp.sum(ub.astype(jnp.float32) * attended, axis=1, keepdims=True)
        grad_probs = _nt(ub, values)
        grad_scores = (weights * (grad_probs - row) * factor).astype(jnp.bfloat16)
        query_grad = _nn(grad_scores, keys)
        key_grad = _tn(grad_scores, qb)
        value_grad = _tn(rounded, ub)
        return query_grad, key_grad, value_grad

    keys_all = x_ref[:, 1, :, :].reshape(length, HD)
    values_all = x_ref[:, 2, :, :].reshape(length, HD)
    for index, block in enumerate((0, count - 1)):
        qb = rows(x_ref, 0, block)[...]
        ub = upstream_rows(block)
        query_grad, key_grad, value_grad = softmax_grads(qb, ub, keys_all, values_all, None)
        rows(o_ref, 0, block)[...] = query_grad.astype(jnp.bfloat16)
        if index == 0:
            dk_acc[...] = key_grad
            dv_acc[...] = value_grad
        else:
            dk_acc[...] += key_grad
            dv_acc[...] += value_grad

    columns = lax.broadcasted_iota(jnp.int32, (BLOCK, SLOTS * BLOCK), 1) // BLOCK

    def mid_step(m, carry):
        base = (m - 1) * RAND
        lower = jnp.where(m - 1 >= 1, m - 1, m)
        upper = jnp.where(m + 1 <= count - 2, m + 1, m)
        ids = [0, count - 1, lower, m, upper] + [rb_ref[base + r] for r in range(RAND)]
        for slot, block in enumerate(ids):
            kg_ref[slot * BLOCK:(slot + 1) * BLOCK, :] = rows(x_ref, 1, block)[...]
            vg_ref[slot * BLOCK:(slot + 1) * BLOCK, :] = rows(x_ref, 2, block)[...]
        start = pl.multiple_of(m * BLOCK, BLOCK)
        qb = rows(x_ref, 0, m)[...]
        ub = upstream_rows(m)
        mask = ((columns == 2) & (m == 1)) | ((columns == 4) & (m == count - 2))
        query_grad, key_grad, value_grad = softmax_grads(qb, ub, kg_ref[...], vg_ref[...], mask)
        rows(o_ref, 0, m)[...] = query_grad.astype(jnp.bfloat16)
        for slot, block in enumerate(ids):
            row = pl.multiple_of(block * BLOCK, BLOCK)
            dk_acc[pl.ds(row, BLOCK), :] += key_grad[slot * BLOCK:(slot + 1) * BLOCK, :]
            dv_acc[pl.ds(row, BLOCK), :] += value_grad[slot * BLOCK:(slot + 1) * BLOCK, :]
        return carry

    lax.fori_loop(1, count - 1, mid_step, 0, unroll=2)
    o_ref[:, 1, :, :] = dk_acc[...].reshape(parts, tokens, HD).astype(jnp.bfloat16)
    o_ref[:, 2, :, :] = dv_acc[...].reshape(parts, tokens, HD).astype(jnp.bfloat16)


def attention_grads(stacked, upstream, head, column, positions, random_ids):
    parts, _, _, tokens, _ = stacked.shape
    length = parts * tokens
    count = length // BLOCK
    source = pl.BlockSpec((parts, 3, None, tokens, HD), lambda h, rb, ps, cl: (0, 0, head, 0, 0))
    whole = pl.BlockSpec((parts, 3, tokens, HD), lambda h, rb, ps, cl: (0, 0, 0, 0))
    spec = pl.BlockSpec((length, HD), lambda h, rb, ps, cl: (0, cl[0]))
    out = jax.ShapeDtypeStruct((parts, 3, tokens, HD), jnp.bfloat16)
    pairs = 2 * BLOCK * length + (count - 2) * BLOCK * SLOTS * BLOCK
    cost = pl.CostEstimate(
        flops=12 * pairs * HD, transcendentals=pairs, bytes_accessed=14 * length * HD
    )
    return pl.pallas_call(
        _attention_kernel,
        out_shape=out,
        grid_spec=pltpu.PrefetchScalarGridSpec(
            num_scalar_prefetch=3,
            grid=(1,),
            in_specs=[source, spec],
            out_specs=whole,
            scratch_shapes=[
                pltpu.VMEM((length, HD), jnp.float32),
                pltpu.VMEM((length, HD), jnp.float32),
                pltpu.VMEM((SLOTS * BLOCK, HD), jnp.bfloat16),
                pltpu.VMEM((SLOTS * BLOCK, HD), jnp.bfloat16),
            ],
        ),
        compiler_params=pltpu.CompilerParams(dimension_semantics=("arbitrary",)),
        cost_estimate=cost,
    )(random_ids.reshape(-1), positions, column.reshape(1), stacked, upstream)


def body(queries, key_rows, value_rows, cotangent, out_weight, random_blocks):
    dp = lax.axis_size("dp")
    ctx = lax.axis_size("context")
    local = (queries[0], key_rows[0], value_rows[0])
    local_cotangent = cotangent[0]
    tokens, width = local[0].shape
    total_heads = width // HD
    local_heads = total_heads // ctx
    rows_per_device = out_weight.shape[0]
    strided = rows_per_device == HD and local_heads == dp and ctx % 2 == 0

    if strided:
        me = lax.axis_index("dp")
        got = [out_weight] + [
            lax.ppermute(out_weight, "dp", [(a, (a + s) % dp) for a in range(dp)])
            for s in range(1, dp)
        ]
        order = (me - jnp.arange(dp)) % dp
        head_weight = jnp.take(jnp.stack(got), order, axis=0).reshape(dp * HD, -1)
        columns = [jnp.array(c, jnp.int32) for c in range(local_heads)]
        j = lax.axis_index("context")
        shifts = list(range(0, ctx, 2))
        mine = jnp.stack([local_cotangent] + [
            lax.ppermute(local_cotangent, "context", [(a, (a + s) % ctx) for a in range(ctx)])
            for s in shifts[1:]
        ])
        head_weight, mine = lax.optimization_barrier((head_weight, mine))
        other = lax.ppermute(mine, "context", [(a, a ^ 1) for a in range(ctx)])

        def project(piece):
            return lax.dot_general(
                piece.reshape(-1, piece.shape[-1]), head_weight, (((1,), (1,)), ((), ())),
                preferred_element_type=jnp.float32,
            ).astype(jnp.bfloat16)

        upstream = jnp.concatenate([project(mine), project(other)], axis=0)
        source = jnp.arange(ctx)
        same = source % 2 == j % 2
        positions = jnp.where(
            same, ((j - source) % ctx) // 2, ctx // 2 + (((j ^ 1) - source) % ctx) // 2
        ).astype(jnp.int32)

        def chunk(array):
            return array.reshape(tokens, dp, ctx, HD).transpose(2, 1, 0, 3)
    else:
        upstream = lax.dot_general(
            local_cotangent,
            lax.all_gather(out_weight, ("dp", "context"), axis=0, tiled=True),
            (((1,), (1,)), ((), ())),
            preferred_element_type=jnp.float32,
        ).astype(jnp.bfloat16)
        local = local + (upstream,)
        positions = jnp.arange(ctx, dtype=jnp.int32)

        def chunk(array):
            return array.reshape(tokens, ctx, local_heads, HD).transpose(1, 2, 0, 3)

    stacked = jnp.stack([chunk(array) for array in local], axis=1)
    moved = lax.all_to_all(stacked, "context", split_axis=0, concat_axis=0, tiled=True)
    if not strided:
        head_upstream = moved[:, 3].transpose(1, 0, 2, 3).reshape(local_heads, tokens * ctx, HD)
        moved = moved[:, :3]
    pieces = []
    for c in range(local_heads):
        if strided:
            grads = attention_grads(
                moved, upstream, c, columns[c].astype(jnp.int32), positions, random_blocks[0]
            )
        else:
            grads = attention_grads(
                moved, head_upstream[c], 0, jnp.zeros((), jnp.int32), positions, random_blocks[0]
            )
        back = lax.all_to_all(grads, "context", split_axis=0, concat_axis=0, tiled=True)
        pieces.append(back.transpose(1, 2, 0, 3))

    outs = []
    for g in range(3):
        joined = jnp.stack([piece[g] for piece in pieces], axis=1 if strided else 2)
        outs.append(joined.reshape(1, tokens, width))
    return tuple(outs)


def solution(mesh):
    return jax.shard_map(
        body,
        mesh=mesh,
        in_specs=(
            P("dp", "context", None),
            P("dp", "context", None),
            P("dp", "context", None),
            P("dp", "context", None),
            P(("dp", "context"), None),
            P("dp", None, None),
        ),
        out_specs=(P("dp", "context", None), P("dp", "context", None), P("dp", "context", None)),
        check_vma=False,
    )
```

```python
import functools
import math

import jax
import jax.numpy as jnp
from jax import lax
from jax.experimental import pallas as pl
from jax.experimental.pallas import tpu as pltpu
from jax.sharding import PartitionSpec as P

HD = 128
BLOCK = 64
RAND = 3
SLOTS = 5 + RAND


def _nt(a, b):
    return lax.dot_general(a, b, (((1,), (1,)), ((), ())), preferred_element_type=jnp.float32)


def _tn(a, b):
    return lax.dot_general(a, b, (((0,), (0,)), ((), ())), preferred_element_type=jnp.float32)


def _nn(a, b):
    return lax.dot_general(a, b, (((1,), (0,)), ((), ())), preferred_element_type=jnp.float32)


def _attention_kernel(rb_ref, x_ref, u_ref, o_ref, dk_acc, dv_acc, kg_ref, vg_ref):
    parts, _, tokens, _ = x_ref.shape
    per_part = tokens // BLOCK
    length = parts * tokens
    count = length // BLOCK
    factor = 1.0 / math.sqrt(HD)

    def rows(ref, which, block):
        if isinstance(block, int):
            offset = (block % per_part) * BLOCK
        else:
            offset = pl.multiple_of((block % per_part) * BLOCK, BLOCK)
        return ref.at[block // per_part, which, pl.ds(offset, BLOCK), :]

    def softmax_grads(qb, ub, keys, values, mask):
        scores = _nt(qb, keys) * factor
        if mask is not None:
            scores = jnp.where(mask, -1e30, scores)
        top = jnp.max(scores, axis=1, keepdims=True)
        expo = jnp.exp(scores - top)
        weights = expo * (1.0 / jnp.sum(expo, axis=1, keepdims=True))
        rounded = weights.astype(jnp.bfloat16)
        attended = _nn(rounded, values)
        row = jnp.sum(ub.astype(jnp.float32) * attended, axis=1, keepdims=True)
        grad_probs = _nt(ub, values)
        grad_scores = (weights * (grad_probs - row) * factor).astype(jnp.bfloat16)
        query_grad = _nn(grad_scores, keys)
        key_grad = _tn(grad_scores, qb)
        value_grad = _tn(rounded, ub)
        return query_grad, key_grad, value_grad

    keys_all = x_ref[:, 1, :, :].reshape(length, HD)
    values_all = x_ref[:, 2, :, :].reshape(length, HD)
    for index, block in enumerate((0, count - 1)):
        qb = rows(x_ref, 0, block)[...]
        ub = u_ref[block * BLOCK:(block + 1) * BLOCK, :]
        query_grad, key_grad, value_grad = softmax_grads(qb, ub, keys_all, values_all, None)
        rows(o_ref, 0, block)[...] = query_grad.astype(jnp.bfloat16)
        if index == 0:
            dk_acc[...] = key_grad
            dv_acc[...] = value_grad
        else:
            dk_acc[...] += key_grad
            dv_acc[...] += value_grad

    columns = lax.broadcasted_iota(jnp.int32, (BLOCK, SLOTS * BLOCK), 1) // BLOCK

    def mid_step(m, carry):
        base = (m - 1) * RAND
        lower = jnp.where(m - 1 >= 1, m - 1, m)
        upper = jnp.where(m + 1 <= count - 2, m + 1, m)
        ids = [0, count - 1, lower, m, upper] + [rb_ref[base + r] for r in range(RAND)]
        for slot, block in enumerate(ids):
            kg_ref[slot * BLOCK:(slot + 1) * BLOCK, :] = rows(x_ref, 1, block)[...]
            vg_ref[slot * BLOCK:(slot + 1) * BLOCK, :] = rows(x_ref, 2, block)[...]
        start = pl.multiple_of(m * BLOCK, BLOCK)
        qb = rows(x_ref, 0, m)[...]
        ub = u_ref[pl.ds(start, BLOCK), :]
        mask = ((columns == 2) & (m == 1)) | ((columns == 4) & (m == count - 2))
        query_grad, key_grad, value_grad = softmax_grads(qb, ub, kg_ref[...], vg_ref[...], mask)
        rows(o_ref, 0, m)[...] = query_grad.astype(jnp.bfloat16)
        for slot, block in enumerate(ids):
            row = pl.multiple_of(block * BLOCK, BLOCK)
            dk_acc[pl.ds(row, BLOCK), :] += key_grad[slot * BLOCK:(slot + 1) * BLOCK, :]
            dv_acc[pl.ds(row, BLOCK), :] += value_grad[slot * BLOCK:(slot + 1) * BLOCK, :]
        return carry

    lax.fori_loop(1, count - 1, mid_step, 0, unroll=2)
    o_ref[:, 1, :, :] = dk_acc[...].reshape(parts, tokens, HD).astype(jnp.bfloat16)
    o_ref[:, 2, :, :] = dv_acc[...].reshape(parts, tokens, HD).astype(jnp.bfloat16)


def attention_grads(stacked, upstream, head, random_ids):
    parts, _, _, tokens, _ = stacked.shape
    length = parts * tokens
    count = length // BLOCK
    source = pl.BlockSpec((parts, 3, None, tokens, HD), lambda h, rb: (0, 0, head, 0, 0))
    whole = pl.BlockSpec((parts, 3, tokens, HD), lambda h, rb: (0, 0, 0, 0))
    spec = pl.BlockSpec((length, HD), lambda h, rb: (0, head))
    out = jax.ShapeDtypeStruct((parts, 3, tokens, HD), jnp.bfloat16)
    pairs = 2 * BLOCK * length + (count - 2) * BLOCK * SLOTS * BLOCK
    cost = pl.CostEstimate(
        flops=12 * pairs * HD, transcendentals=pairs, bytes_accessed=14 * length * HD
    )
    return pl.pallas_call(
        _attention_kernel,
        out_shape=out,
        grid_spec=pltpu.PrefetchScalarGridSpec(
            num_scalar_prefetch=1,
            grid=(1,),
            in_specs=[source, spec],
            out_specs=whole,
            scratch_shapes=[
                pltpu.VMEM((length, HD), jnp.float32),
                pltpu.VMEM((length, HD), jnp.float32),
                pltpu.VMEM((SLOTS * BLOCK, HD), jnp.bfloat16),
                pltpu.VMEM((SLOTS * BLOCK, HD), jnp.bfloat16),
            ],
        ),
        compiler_params=pltpu.CompilerParams(dimension_semantics=("arbitrary",)),
        cost_estimate=cost,
    )(random_ids.reshape(-1), stacked, upstream)


def _assemble_kernel(*refs):
    pieces, outs = refs[:-3], refs[-3:]
    parts = pieces[0].shape[0]
    for c, piece in enumerate(pieces):
        for source in range(parts):
            start = (c * parts + source) * HD
            for g, out in enumerate(outs):
                out[0, :, start:start + HD] = piece[source, g]


def assemble(pieces, tokens, width):
    out = jax.ShapeDtypeStruct((1, tokens, width), jnp.bfloat16)
    return pl.pallas_call(_assemble_kernel, out_shape=(out, out, out))(*pieces)


def body(queries, key_rows, value_rows, cotangent, out_weight, random_blocks):
    dp = lax.axis_size("dp")
    ctx = lax.axis_size("context")
    local = (queries[0], key_rows[0], value_rows[0])
    local_cotangent = cotangent[0]
    tokens, width = local[0].shape
    total_heads = width // HD
    local_heads = total_heads // ctx
    rows_per_device = out_weight.shape[0]
    strided = rows_per_device == HD and local_heads == dp and ctx % 2 == 0

    if strided:
        me = lax.axis_index("dp")
        got = [out_weight] + [
            lax.ppermute(out_weight, "dp", [(a, (a + s) % dp) for a in range(dp)])
            for s in range(1, dp)
        ]
        order = (me - jnp.arange(dp)) % dp
        head_weight = jnp.take(jnp.stack(got), order, axis=0).reshape(dp * HD, -1)
        j = lax.axis_index("context")
        shifts = list(range(0, ctx, 2))
        mine = jnp.stack([local_cotangent] + [
            lax.ppermute(local_cotangent, "context", [(a, (a + s) % ctx) for a in range(ctx)])
            for s in shifts[1:]
        ])
        other = lax.ppermute(mine, "context", [(a, a ^ 1) for a in range(ctx)])
        gathered = jnp.concatenate([mine, other]).reshape(ctx * tokens, -1)
        upstream = lax.dot_general(
            gathered, head_weight, (((1,), (1,)), ((), ())),
            preferred_element_type=jnp.float32,
        ).astype(jnp.bfloat16)
        source = jnp.arange(ctx)
        same = source % 2 == j % 2
        position = jnp.where(
            same, ((j - source) % ctx) // 2, ctx // 2 + (((j ^ 1) - source) % ctx) // 2
        )
        upstream = jnp.take(upstream.reshape(ctx, tokens, -1), position, axis=0)
        upstream = upstream.reshape(ctx * tokens, -1)

        def chunk(array):
            return array.reshape(tokens, dp, ctx, HD).transpose(2, 1, 0, 3)
    else:
        upstream = lax.dot_general(
            local_cotangent,
            lax.all_gather(out_weight, ("dp", "context"), axis=0, tiled=True),
            (((1,), (1,)), ((), ())),
            preferred_element_type=jnp.float32,
        ).astype(jnp.bfloat16)
        local = local + (upstream,)

        def chunk(array):
            return array.reshape(tokens, ctx, local_heads, HD).transpose(1, 2, 0, 3)

    stacked = jnp.stack([chunk(array) for array in local], axis=1)
    moved = lax.all_to_all(stacked, "context", split_axis=0, concat_axis=0, tiled=True)
    if not strided:
        head_upstream = moved[:, 3].transpose(1, 0, 2, 3).reshape(local_heads, tokens * ctx, HD)
        moved = moved[:, :3]
    pieces = []
    for c in range(local_heads):
        if strided:
            grads = attention_grads(moved, upstream, c, random_blocks[0])
        else:
            grads = attention_grads(moved, head_upstream[c], 0, random_blocks[0])
        back = lax.all_to_all(grads, "context", split_axis=0, concat_axis=0, tiled=True)
        pieces.append(back if strided else back.transpose(1, 2, 0, 3))

    if strided:
        return assemble(pieces, tokens, width)
    outs = []
    for g in range(3):
        joined = jnp.stack([piece[g] for piece in pieces], axis=1 if strided else 2)
        outs.append(joined.reshape(1, tokens, width))
    return tuple(outs)


def solution(mesh):
    return jax.shard_map(
        body,
        mesh=mesh,
        in_specs=(
            P("dp", "context", None),
            P("dp", "context", None),
            P("dp", "context", None),
            P("dp", "context", None),
            P(("dp", "context"), None),
            P("dp", None, None),
        ),
        out_specs=(P("dp", "context", None), P("dp", "context", None), P("dp", "context", None)),
        check_vma=False,
    )
```

```python
import functools
import math

import jax
import jax.numpy as jnp
from jax import lax
from jax.experimental import pallas as pl
from jax.experimental.pallas import tpu as pltpu
from jax.sharding import PartitionSpec as P

HD = 128
BLOCK = 64
RAND = 3
SLOTS = 5 + RAND


def _nt(a, b):
    return lax.dot_general(a, b, (((1,), (1,)), ((), ())), preferred_element_type=jnp.float32)


def _tn(a, b):
    return lax.dot_general(a, b, (((0,), (0,)), ((), ())), preferred_element_type=jnp.float32)


def _nn(a, b):
    return lax.dot_general(a, b, (((1,), (0,)), ((), ())), preferred_element_type=jnp.float32)


def _attention_kernel(rb_ref, x_ref, u_ref, o_ref, dk_acc, dv_acc, kg_ref, vg_ref):
    parts, _, tokens, _ = x_ref.shape
    per_part = tokens // BLOCK
    length = parts * tokens
    count = length // BLOCK
    factor = 1.0 / math.sqrt(HD)

    def rows(ref, which, block):
        if isinstance(block, int):
            offset = (block % per_part) * BLOCK
        else:
            offset = pl.multiple_of((block % per_part) * BLOCK, BLOCK)
        return ref.at[block // per_part, which, pl.ds(offset, BLOCK), :]

    def softmax_grads(qb, ub, keys, values, mask):
        scores = _nt(qb, keys) * factor
        if mask is not None:
            scores = jnp.where(mask, -1e30, scores)
        top = jnp.max(scores, axis=1, keepdims=True)
        expo = jnp.exp(scores - top)
        weights = expo * (1.0 / jnp.sum(expo, axis=1, keepdims=True))
        rounded = weights.astype(jnp.bfloat16)
        attended = _nn(rounded, values)
        row = jnp.sum(ub.astype(jnp.float32) * attended, axis=1, keepdims=True)
        grad_probs = _nt(ub, values)
        grad_scores = (weights * (grad_probs - row) * factor).astype(jnp.bfloat16)
        query_grad = _nn(grad_scores, keys)
        key_grad = _tn(grad_scores, qb)
        value_grad = _tn(rounded, ub)
        return query_grad, key_grad, value_grad

    keys_all = x_ref[:, 1, :, :].reshape(length, HD)
    values_all = x_ref[:, 2, :, :].reshape(length, HD)
    last = count - 1
    qb = jnp.concatenate([rows(x_ref, 0, 0)[...], rows(x_ref, 0, last)[...]], axis=0)
    ub = jnp.concatenate(
        [u_ref[0:BLOCK, :], u_ref[last * BLOCK:(last + 1) * BLOCK, :]], axis=0
    )
    query_grad, key_grad, value_grad = softmax_grads(qb, ub, keys_all, values_all, None)
    query_grad = query_grad.astype(jnp.bfloat16)
    rows(o_ref, 0, 0)[...] = query_grad[:BLOCK]
    rows(o_ref, 0, last)[...] = query_grad[BLOCK:]
    dk_acc[...] = key_grad
    dv_acc[...] = value_grad

    columns = lax.broadcasted_iota(jnp.int32, (BLOCK, SLOTS * BLOCK), 1) // BLOCK

    def mid_step(m, carry):
        base = (m - 1) * RAND
        lower = jnp.where(m - 1 >= 1, m - 1, m)
        upper = jnp.where(m + 1 <= count - 2, m + 1, m)
        ids = [0, count - 1, lower, m, upper] + [rb_ref[base + r] for r in range(RAND)]
        for slot, block in enumerate(ids):
            kg_ref[slot * BLOCK:(slot + 1) * BLOCK, :] = rows(x_ref, 1, block)[...]
            vg_ref[slot * BLOCK:(slot + 1) * BLOCK, :] = rows(x_ref, 2, block)[...]
        start = pl.multiple_of(m * BLOCK, BLOCK)
        qb = rows(x_ref, 0, m)[...]
        ub = u_ref[pl.ds(start, BLOCK), :]
        mask = ((columns == 2) & (m == 1)) | ((columns == 4) & (m == count - 2))
        query_grad, key_grad, value_grad = softmax_grads(qb, ub, kg_ref[...], vg_ref[...], mask)
        rows(o_ref, 0, m)[...] = query_grad.astype(jnp.bfloat16)
        for slot, block in enumerate(ids):
            row = pl.multiple_of(block * BLOCK, BLOCK)
            dk_acc[pl.ds(row, BLOCK), :] += key_grad[slot * BLOCK:(slot + 1) * BLOCK, :]
            dv_acc[pl.ds(row, BLOCK), :] += value_grad[slot * BLOCK:(slot + 1) * BLOCK, :]
        return carry

    lax.fori_loop(1, count - 1, mid_step, 0, unroll=2)
    o_ref[:, 1, :, :] = dk_acc[...].reshape(parts, tokens, HD).astype(jnp.bfloat16)
    o_ref[:, 2, :, :] = dv_acc[...].reshape(parts, tokens, HD).astype(jnp.bfloat16)


def attention_grads(stacked, upstream, head, random_ids):
    parts, _, _, tokens, _ = stacked.shape
    length = parts * tokens
    count = length // BLOCK
    source = pl.BlockSpec((parts, 3, None, tokens, HD), lambda h, rb: (0, 0, head, 0, 0))
    whole = pl.BlockSpec((parts, 3, tokens, HD), lambda h, rb: (0, 0, 0, 0))
    spec = pl.BlockSpec((length, HD), lambda h, rb: (0, head))
    out = jax.ShapeDtypeStruct((parts, 3, tokens, HD), jnp.bfloat16)
    pairs = 2 * BLOCK * length + (count - 2) * BLOCK * SLOTS * BLOCK
    cost = pl.CostEstimate(
        flops=12 * pairs * HD, transcendentals=pairs, bytes_accessed=14 * length * HD
    )
    return pl.pallas_call(
        _attention_kernel,
        out_shape=out,
        grid_spec=pltpu.PrefetchScalarGridSpec(
            num_scalar_prefetch=1,
            grid=(1,),
            in_specs=[source, spec],
            out_specs=whole,
            scratch_shapes=[
                pltpu.VMEM((length, HD), jnp.float32),
                pltpu.VMEM((length, HD), jnp.float32),
                pltpu.VMEM((SLOTS * BLOCK, HD), jnp.bfloat16),
                pltpu.VMEM((SLOTS * BLOCK, HD), jnp.bfloat16),
            ],
        ),
        compiler_params=pltpu.CompilerParams(dimension_semantics=("arbitrary",)),
        cost_estimate=cost,
    )(random_ids.reshape(-1), stacked, upstream)


def _assemble_kernel(*refs):
    pieces, outs = refs[:-3], refs[-3:]
    parts = pieces[0].shape[0]
    for c, piece in enumerate(pieces):
        for source in range(parts):
            start = (c * parts + source) * HD
            for g, out in enumerate(outs):
                out[0, :, start:start + HD] = piece[source, g]


def assemble(pieces, tokens, width):
    out = jax.ShapeDtypeStruct((1, tokens, width), jnp.bfloat16)
    return pl.pallas_call(_assemble_kernel, out_shape=(out, out, out))(*pieces)


def body(queries, key_rows, value_rows, cotangent, out_weight, random_blocks):
    dp = lax.axis_size("dp")
    ctx = lax.axis_size("context")
    local = (queries[0], key_rows[0], value_rows[0])
    local_cotangent = cotangent[0]
    tokens, width = local[0].shape
    total_heads = width // HD
    local_heads = total_heads // ctx
    rows_per_device = out_weight.shape[0]
    strided = rows_per_device == HD and local_heads == dp and ctx % 2 == 0

    if strided:
        me = lax.axis_index("dp")
        got = [out_weight] + [
            lax.ppermute(out_weight, "dp", [(a, (a + s) % dp) for a in range(dp)])
            for s in range(1, dp)
        ]
        order = (me - jnp.arange(dp)) % dp
        head_weight = jnp.take(jnp.stack(got), order, axis=0).reshape(dp * HD, -1)
        j = lax.axis_index("context")
        shifts = list(range(0, ctx, 2))
        mine = jnp.stack([local_cotangent] + [
            lax.ppermute(local_cotangent, "context", [(a, (a + s) % ctx) for a in range(ctx)])
            for s in shifts[1:]
        ])
        other = lax.ppermute(mine, "context", [(a, a ^ 1) for a in range(ctx)])
        gathered = jnp.concatenate([mine, other]).reshape(ctx * tokens, -1)
        upstream = lax.dot_general(
            gathered, head_weight, (((1,), (1,)), ((), ())),
            preferred_element_type=jnp.float32,
        ).astype(jnp.bfloat16)
        source = jnp.arange(ctx)
        same = source % 2 == j % 2
        position = jnp.where(
            same, ((j - source) % ctx) // 2, ctx // 2 + (((j ^ 1) - source) % ctx) // 2
        )
        upstream = jnp.take(upstream.reshape(ctx, tokens, -1), position, axis=0)
        upstream = upstream.reshape(ctx * tokens, -1)

        def chunk(array):
            return array.reshape(tokens, dp, ctx, HD).transpose(2, 1, 0, 3)
    else:
        upstream = lax.dot_general(
            local_cotangent,
            lax.all_gather(out_weight, ("dp", "context"), axis=0, tiled=True),
            (((1,), (1,)), ((), ())),
            preferred_element_type=jnp.float32,
        ).astype(jnp.bfloat16)
        local = local + (upstream,)

        def chunk(array):
            return array.reshape(tokens, ctx, local_heads, HD).transpose(1, 2, 0, 3)

    stacked = jnp.stack([chunk(array) for array in local], axis=1)
    moved = lax.all_to_all(stacked, "context", split_axis=0, concat_axis=0, tiled=True)
    if not strided:
        head_upstream = moved[:, 3].transpose(1, 0, 2, 3).reshape(local_heads, tokens * ctx, HD)
        moved = moved[:, :3]
    pieces = []
    for c in range(local_heads):
        if strided:
            grads = attention_grads(moved, upstream, c, random_blocks[0])
        else:
            grads = attention_grads(moved, head_upstream[c], 0, random_blocks[0])
        back = lax.all_to_all(grads, "context", split_axis=0, concat_axis=0, tiled=True)
        pieces.append(back if strided else back.transpose(1, 2, 0, 3))

    if strided:
        return assemble(pieces, tokens, width)
    outs = []
    for g in range(3):
        joined = jnp.stack([piece[g] for piece in pieces], axis=1 if strided else 2)
        outs.append(joined.reshape(1, tokens, width))
    return tuple(outs)


def solution(mesh):
    return jax.shard_map(
        body,
        mesh=mesh,
        in_specs=(
            P("dp", "context", None),
            P("dp", "context", None),
            P("dp", "context", None),
            P("dp", "context", None),
            P(("dp", "context"), None),
            P("dp", None, None),
        ),
        out_specs=(P("dp", "context", None), P("dp", "context", None), P("dp", "context", None)),
        check_vma=False,
    )
```

```python
import functools
import math

import jax
import jax.numpy as jnp
from jax import lax
from jax.experimental import pallas as pl
from jax.experimental.pallas import tpu as pltpu
from jax.sharding import PartitionSpec as P

HD = 128
BLOCK = 64
RAND = 3
SLOTS = 5 + RAND


def _nt(a, b):
    return lax.dot_general(a, b, (((1,), (1,)), ((), ())), preferred_element_type=jnp.float32)


def _tn(a, b):
    return lax.dot_general(a, b, (((0,), (0,)), ((), ())), preferred_element_type=jnp.float32)


def _nn(a, b):
    return lax.dot_general(a, b, (((1,), (0,)), ((), ())), preferred_element_type=jnp.float32)


def _attention_kernel(rb_ref, x_ref, u_ref, o_ref, dk_acc, dv_acc, kg_ref, vg_ref):
    parts, _, tokens, _ = x_ref.shape
    per_part = tokens // BLOCK
    length = parts * tokens
    count = length // BLOCK
    factor = 1.0 / math.sqrt(HD)

    def rows(ref, which, block):
        if isinstance(block, int):
            offset = (block % per_part) * BLOCK
        else:
            offset = pl.multiple_of((block % per_part) * BLOCK, BLOCK)
        return ref.at[block // per_part, which, pl.ds(offset, BLOCK), :]

    def softmax_grads(qb, ub, keys, values, mask):
        scores = _nt(qb, keys) * factor
        if mask is not None:
            scores = jnp.where(mask, -1e30, scores)
        top = jnp.max(scores, axis=1, keepdims=True)
        expo = jnp.exp(scores - top)
        weights = expo * (1.0 / jnp.sum(expo, axis=1, keepdims=True))
        rounded = weights.astype(jnp.bfloat16)
        attended = _nn(rounded, values)
        row = jnp.sum(ub.astype(jnp.float32) * attended, axis=1, keepdims=True)
        grad_probs = _nt(ub, values)
        grad_scores = (weights * (grad_probs - row) * factor).astype(jnp.bfloat16)
        query_grad = _nn(grad_scores, keys)
        key_grad = _tn(grad_scores, qb)
        value_grad = _tn(rounded, ub)
        return query_grad, key_grad, value_grad

    keys_all = x_ref[:, 1, :, :].reshape(length, HD)
    values_all = x_ref[:, 2, :, :].reshape(length, HD)
    last = count - 1
    qb = jnp.concatenate([rows(x_ref, 0, 0)[...], rows(x_ref, 0, last)[...]], axis=0)
    ub = jnp.concatenate(
        [u_ref[0:BLOCK, :], u_ref[last * BLOCK:(last + 1) * BLOCK, :]], axis=0
    )
    query_grad, key_grad, value_grad = softmax_grads(qb, ub, keys_all, values_all, None)
    query_grad = query_grad.astype(jnp.bfloat16)
    rows(o_ref, 0, 0)[...] = query_grad[:BLOCK]
    rows(o_ref, 0, last)[...] = query_grad[BLOCK:]
    dk_acc[...] = key_grad
    dv_acc[...] = value_grad

    columns = lax.broadcasted_iota(jnp.int32, (BLOCK, SLOTS * BLOCK), 1) // BLOCK

    def mid_step(m, carry):
        base = (m - 1) * RAND
        lower = jnp.where(m - 1 >= 1, m - 1, m)
        upper = jnp.where(m + 1 <= count - 2, m + 1, m)
        ids = [0, count - 1, lower, m, upper] + [rb_ref[base + r] for r in range(RAND)]
        for slot, block in enumerate(ids):
            kg_ref[slot * BLOCK:(slot + 1) * BLOCK, :] = rows(x_ref, 1, block)[...]
            vg_ref[slot * BLOCK:(slot + 1) * BLOCK, :] = rows(x_ref, 2, block)[...]
        start = pl.multiple_of(m * BLOCK, BLOCK)
        qb = rows(x_ref, 0, m)[...]
        ub = u_ref[pl.ds(start, BLOCK), :]
        mask = ((columns == 2) & (m == 1)) | ((columns == 4) & (m == count - 2))
        query_grad, key_grad, value_grad = softmax_grads(qb, ub, kg_ref[...], vg_ref[...], mask)
        rows(o_ref, 0, m)[...] = query_grad.astype(jnp.bfloat16)
        for slot, block in enumerate(ids):
            row = pl.multiple_of(block * BLOCK, BLOCK)
            dk_acc[pl.ds(row, BLOCK), :] += key_grad[slot * BLOCK:(slot + 1) * BLOCK, :]
            dv_acc[pl.ds(row, BLOCK), :] += value_grad[slot * BLOCK:(slot + 1) * BLOCK, :]
        return carry

    lax.fori_loop(1, count - 1, mid_step, 0, unroll=2)
    o_ref[:, 1, :, :] = dk_acc[...].reshape(parts, tokens, HD).astype(jnp.bfloat16)
    o_ref[:, 2, :, :] = dv_acc[...].reshape(parts, tokens, HD).astype(jnp.bfloat16)


def attention_grads(stacked, upstream, head, random_ids):
    parts, _, _, tokens, _ = stacked.shape
    length = parts * tokens
    count = length // BLOCK
    source = pl.BlockSpec((parts, 3, None, tokens, HD), lambda h, rb: (0, 0, head, 0, 0))
    whole = pl.BlockSpec((parts, 3, tokens, HD), lambda h, rb: (0, 0, 0, 0))
    spec = pl.BlockSpec((length, HD), lambda h, rb: (0, head))
    out = jax.ShapeDtypeStruct((parts, 3, tokens, HD), jnp.bfloat16)
    pairs = 2 * BLOCK * length + (count - 2) * BLOCK * SLOTS * BLOCK
    cost = pl.CostEstimate(
        flops=12 * pairs * HD, transcendentals=pairs, bytes_accessed=14 * length * HD
    )
    return pl.pallas_call(
        _attention_kernel,
        out_shape=out,
        grid_spec=pltpu.PrefetchScalarGridSpec(
            num_scalar_prefetch=1,
            grid=(1,),
            in_specs=[source, spec],
            out_specs=whole,
            scratch_shapes=[
                pltpu.VMEM((length, HD), jnp.float32),
                pltpu.VMEM((length, HD), jnp.float32),
                pltpu.VMEM((SLOTS * BLOCK, HD), jnp.bfloat16),
                pltpu.VMEM((SLOTS * BLOCK, HD), jnp.bfloat16),
            ],
        ),
        compiler_params=pltpu.CompilerParams(dimension_semantics=("arbitrary",)),
        cost_estimate=cost,
    )(random_ids.reshape(-1), stacked, upstream)


def _assemble_kernel(*refs):
    *pieces, first, second, third, sems = refs
    outs = (first, second, third)
    parts = pieces[0].shape[0]
    copies = []
    for c, piece in enumerate(pieces):
        for source in range(parts):
            start = (c * parts + source) * HD
            for g, out in enumerate(outs):
                copy = pltpu.make_async_copy(
                    piece.at[source, g], out.at[0, :, pl.ds(start, HD)], sems.at[len(copies)]
                )
                copy.start()
                copies.append(copy)
    for copy in copies:
        copy.wait()


def assemble(pieces, tokens, width):
    out = jax.ShapeDtypeStruct((1, tokens, width), jnp.bfloat16)
    total = len(pieces) * pieces[0].shape[0] * 3
    anywhere = pl.BlockSpec(memory_space=pl.ANY)
    return pl.pallas_call(
        _assemble_kernel,
        out_shape=(out, out, out),
        in_specs=[anywhere] * len(pieces),
        out_specs=(anywhere, anywhere, anywhere),
        scratch_shapes=[pltpu.SemaphoreType.DMA((total,))],
    )(*pieces)


def body(queries, key_rows, value_rows, cotangent, out_weight, random_blocks):
    dp = lax.axis_size("dp")
    ctx = lax.axis_size("context")
    local = (queries[0], key_rows[0], value_rows[0])
    local_cotangent = cotangent[0]
    tokens, width = local[0].shape
    total_heads = width // HD
    local_heads = total_heads // ctx
    rows_per_device = out_weight.shape[0]
    strided = rows_per_device == HD and local_heads == dp and ctx % 2 == 0

    if strided:
        me = lax.axis_index("dp")
        got = [out_weight] + [
            lax.ppermute(out_weight, "dp", [(a, (a + s) % dp) for a in range(dp)])
            for s in range(1, dp)
        ]
        order = (me - jnp.arange(dp)) % dp
        head_weight = jnp.take(jnp.stack(got), order, axis=0).reshape(dp * HD, -1)
        j = lax.axis_index("context")
        shifts = list(range(0, ctx, 2))
        mine = jnp.stack([local_cotangent] + [
            lax.ppermute(local_cotangent, "context", [(a, (a + s) % ctx) for a in range(ctx)])
            for s in shifts[1:]
        ])
        other = lax.ppermute(mine, "context", [(a, a ^ 1) for a in range(ctx)])
        gathered = jnp.concatenate([mine, other]).reshape(ctx * tokens, -1)
        upstream = lax.dot_general(
            gathered, head_weight, (((1,), (1,)), ((), ())),
            preferred_element_type=jnp.float32,
        ).astype(jnp.bfloat16)
        source = jnp.arange(ctx)
        same = source % 2 == j % 2
        position = jnp.where(
            same, ((j - source) % ctx) // 2, ctx // 2 + (((j ^ 1) - source) % ctx) // 2
        )
        upstream = jnp.take(upstream.reshape(ctx, tokens, -1), position, axis=0)
        upstream = upstream.reshape(ctx * tokens, -1)

        def chunk(array):
            return array.reshape(tokens, dp, ctx, HD).transpose(2, 1, 0, 3)
    else:
        upstream = lax.dot_general(
            local_cotangent,
            lax.all_gather(out_weight, ("dp", "context"), axis=0, tiled=True),
            (((1,), (1,)), ((), ())),
            preferred_element_type=jnp.float32,
        ).astype(jnp.bfloat16)
        local = local + (upstream,)

        def chunk(array):
            return array.reshape(tokens, ctx, local_heads, HD).transpose(1, 2, 0, 3)

    stacked = jnp.stack([chunk(array) for array in local], axis=1)
    moved = lax.all_to_all(stacked, "context", split_axis=0, concat_axis=0, tiled=True)
    if not strided:
        head_upstream = moved[:, 3].transpose(1, 0, 2, 3).reshape(local_heads, tokens * ctx, HD)
        moved = moved[:, :3]
    pieces = []
    for c in range(local_heads):
        if strided:
            grads = attention_grads(moved, upstream, c, random_blocks[0])
        else:
            grads = attention_grads(moved, head_upstream[c], 0, random_blocks[0])
        back = lax.all_to_all(grads, "context", split_axis=0, concat_axis=0, tiled=True)
        pieces.append(back if strided else back.transpose(1, 2, 0, 3))

    if strided:
        return assemble(pieces, tokens, width)
    outs = []
    for g in range(3):
        joined = jnp.stack([piece[g] for piece in pieces], axis=1 if strided else 2)
        outs.append(joined.reshape(1, tokens, width))
    return tuple(outs)


def solution(mesh):
    return jax.shard_map(
        body,
        mesh=mesh,
        in_specs=(
            P("dp", "context", None),
            P("dp", "context", None),
            P("dp", "context", None),
            P("dp", "context", None),
            P(("dp", "context"), None),
            P("dp", None, None),
        ),
        out_specs=(P("dp", "context", None), P("dp", "context", None), P("dp", "context", None)),
        check_vma=False,
    )
```

```python
import functools
import math

import jax
import jax.numpy as jnp
from jax import lax
from jax.experimental import pallas as pl
from jax.experimental.pallas import tpu as pltpu
from jax.sharding import PartitionSpec as P

HD = 128
BLOCK = 64
RAND = 3
SLOTS = 5 + RAND


def _nt(a, b):
    return lax.dot_general(a, b, (((1,), (1,)), ((), ())), preferred_element_type=jnp.float32)


def _tn(a, b):
    return lax.dot_general(a, b, (((0,), (0,)), ((), ())), preferred_element_type=jnp.float32)


def _nn(a, b):
    return lax.dot_general(a, b, (((1,), (0,)), ((), ())), preferred_element_type=jnp.float32)


def _attention_kernel(rb_ref, x_ref, u_ref, o_ref, dk_acc, dv_acc, kg_ref, vg_ref):
    parts, _, tokens, _ = x_ref.shape
    per_part = tokens // BLOCK
    length = parts * tokens
    count = length // BLOCK
    factor = 1.0 / math.sqrt(HD)

    def rows(ref, which, block):
        if isinstance(block, int):
            offset = (block % per_part) * BLOCK
        else:
            offset = pl.multiple_of((block % per_part) * BLOCK, BLOCK)
        return ref.at[block // per_part, which, pl.ds(offset, BLOCK), :]

    def softmax_grads(qb, ub, keys, values, mask):
        scores = _nt(qb, keys) * factor
        if mask is not None:
            scores = jnp.where(mask, -1e30, scores)
        top = jnp.max(scores, axis=1, keepdims=True)
        expo = jnp.exp(scores - top)
        weights = expo * (1.0 / jnp.sum(expo, axis=1, keepdims=True))
        rounded = weights.astype(jnp.bfloat16)
        attended = _nn(rounded, values)
        row = jnp.sum(ub.astype(jnp.float32) * attended, axis=1, keepdims=True)
        grad_probs = _nt(ub, values)
        grad_scores = (weights * (grad_probs - row) * factor).astype(jnp.bfloat16)
        query_grad = _nn(grad_scores, keys)
        key_grad = _tn(grad_scores, qb)
        value_grad = _tn(rounded, ub)
        return query_grad, key_grad, value_grad

    keys_all = x_ref[:, 1, :, :].reshape(length, HD)
    values_all = x_ref[:, 2, :, :].reshape(length, HD)
    last = count - 1
    qb = jnp.concatenate([rows(x_ref, 0, 0)[...], rows(x_ref, 0, last)[...]], axis=0)
    ub = jnp.concatenate(
        [u_ref[0:BLOCK, :], u_ref[last * BLOCK:(last + 1) * BLOCK, :]], axis=0
    )
    query_grad, key_grad, value_grad = softmax_grads(qb, ub, keys_all, values_all, None)
    query_grad = query_grad.astype(jnp.bfloat16)
    rows(o_ref, 0, 0)[...] = query_grad[:BLOCK]
    rows(o_ref, 0, last)[...] = query_grad[BLOCK:]
    dk_acc[...] = key_grad
    dv_acc[...] = value_grad

    columns = lax.broadcasted_iota(jnp.int32, (BLOCK, SLOTS * BLOCK), 1) // BLOCK

    def mid_step(m, carry):
        base = (m - 1) * RAND
        lower = jnp.where(m - 1 >= 1, m - 1, m)
        upper = jnp.where(m + 1 <= count - 2, m + 1, m)
        ids = [0, count - 1, lower, m, upper] + [rb_ref[base + r] for r in range(RAND)]
        for slot, block in enumerate(ids):
            kg_ref[slot * BLOCK:(slot + 1) * BLOCK, :] = rows(x_ref, 1, block)[...]
            vg_ref[slot * BLOCK:(slot + 1) * BLOCK, :] = rows(x_ref, 2, block)[...]
        start = pl.multiple_of(m * BLOCK, BLOCK)
        qb = rows(x_ref, 0, m)[...]
        ub = u_ref[pl.ds(start, BLOCK), :]
        mask = ((columns == 2) & (m == 1)) | ((columns == 4) & (m == count - 2))
        query_grad, key_grad, value_grad = softmax_grads(qb, ub, kg_ref[...], vg_ref[...], mask)
        rows(o_ref, 0, m)[...] = query_grad.astype(jnp.bfloat16)
        for slot, block in enumerate(ids):
            row = pl.multiple_of(block * BLOCK, BLOCK)
            dk_acc[pl.ds(row, BLOCK), :] += key_grad[slot * BLOCK:(slot + 1) * BLOCK, :]
            dv_acc[pl.ds(row, BLOCK), :] += value_grad[slot * BLOCK:(slot + 1) * BLOCK, :]
        return carry

    lax.fori_loop(1, count - 1, mid_step, 0, unroll=2)
    o_ref[:, 1, :, :] = dk_acc[...].reshape(parts, tokens, HD).astype(jnp.bfloat16)
    o_ref[:, 2, :, :] = dv_acc[...].reshape(parts, tokens, HD).astype(jnp.bfloat16)


def attention_grads(stacked, upstream, head, random_ids):
    parts, _, _, tokens, _ = stacked.shape
    length = parts * tokens
    count = length // BLOCK
    source = pl.BlockSpec((parts, 3, None, tokens, HD), lambda h, rb: (0, 0, head, 0, 0))
    whole = pl.BlockSpec((parts, 3, tokens, HD), lambda h, rb: (0, 0, 0, 0))
    spec = pl.BlockSpec((length, HD), lambda h, rb: (0, head))
    out = jax.ShapeDtypeStruct((parts, 3, tokens, HD), jnp.bfloat16)
    pairs = 2 * BLOCK * length + (count - 2) * BLOCK * SLOTS * BLOCK
    cost = pl.CostEstimate(
        flops=12 * pairs * HD, transcendentals=pairs, bytes_accessed=14 * length * HD
    )
    return pl.pallas_call(
        _attention_kernel,
        out_shape=out,
        grid_spec=pltpu.PrefetchScalarGridSpec(
            num_scalar_prefetch=1,
            grid=(1,),
            in_specs=[source, spec],
            out_specs=whole,
            scratch_shapes=[
                pltpu.VMEM((length, HD), jnp.float32),
                pltpu.VMEM((length, HD), jnp.float32),
                pltpu.VMEM((SLOTS * BLOCK, HD), jnp.bfloat16),
                pltpu.VMEM((SLOTS * BLOCK, HD), jnp.bfloat16),
            ],
        ),
        compiler_params=pltpu.CompilerParams(dimension_semantics=("arbitrary",)),
        cost_estimate=cost,
    )(random_ids.reshape(-1), stacked, upstream)


def _assemble_kernel(*refs, first_head):
    pieces, outs = refs[:-3], refs[-3:]
    parts = pieces[0].shape[0]
    for c, piece in enumerate(pieces):
        for source in range(parts):
            start = (c * parts + source) * HD
            for g, out in enumerate(outs):
                out[0, :, start:start + HD] = piece[source, g]


def assemble(pieces, tokens, width):
    out = jax.ShapeDtypeStruct((1, tokens, width), jnp.bfloat16)
    span = pieces[0].shape[0] * HD
    early = len(pieces) - 1
    whole = pl.BlockSpec(memory_space=pltpu.VMEM)
    head_spec = pl.BlockSpec((1, tokens, early * span), lambda i: (0, 0, 0))
    partial = pl.pallas_call(
        functools.partial(_assemble_kernel, first_head=0),
        out_shape=(out, out, out),
        grid=(1,),
        in_specs=[whole] * early,
        out_specs=(head_spec, head_spec, head_spec),
    )(*pieces[:early])
    last_spec = pl.BlockSpec((1, tokens, span), lambda i: (0, 0, early))
    return pl.pallas_call(
        _assemble_last_kernel,
        out_shape=(out, out, out),
        grid=(1,),
        in_specs=[whole, last_spec, last_spec, last_spec],
        out_specs=(last_spec, last_spec, last_spec),
        input_output_aliases={1: 0, 2: 1, 3: 2},
    )(pieces[early], *partial)


def _assemble_last_kernel(piece, _first, _second, _third, *outs):
    parts = piece.shape[0]
    for source in range(parts):
        for g, out in enumerate(outs):
            out[0, :, source * HD:(source + 1) * HD] = piece[source, g]


def body(queries, key_rows, value_rows, cotangent, out_weight, random_blocks):
    dp = lax.axis_size("dp")
    ctx = lax.axis_size("context")
    local = (queries[0], key_rows[0], value_rows[0])
    local_cotangent = cotangent[0]
    tokens, width = local[0].shape
    total_heads = width // HD
    local_heads = total_heads // ctx
    rows_per_device = out_weight.shape[0]
    strided = rows_per_device == HD and local_heads == dp and ctx % 2 == 0

    if strided:
        me = lax.axis_index("dp")
        got = [out_weight] + [
            lax.ppermute(out_weight, "dp", [(a, (a + s) % dp) for a in range(dp)])
            for s in range(1, dp)
        ]
        order = (me - jnp.arange(dp)) % dp
        head_weight = jnp.take(jnp.stack(got), order, axis=0).reshape(dp * HD, -1)
        j = lax.axis_index("context")
        shifts = list(range(0, ctx, 2))
        mine = jnp.stack([local_cotangent] + [
            lax.ppermute(local_cotangent, "context", [(a, (a + s) % ctx) for a in range(ctx)])
            for s in shifts[1:]
        ])
        other = lax.ppermute(mine, "context", [(a, a ^ 1) for a in range(ctx)])
        gathered = jnp.concatenate([mine, other]).reshape(ctx * tokens, -1)
        upstream = lax.dot_general(
            gathered, head_weight, (((1,), (1,)), ((), ())),
            preferred_element_type=jnp.float32,
        ).astype(jnp.bfloat16)
        source = jnp.arange(ctx)
        same = source % 2 == j % 2
        position = jnp.where(
            same, ((j - source) % ctx) // 2, ctx // 2 + (((j ^ 1) - source) % ctx) // 2
        )
        upstream = jnp.take(upstream.reshape(ctx, tokens, -1), position, axis=0)
        upstream = upstream.reshape(ctx * tokens, -1)

        def chunk(array):
            return array.reshape(tokens, dp, ctx, HD).transpose(2, 1, 0, 3)
    else:
        upstream = lax.dot_general(
            local_cotangent,
            lax.all_gather(out_weight, ("dp", "context"), axis=0, tiled=True),
            (((1,), (1,)), ((), ())),
            preferred_element_type=jnp.float32,
        ).astype(jnp.bfloat16)
        local = local + (upstream,)

        def chunk(array):
            return array.reshape(tokens, ctx, local_heads, HD).transpose(1, 2, 0, 3)

    stacked = jnp.stack([chunk(array) for array in local], axis=1)
    moved = lax.all_to_all(stacked, "context", split_axis=0, concat_axis=0, tiled=True)
    if not strided:
        head_upstream = moved[:, 3].transpose(1, 0, 2, 3).reshape(local_heads, tokens * ctx, HD)
        moved = moved[:, :3]
    pieces = []
    for c in range(local_heads):
        if strided:
            grads = attention_grads(moved, upstream, c, random_blocks[0])
        else:
            grads = attention_grads(moved, head_upstream[c], 0, random_blocks[0])
        back = lax.all_to_all(grads, "context", split_axis=0, concat_axis=0, tiled=True)
        pieces.append(back if strided else back.transpose(1, 2, 0, 3))

    if strided:
        return assemble(pieces, tokens, width)
    outs = []
    for g in range(3):
        joined = jnp.stack([piece[g] for piece in pieces], axis=1 if strided else 2)
        outs.append(joined.reshape(1, tokens, width))
    return tuple(outs)


def solution(mesh):
    return jax.shard_map(
        body,
        mesh=mesh,
        in_specs=(
            P("dp", "context", None),
            P("dp", "context", None),
            P("dp", "context", None),
            P("dp", "context", None),
            P(("dp", "context"), None),
            P("dp", None, None),
        ),
        out_specs=(P("dp", "context", None), P("dp", "context", None), P("dp", "context", None)),
        check_vma=False,
    )
```

```python
import functools
import math

import jax
import jax.numpy as jnp
from jax import lax
from jax.experimental import pallas as pl
from jax.experimental.pallas import tpu as pltpu
from jax.sharding import PartitionSpec as P

HD = 128
BLOCK = 64
RAND = 3
SLOTS = 5 + RAND


def _nt(a, b):
    return lax.dot_general(a, b, (((1,), (1,)), ((), ())), preferred_element_type=jnp.float32)


def _tn(a, b):
    return lax.dot_general(a, b, (((0,), (0,)), ((), ())), preferred_element_type=jnp.float32)


def _nn(a, b):
    return lax.dot_general(a, b, (((1,), (0,)), ((), ())), preferred_element_type=jnp.float32)


def _attention_kernel(rb_ref, pos_ref, x_ref, u_ref, o_ref, dk_acc, dv_acc, kg_ref, vg_ref):
    parts, _, tokens, _ = x_ref.shape
    per_part = tokens // BLOCK
    length = parts * tokens
    count = length // BLOCK
    factor = 1.0 / math.sqrt(HD)

    def rows(ref, which, block):
        if isinstance(block, int):
            offset = (block % per_part) * BLOCK
        else:
            offset = pl.multiple_of((block % per_part) * BLOCK, BLOCK)
        return ref.at[block // per_part, which, pl.ds(offset, BLOCK), :]

    def upstream_rows(block):
        offset = pos_ref[block // per_part] * tokens + (block % per_part) * BLOCK
        return u_ref[pl.ds(pl.multiple_of(offset, BLOCK), BLOCK), :]

    def softmax_grads(qb, ub, keys, values, mask):
        scores = _nt(qb, keys) * factor
        if mask is not None:
            scores = jnp.where(mask, -1e30, scores)
        top = jnp.max(scores, axis=1, keepdims=True)
        expo = jnp.exp(scores - top)
        weights = expo * (1.0 / jnp.sum(expo, axis=1, keepdims=True))
        rounded = weights.astype(jnp.bfloat16)
        attended = _nn(rounded, values)
        row = jnp.sum(ub.astype(jnp.float32) * attended, axis=1, keepdims=True)
        grad_probs = _nt(ub, values)
        grad_scores = (weights * (grad_probs - row) * factor).astype(jnp.bfloat16)
        query_grad = _nn(grad_scores, keys)
        key_grad = _tn(grad_scores, qb)
        value_grad = _tn(rounded, ub)
        return query_grad, key_grad, value_grad

    keys_all = x_ref[:, 1, :, :].reshape(length, HD)
    values_all = x_ref[:, 2, :, :].reshape(length, HD)
    last = count - 1
    qb = jnp.concatenate([rows(x_ref, 0, 0)[...], rows(x_ref, 0, last)[...]], axis=0)
    ub = jnp.concatenate([upstream_rows(0), upstream_rows(last)], axis=0)
    query_grad, key_grad, value_grad = softmax_grads(qb, ub, keys_all, values_all, None)
    query_grad = query_grad.astype(jnp.bfloat16)
    rows(o_ref, 0, 0)[...] = query_grad[:BLOCK]
    rows(o_ref, 0, last)[...] = query_grad[BLOCK:]
    dk_acc[...] = key_grad
    dv_acc[...] = value_grad

    columns = lax.broadcasted_iota(jnp.int32, (BLOCK, SLOTS * BLOCK), 1) // BLOCK

    def mid_step(m, carry):
        base = (m - 1) * RAND
        lower = jnp.where(m - 1 >= 1, m - 1, m)
        upper = jnp.where(m + 1 <= count - 2, m + 1, m)
        ids = [0, count - 1, lower, m, upper] + [rb_ref[base + r] for r in range(RAND)]
        for slot, block in enumerate(ids):
            kg_ref[slot * BLOCK:(slot + 1) * BLOCK, :] = rows(x_ref, 1, block)[...]
            vg_ref[slot * BLOCK:(slot + 1) * BLOCK, :] = rows(x_ref, 2, block)[...]
        start = pl.multiple_of(m * BLOCK, BLOCK)
        qb = rows(x_ref, 0, m)[...]
        ub = upstream_rows(m)
        mask = ((columns == 2) & (m == 1)) | ((columns == 4) & (m == count - 2))
        query_grad, key_grad, value_grad = softmax_grads(qb, ub, kg_ref[...], vg_ref[...], mask)
        rows(o_ref, 0, m)[...] = query_grad.astype(jnp.bfloat16)
        for slot, block in enumerate(ids):
            row = pl.multiple_of(block * BLOCK, BLOCK)
            dk_acc[pl.ds(row, BLOCK), :] += key_grad[slot * BLOCK:(slot + 1) * BLOCK, :]
            dv_acc[pl.ds(row, BLOCK), :] += value_grad[slot * BLOCK:(slot + 1) * BLOCK, :]
        return carry

    lax.fori_loop(1, count - 1, mid_step, 0, unroll=2)
    o_ref[:, 1, :, :] = dk_acc[...].reshape(parts, tokens, HD).astype(jnp.bfloat16)
    o_ref[:, 2, :, :] = dv_acc[...].reshape(parts, tokens, HD).astype(jnp.bfloat16)


def attention_grads(stacked, upstream, head, positions, random_ids):
    parts, _, _, tokens, _ = stacked.shape
    length = parts * tokens
    count = length // BLOCK
    source = pl.BlockSpec((parts, 3, None, tokens, HD), lambda h, rb, ps: (0, 0, head, 0, 0))
    whole = pl.BlockSpec((parts, 3, tokens, HD), lambda h, rb, ps: (0, 0, 0, 0))
    spec = pl.BlockSpec((length, HD), lambda h, rb, ps: (0, head))
    out = jax.ShapeDtypeStruct((parts, 3, tokens, HD), jnp.bfloat16)
    pairs = 2 * BLOCK * length + (count - 2) * BLOCK * SLOTS * BLOCK
    cost = pl.CostEstimate(
        flops=12 * pairs * HD, transcendentals=pairs, bytes_accessed=14 * length * HD
    )
    return pl.pallas_call(
        _attention_kernel,
        out_shape=out,
        grid_spec=pltpu.PrefetchScalarGridSpec(
            num_scalar_prefetch=2,
            grid=(1,),
            in_specs=[source, spec],
            out_specs=whole,
            scratch_shapes=[
                pltpu.VMEM((length, HD), jnp.float32),
                pltpu.VMEM((length, HD), jnp.float32),
                pltpu.VMEM((SLOTS * BLOCK, HD), jnp.bfloat16),
                pltpu.VMEM((SLOTS * BLOCK, HD), jnp.bfloat16),
            ],
        ),
        compiler_params=pltpu.CompilerParams(dimension_semantics=("arbitrary",)),
        cost_estimate=cost,
    )(random_ids.reshape(-1), positions, stacked, upstream)


def _assemble_kernel(*refs, first_head):
    pieces, outs = refs[:-3], refs[-3:]
    parts = pieces[0].shape[0]
    for c, piece in enumerate(pieces):
        for source in range(parts):
            start = (c * parts + source) * HD
            for g, out in enumerate(outs):
                out[0, :, start:start + HD] = piece[source, g]


def assemble(pieces, tokens, width):
    out = jax.ShapeDtypeStruct((1, tokens, width), jnp.bfloat16)
    span = pieces[0].shape[0] * HD
    early = len(pieces) - 1
    whole = pl.BlockSpec(memory_space=pltpu.VMEM)
    head_spec = pl.BlockSpec((1, tokens, early * span), lambda i: (0, 0, 0))
    partial = pl.pallas_call(
        functools.partial(_assemble_kernel, first_head=0),
        out_shape=(out, out, out),
        grid=(1,),
        in_specs=[whole] * early,
        out_specs=(head_spec, head_spec, head_spec),
    )(*pieces[:early])
    last_spec = pl.BlockSpec((1, tokens, span), lambda i: (0, 0, early))
    return pl.pallas_call(
        _assemble_last_kernel,
        out_shape=(out, out, out),
        grid=(1,),
        in_specs=[whole, last_spec, last_spec, last_spec],
        out_specs=(last_spec, last_spec, last_spec),
        input_output_aliases={1: 0, 2: 1, 3: 2},
    )(pieces[early], *partial)


def _assemble_last_kernel(piece, _first, _second, _third, *outs):
    parts = piece.shape[0]
    for source in range(parts):
        for g, out in enumerate(outs):
            out[0, :, source * HD:(source + 1) * HD] = piece[source, g]


def body(queries, key_rows, value_rows, cotangent, out_weight, random_blocks):
    dp = lax.axis_size("dp")
    ctx = lax.axis_size("context")
    local = (queries[0], key_rows[0], value_rows[0])
    local_cotangent = cotangent[0]
    tokens, width = local[0].shape
    total_heads = width // HD
    local_heads = total_heads // ctx
    rows_per_device = out_weight.shape[0]
    strided = rows_per_device == HD and local_heads == dp and ctx % 2 == 0

    if strided:
        me = lax.axis_index("dp")
        got = [out_weight] + [
            lax.ppermute(out_weight, "dp", [(a, (a + s) % dp) for a in range(dp)])
            for s in range(1, dp)
        ]
        order = (me - jnp.arange(dp)) % dp
        head_weight = jnp.take(jnp.stack(got), order, axis=0).reshape(dp * HD, -1)
        j = lax.axis_index("context")
        shifts = list(range(0, ctx, 2))
        mine = jnp.stack([local_cotangent] + [
            lax.ppermute(local_cotangent, "context", [(a, (a + s) % ctx) for a in range(ctx)])
            for s in shifts[1:]
        ])
        other = lax.ppermute(mine, "context", [(a, a ^ 1) for a in range(ctx)])
        gathered = jnp.concatenate([mine, other]).reshape(ctx * tokens, -1)
        upstream = lax.dot_general(
            gathered, head_weight, (((1,), (1,)), ((), ())),
            preferred_element_type=jnp.float32,
        ).astype(jnp.bfloat16)
        source = jnp.arange(ctx)
        same = source % 2 == j % 2
        position = jnp.where(
            same, ((j - source) % ctx) // 2, ctx // 2 + (((j ^ 1) - source) % ctx) // 2
        )
        positions = position.astype(jnp.int32)

        def chunk(array):
            return array.reshape(tokens, dp, ctx, HD).transpose(2, 1, 0, 3)
    else:
        upstream = lax.dot_general(
            local_cotangent,
            lax.all_gather(out_weight, ("dp", "context"), axis=0, tiled=True),
            (((1,), (1,)), ((), ())),
            preferred_element_type=jnp.float32,
        ).astype(jnp.bfloat16)
        local = local + (upstream,)
        positions = jnp.arange(ctx, dtype=jnp.int32)

        def chunk(array):
            return array.reshape(tokens, ctx, local_heads, HD).transpose(1, 2, 0, 3)

    stacked = jnp.stack([chunk(array) for array in local], axis=1)
    moved = lax.all_to_all(stacked, "context", split_axis=0, concat_axis=0, tiled=True)
    if not strided:
        head_upstream = moved[:, 3].transpose(1, 0, 2, 3).reshape(local_heads, tokens * ctx, HD)
        moved = moved[:, :3]
    pieces = []
    for c in range(local_heads):
        if strided:
            grads = attention_grads(moved, upstream, c, positions, random_blocks[0])
        else:
            grads = attention_grads(moved, head_upstream[c], 0, positions, random_blocks[0])
        back = lax.all_to_all(grads, "context", split_axis=0, concat_axis=0, tiled=True)
        pieces.append(back if strided else back.transpose(1, 2, 0, 3))

    if strided:
        return assemble(pieces, tokens, width)
    outs = []
    for g in range(3):
        joined = jnp.stack([piece[g] for piece in pieces], axis=1 if strided else 2)
        outs.append(joined.reshape(1, tokens, width))
    return tuple(outs)


def solution(mesh):
    return jax.shard_map(
        body,
        mesh=mesh,
        in_specs=(
            P("dp", "context", None),
            P("dp", "context", None),
            P("dp", "context", None),
            P("dp", "context", None),
            P(("dp", "context"), None),
            P("dp", None, None),
        ),
        out_specs=(P("dp", "context", None), P("dp", "context", None), P("dp", "context", None)),
        check_vma=False,
    )
```

```python
import functools
import math

import jax
import jax.numpy as jnp
from jax import lax
from jax.experimental import pallas as pl
from jax.experimental.pallas import tpu as pltpu
from jax.sharding import PartitionSpec as P

HD = 128
BLOCK = 64
RAND = 3
SLOTS = 5 + RAND


def _nt(a, b):
    return lax.dot_general(a, b, (((1,), (1,)), ((), ())), preferred_element_type=jnp.float32)


def _tn(a, b):
    return lax.dot_general(a, b, (((0,), (0,)), ((), ())), preferred_element_type=jnp.float32)


def _nn(a, b):
    return lax.dot_general(a, b, (((1,), (0,)), ((), ())), preferred_element_type=jnp.float32)


def _attention_kernel(rb_ref, pos_ref, x_ref, u_ref, *refs):
    *_, o_ref, dk_acc, dv_acc, kg_ref, vg_ref = refs
    parts, _, tokens, _ = x_ref.shape
    per_part = tokens // BLOCK
    length = parts * tokens
    count = length // BLOCK
    factor = 1.0 / math.sqrt(HD)

    def rows(ref, which, block):
        if isinstance(block, int):
            offset = (block % per_part) * BLOCK
        else:
            offset = pl.multiple_of((block % per_part) * BLOCK, BLOCK)
        return ref.at[block // per_part, which, pl.ds(offset, BLOCK), :]

    def upstream_rows(block):
        offset = pos_ref[block // per_part] * tokens + (block % per_part) * BLOCK
        return u_ref[pl.ds(pl.multiple_of(offset, BLOCK), BLOCK), :]

    def softmax_grads(qb, ub, keys, values, mask):
        scores = _nt(qb, keys) * factor
        if mask is not None:
            scores = jnp.where(mask, -1e30, scores)
        top = jnp.max(scores, axis=1, keepdims=True)
        expo = jnp.exp(scores - top)
        weights = expo * (1.0 / jnp.sum(expo, axis=1, keepdims=True))
        rounded = weights.astype(jnp.bfloat16)
        attended = _nn(rounded, values)
        row = jnp.sum(ub.astype(jnp.float32) * attended, axis=1, keepdims=True)
        grad_probs = _nt(ub, values)
        grad_scores = (weights * (grad_probs - row) * factor).astype(jnp.bfloat16)
        query_grad = _nn(grad_scores, keys)
        key_grad = _tn(grad_scores, qb)
        value_grad = _tn(rounded, ub)
        return query_grad, key_grad, value_grad

    keys_all = x_ref[:, 1, :, :].reshape(length, HD)
    values_all = x_ref[:, 2, :, :].reshape(length, HD)
    last = count - 1
    qb = jnp.concatenate([rows(x_ref, 0, 0)[...], rows(x_ref, 0, last)[...]], axis=0)
    ub = jnp.concatenate([upstream_rows(0), upstream_rows(last)], axis=0)
    query_grad, key_grad, value_grad = softmax_grads(qb, ub, keys_all, values_all, None)
    query_grad = query_grad.astype(jnp.bfloat16)
    rows(o_ref, 0, 0)[...] = query_grad[:BLOCK]
    rows(o_ref, 0, last)[...] = query_grad[BLOCK:]
    dk_acc[...] = key_grad
    dv_acc[...] = value_grad

    columns = lax.broadcasted_iota(jnp.int32, (BLOCK, SLOTS * BLOCK), 1) // BLOCK

    def mid_step(m, carry):
        base = (m - 1) * RAND
        lower = jnp.where(m - 1 >= 1, m - 1, m)
        upper = jnp.where(m + 1 <= count - 2, m + 1, m)
        ids = [0, count - 1, lower, m, upper] + [rb_ref[base + r] for r in range(RAND)]
        for slot, block in enumerate(ids):
            kg_ref[slot * BLOCK:(slot + 1) * BLOCK, :] = rows(x_ref, 1, block)[...]
            vg_ref[slot * BLOCK:(slot + 1) * BLOCK, :] = rows(x_ref, 2, block)[...]
        start = pl.multiple_of(m * BLOCK, BLOCK)
        qb = rows(x_ref, 0, m)[...]
        ub = upstream_rows(m)
        mask = ((columns == 2) & (m == 1)) | ((columns == 4) & (m == count - 2))
        query_grad, key_grad, value_grad = softmax_grads(qb, ub, kg_ref[...], vg_ref[...], mask)
        rows(o_ref, 0, m)[...] = query_grad.astype(jnp.bfloat16)
        for slot, block in enumerate(ids):
            row = pl.multiple_of(block * BLOCK, BLOCK)
            dk_acc[pl.ds(row, BLOCK), :] += key_grad[slot * BLOCK:(slot + 1) * BLOCK, :]
            dv_acc[pl.ds(row, BLOCK), :] += value_grad[slot * BLOCK:(slot + 1) * BLOCK, :]
        return carry

    lax.fori_loop(1, count - 1, mid_step, 0, unroll=2)
    o_ref[:, 1, :, :] = dk_acc[...].reshape(parts, tokens, HD).astype(jnp.bfloat16)
    o_ref[:, 2, :, :] = dv_acc[...].reshape(parts, tokens, HD).astype(jnp.bfloat16)


def attention_grads(stacked, upstream, head, positions, random_ids, slots=1, slot=0, into=None):
    parts, _, _, tokens, _ = stacked.shape
    length = parts * tokens
    count = length // BLOCK
    source = pl.BlockSpec((parts, 3, None, tokens, HD), lambda h, rb, ps: (0, 0, head, 0, 0))
    whole = pl.BlockSpec((parts, 3, None, tokens, HD), lambda h, rb, ps: (0, 0, slot, 0, 0))
    spec = pl.BlockSpec((length, HD), lambda h, rb, ps: (0, head))
    out = jax.ShapeDtypeStruct((parts, 3, slots, tokens, HD), jnp.bfloat16)
    extra = () if into is None else (into,)
    aliases = {} if into is None else {4: 0}
    pairs = 2 * BLOCK * length + (count - 2) * BLOCK * SLOTS * BLOCK
    cost = pl.CostEstimate(
        flops=12 * pairs * HD, transcendentals=pairs, bytes_accessed=14 * length * HD
    )
    return pl.pallas_call(
        _attention_kernel,
        out_shape=out,
        grid_spec=pltpu.PrefetchScalarGridSpec(
            num_scalar_prefetch=2,
            grid=(1,),
            in_specs=[source, spec] + [pl.BlockSpec(memory_space=pl.ANY)] * len(extra),
            out_specs=whole,
            scratch_shapes=[
                pltpu.VMEM((length, HD), jnp.float32),
                pltpu.VMEM((length, HD), jnp.float32),
                pltpu.VMEM((SLOTS * BLOCK, HD), jnp.bfloat16),
                pltpu.VMEM((SLOTS * BLOCK, HD), jnp.bfloat16),
            ],
        ),
        compiler_params=pltpu.CompilerParams(dimension_semantics=("arbitrary",)),
        cost_estimate=cost,
        input_output_aliases=aliases,
    )(random_ids.reshape(-1), positions, stacked, upstream, *extra)


def _assemble_kernel(*refs, heads):
    pieces, outs = refs[:len(heads)], refs[len(heads):]
    parts = pieces[0].shape[0]
    for piece, group in zip(pieces, heads):
        for k, c in enumerate(group):
            for source in range(parts):
                start = (c * parts + source) * HD
                for g, out in enumerate(outs):
                    out[0, :, start:start + HD] = piece[source, g, k]


def _assemble_last_kernel(piece, _first, _second, _third, *outs):
    parts = piece.shape[0]
    for source in range(parts):
        for g, out in enumerate(outs):
            out[0, :, source * HD:(source + 1) * HD] = piece[source, g, 0]


def assemble(pieces, heads, tokens, width):
    out = jax.ShapeDtypeStruct((1, tokens, width), jnp.bfloat16)
    span = pieces[0].shape[0] * HD
    early = heads[-1][0]
    whole = pl.BlockSpec(memory_space=pltpu.VMEM)
    head_spec = pl.BlockSpec((1, tokens, early * span), lambda i: (0, 0, 0))
    partial = pl.pallas_call(
        functools.partial(_assemble_kernel, heads=heads[:-1]),
        out_shape=(out, out, out),
        grid=(1,),
        in_specs=[whole] * (len(pieces) - 1),
        out_specs=(head_spec, head_spec, head_spec),
    )(*pieces[:-1])
    last_spec = pl.BlockSpec((1, tokens, span), lambda i: (0, 0, early))
    return pl.pallas_call(
        _assemble_last_kernel,
        out_shape=(out, out, out),
        grid=(1,),
        in_specs=[whole, last_spec, last_spec, last_spec],
        out_specs=(last_spec, last_spec, last_spec),
        input_output_aliases={1: 0, 2: 1, 3: 2},
    )(pieces[-1], *partial)


def body(queries, key_rows, value_rows, cotangent, out_weight, random_blocks):
    dp = lax.axis_size("dp")
    ctx = lax.axis_size("context")
    local = (queries[0], key_rows[0], value_rows[0])
    local_cotangent = cotangent[0]
    tokens, width = local[0].shape
    total_heads = width // HD
    local_heads = total_heads // ctx
    rows_per_device = out_weight.shape[0]
    strided = rows_per_device == HD and local_heads == dp and ctx % 2 == 0

    if strided:
        me = lax.axis_index("dp")
        got = [out_weight] + [
            lax.ppermute(out_weight, "dp", [(a, (a + s) % dp) for a in range(dp)])
            for s in range(1, dp)
        ]
        order = (me - jnp.arange(dp)) % dp
        head_weight = jnp.take(jnp.stack(got), order, axis=0).reshape(dp * HD, -1)
        j = lax.axis_index("context")
        shifts = list(range(0, ctx, 2))
        mine = jnp.stack([local_cotangent] + [
            lax.ppermute(local_cotangent, "context", [(a, (a + s) % ctx) for a in range(ctx)])
            for s in shifts[1:]
        ])
        other = lax.ppermute(mine, "context", [(a, a ^ 1) for a in range(ctx)])
        gathered = jnp.concatenate([mine, other]).reshape(ctx * tokens, -1)
        upstream = lax.dot_general(
            gathered, head_weight, (((1,), (1,)), ((), ())),
            preferred_element_type=jnp.float32,
        ).astype(jnp.bfloat16)
        source = jnp.arange(ctx)
        same = source % 2 == j % 2
        position = jnp.where(
            same, ((j - source) % ctx) // 2, ctx // 2 + (((j ^ 1) - source) % ctx) // 2
        )
        positions = position.astype(jnp.int32)

        def chunk(array):
            return array.reshape(tokens, dp, ctx, HD).transpose(2, 1, 0, 3)
    else:
        upstream = lax.dot_general(
            local_cotangent,
            lax.all_gather(out_weight, ("dp", "context"), axis=0, tiled=True),
            (((1,), (1,)), ((), ())),
            preferred_element_type=jnp.float32,
        ).astype(jnp.bfloat16)
        local = local + (upstream,)
        positions = jnp.arange(ctx, dtype=jnp.int32)

        def chunk(array):
            return array.reshape(tokens, ctx, local_heads, HD).transpose(1, 2, 0, 3)

    stacked = jnp.stack([chunk(array) for array in local], axis=1)
    moved = lax.all_to_all(stacked, "context", split_axis=0, concat_axis=0, tiled=True)
    if not strided:
        head_upstream = moved[:, 3].transpose(1, 0, 2, 3).reshape(local_heads, tokens * ctx, HD)
        moved = moved[:, :3]
    if strided and local_heads >= 3:
        heads = [[0, 1]] + [[c] for c in range(2, local_heads)]
    else:
        heads = [[c] for c in range(local_heads)]
    pieces = []
    for group in heads:
        grads = None
        for k, c in enumerate(group):
            if strided:
                grads = attention_grads(
                    moved, upstream, c, positions, random_blocks[0], len(group), k, grads
                )
            else:
                grads = attention_grads(moved, head_upstream[c], 0, positions, random_blocks[0])
        back = lax.all_to_all(grads, "context", split_axis=0, concat_axis=0, tiled=True)
        pieces.append(back if strided else back[:, :, 0].transpose(1, 2, 0, 3))

    if strided:
        return assemble(pieces, heads, tokens, width)
    outs = []
    for g in range(3):
        joined = jnp.stack([piece[g] for piece in pieces], axis=1 if strided else 2)
        outs.append(joined.reshape(1, tokens, width))
    return tuple(outs)


def solution(mesh):
    return jax.shard_map(
        body,
        mesh=mesh,
        in_specs=(
            P("dp", "context", None),
            P("dp", "context", None),
            P("dp", "context", None),
            P("dp", "context", None),
            P(("dp", "context"), None),
            P("dp", None, None),
        ),
        out_specs=(P("dp", "context", None), P("dp", "context", None), P("dp", "context", None)),
        check_vma=False,
    )
```

```python
import functools
import math

import jax
import jax.numpy as jnp
from jax import lax
from jax.experimental import pallas as pl
from jax.experimental.pallas import tpu as pltpu
from jax.sharding import PartitionSpec as P

HD = 128
BLOCK = 64
RAND = 3
SLOTS = 5 + RAND


def _nt(a, b):
    return lax.dot_general(a, b, (((1,), (1,)), ((), ())), preferred_element_type=jnp.float32)


def _tn(a, b):
    return lax.dot_general(a, b, (((0,), (0,)), ((), ())), preferred_element_type=jnp.float32)


def _nn(a, b):
    return lax.dot_general(a, b, (((1,), (0,)), ((), ())), preferred_element_type=jnp.float32)


def _attention_kernel(rb_ref, pos_ref, x_ref, u_ref, o_ref, dk_acc, dv_acc, kg_ref, vg_ref):
    parts, _, tokens, _ = x_ref.shape
    per_part = tokens // BLOCK
    length = parts * tokens
    count = length // BLOCK
    factor = 1.0 / math.sqrt(HD)

    def rows(ref, which, block):
        if isinstance(block, int):
            offset = (block % per_part) * BLOCK
        else:
            offset = pl.multiple_of((block % per_part) * BLOCK, BLOCK)
        return ref.at[block // per_part, which, pl.ds(offset, BLOCK), :]

    def upstream_rows(block):
        offset = pos_ref[block // per_part] * tokens + (block % per_part) * BLOCK
        return u_ref[pl.ds(pl.multiple_of(offset, BLOCK), BLOCK), :]

    def softmax_grads(qb, ub, keys, values, mask):
        scores = _nt(qb, keys) * factor
        if mask is not None:
            scores = jnp.where(mask, -1e30, scores)
        top = jnp.max(scores, axis=1, keepdims=True)
        expo = jnp.exp(scores - top)
        weights = expo * (1.0 / jnp.sum(expo, axis=1, keepdims=True))
        rounded = weights.astype(jnp.bfloat16)
        attended = _nn(rounded, values)
        row = jnp.sum(ub.astype(jnp.float32) * attended, axis=1, keepdims=True)
        grad_probs = _nt(ub, values)
        grad_scores = (weights * (grad_probs - row) * factor).astype(jnp.bfloat16)
        query_grad = _nn(grad_scores, keys)
        key_grad = _tn(grad_scores, qb)
        value_grad = _tn(rounded, ub)
        return query_grad, key_grad, value_grad

    keys_all = x_ref[:, 1, :, :].reshape(length, HD)
    values_all = x_ref[:, 2, :, :].reshape(length, HD)
    last = count - 1
    qb = jnp.concatenate([rows(x_ref, 0, 0)[...], rows(x_ref, 0, last)[...]], axis=0)
    ub = jnp.concatenate([upstream_rows(0), upstream_rows(last)], axis=0)
    query_grad, key_grad, value_grad = softmax_grads(qb, ub, keys_all, values_all, None)
    query_grad = query_grad.astype(jnp.bfloat16)
    rows(o_ref, 0, 0)[...] = query_grad[:BLOCK]
    rows(o_ref, 0, last)[...] = query_grad[BLOCK:]
    dk_acc[...] = key_grad
    dv_acc[...] = value_grad

    columns = lax.broadcasted_iota(jnp.int32, (BLOCK, SLOTS * BLOCK), 1) // BLOCK

    def mid_step(m, carry):
        base = (m - 1) * RAND
        lower = jnp.where(m - 1 >= 1, m - 1, m)
        upper = jnp.where(m + 1 <= count - 2, m + 1, m)
        ids = [0, count - 1, lower, m, upper] + [rb_ref[base + r] for r in range(RAND)]
        for slot, block in enumerate(ids):
            kg_ref[slot * BLOCK:(slot + 1) * BLOCK, :] = rows(x_ref, 1, block)[...]
            vg_ref[slot * BLOCK:(slot + 1) * BLOCK, :] = rows(x_ref, 2, block)[...]
        start = pl.multiple_of(m * BLOCK, BLOCK)
        qb = rows(x_ref, 0, m)[...]
        ub = upstream_rows(m)
        mask = ((columns == 2) & (m == 1)) | ((columns == 4) & (m == count - 2))
        query_grad, key_grad, value_grad = softmax_grads(qb, ub, kg_ref[...], vg_ref[...], mask)
        rows(o_ref, 0, m)[...] = query_grad.astype(jnp.bfloat16)
        for slot, block in enumerate(ids):
            row = pl.multiple_of(block * BLOCK, BLOCK)
            dk_acc[pl.ds(row, BLOCK), :] += key_grad[slot * BLOCK:(slot + 1) * BLOCK, :]
            dv_acc[pl.ds(row, BLOCK), :] += value_grad[slot * BLOCK:(slot + 1) * BLOCK, :]
        return carry

    lax.fori_loop(1, count - 1, mid_step, 0, unroll=7)
    o_ref[:, 1, :, :] = dk_acc[...].reshape(parts, tokens, HD).astype(jnp.bfloat16)
    o_ref[:, 2, :, :] = dv_acc[...].reshape(parts, tokens, HD).astype(jnp.bfloat16)


def attention_grads(stacked, upstream, head, positions, random_ids):
    parts, _, _, tokens, _ = stacked.shape
    length = parts * tokens
    count = length // BLOCK
    source = pl.BlockSpec((parts, 3, None, tokens, HD), lambda h, rb, ps: (0, 0, head, 0, 0))
    whole = pl.BlockSpec((parts, 3, tokens, HD), lambda h, rb, ps: (0, 0, 0, 0))
    spec = pl.BlockSpec((length, HD), lambda h, rb, ps: (0, head))
    out = jax.ShapeDtypeStruct((parts, 3, tokens, HD), jnp.bfloat16)
    pairs = 2 * BLOCK * length + (count - 2) * BLOCK * SLOTS * BLOCK
    cost = pl.CostEstimate(
        flops=12 * pairs * HD, transcendentals=pairs, bytes_accessed=14 * length * HD
    )
    return pl.pallas_call(
        _attention_kernel,
        out_shape=out,
        grid_spec=pltpu.PrefetchScalarGridSpec(
            num_scalar_prefetch=2,
            grid=(1,),
            in_specs=[source, spec],
            out_specs=whole,
            scratch_shapes=[
                pltpu.VMEM((length, HD), jnp.float32),
                pltpu.VMEM((length, HD), jnp.float32),
                pltpu.VMEM((SLOTS * BLOCK, HD), jnp.bfloat16),
                pltpu.VMEM((SLOTS * BLOCK, HD), jnp.bfloat16),
            ],
        ),
        compiler_params=pltpu.CompilerParams(dimension_semantics=("arbitrary",)),
        cost_estimate=cost,
    )(random_ids.reshape(-1), positions, stacked, upstream)


def _assemble_kernel(*refs, first_head):
    pieces, outs = refs[:-3], refs[-3:]
    parts = pieces[0].shape[0]
    for c, piece in enumerate(pieces):
        for source in range(parts):
            start = (c * parts + source) * HD
            for g, out in enumerate(outs):
                out[0, :, start:start + HD] = piece[source, g]


def assemble(pieces, tokens, width):
    out = jax.ShapeDtypeStruct((1, tokens, width), jnp.bfloat16)
    span = pieces[0].shape[0] * HD
    early = len(pieces) - 1
    whole = pl.BlockSpec(memory_space=pltpu.VMEM)
    head_spec = pl.BlockSpec((1, tokens, early * span), lambda i: (0, 0, 0))
    partial = pl.pallas_call(
        functools.partial(_assemble_kernel, first_head=0),
        out_shape=(out, out, out),
        grid=(1,),
        in_specs=[whole] * early,
        out_specs=(head_spec, head_spec, head_spec),
    )(*pieces[:early])
    last_spec = pl.BlockSpec((1, tokens, span), lambda i: (0, 0, early))
    return pl.pallas_call(
        _assemble_last_kernel,
        out_shape=(out, out, out),
        grid=(1,),
        in_specs=[whole, last_spec, last_spec, last_spec],
        out_specs=(last_spec, last_spec, last_spec),
        input_output_aliases={1: 0, 2: 1, 3: 2},
    )(pieces[early], *partial)


def _assemble_last_kernel(piece, _first, _second, _third, *outs):
    parts = piece.shape[0]
    for source in range(parts):
        for g, out in enumerate(outs):
            out[0, :, source * HD:(source + 1) * HD] = piece[source, g]


def body(queries, key_rows, value_rows, cotangent, out_weight, random_blocks):
    dp = lax.axis_size("dp")
    ctx = lax.axis_size("context")
    local = (queries[0], key_rows[0], value_rows[0])
    local_cotangent = cotangent[0]
    tokens, width = local[0].shape
    total_heads = width // HD
    local_heads = total_heads // ctx
    rows_per_device = out_weight.shape[0]
    strided = rows_per_device == HD and local_heads == dp and ctx % 2 == 0

    if strided:
        me = lax.axis_index("dp")
        got = [out_weight] + [
            lax.ppermute(out_weight, "dp", [(a, (a + s) % dp) for a in range(dp)])
            for s in range(1, dp)
        ]
        order = (me - jnp.arange(dp)) % dp
        head_weight = jnp.take(jnp.stack(got), order, axis=0).reshape(dp * HD, -1)
        j = lax.axis_index("context")
        shifts = list(range(0, ctx, 2))
        mine = jnp.stack([local_cotangent] + [
            lax.ppermute(local_cotangent, "context", [(a, (a + s) % ctx) for a in range(ctx)])
            for s in shifts[1:]
        ])
        other = lax.ppermute(mine, "context", [(a, a ^ 1) for a in range(ctx)])
        gathered = jnp.concatenate([mine, other]).reshape(ctx * tokens, -1)
        upstream = lax.dot_general(
            gathered, head_weight, (((1,), (1,)), ((), ())),
            preferred_element_type=jnp.float32,
        ).astype(jnp.bfloat16)
        source = jnp.arange(ctx)
        same = source % 2 == j % 2
        position = jnp.where(
            same, ((j - source) % ctx) // 2, ctx // 2 + (((j ^ 1) - source) % ctx) // 2
        )
        positions = position.astype(jnp.int32)

        def chunk(array):
            return array.reshape(tokens, dp, ctx, HD).transpose(2, 1, 0, 3)
    else:
        upstream = lax.dot_general(
            local_cotangent,
            lax.all_gather(out_weight, ("dp", "context"), axis=0, tiled=True),
            (((1,), (1,)), ((), ())),
            preferred_element_type=jnp.float32,
        ).astype(jnp.bfloat16)
        local = local + (upstream,)
        positions = jnp.arange(ctx, dtype=jnp.int32)

        def chunk(array):
            return array.reshape(tokens, ctx, local_heads, HD).transpose(1, 2, 0, 3)

    stacked = jnp.stack([chunk(array) for array in local], axis=1)
    moved = lax.all_to_all(stacked, "context", split_axis=0, concat_axis=0, tiled=True)
    if not strided:
        head_upstream = moved[:, 3].transpose(1, 0, 2, 3).reshape(local_heads, tokens * ctx, HD)
        moved = moved[:, :3]
    pieces = []
    for c in range(local_heads):
        if strided:
            grads = attention_grads(moved, upstream, c, positions, random_blocks[0])
        else:
            grads = attention_grads(moved, head_upstream[c], 0, positions, random_blocks[0])
        back = lax.all_to_all(grads, "context", split_axis=0, concat_axis=0, tiled=True)
        pieces.append(back if strided else back.transpose(1, 2, 0, 3))

    if strided:
        return assemble(pieces, tokens, width)
    outs = []
    for g in range(3):
        joined = jnp.stack([piece[g] for piece in pieces], axis=1 if strided else 2)
        outs.append(joined.reshape(1, tokens, width))
    return tuple(outs)


def solution(mesh):
    return jax.shard_map(
        body,
        mesh=mesh,
        in_specs=(
            P("dp", "context", None),
            P("dp", "context", None),
            P("dp", "context", None),
            P("dp", "context", None),
            P(("dp", "context"), None),
            P("dp", None, None),
        ),
        out_specs=(P("dp", "context", None), P("dp", "context", None), P("dp", "context", None)),
        check_vma=False,
    )
```

```python
import functools
import math

import jax
import jax.numpy as jnp
from jax import lax
from jax.experimental import pallas as pl
from jax.experimental.pallas import tpu as pltpu
from jax.sharding import PartitionSpec as P

HD = 128
BLOCK = 64
RAND = 3
SLOTS = 5 + RAND


def _nt(a, b):
    return lax.dot_general(a, b, (((1,), (1,)), ((), ())), preferred_element_type=jnp.float32)


def _tn(a, b):
    return lax.dot_general(a, b, (((0,), (0,)), ((), ())), preferred_element_type=jnp.float32)


def _nn(a, b):
    return lax.dot_general(a, b, (((1,), (0,)), ((), ())), preferred_element_type=jnp.float32)


def _attention_kernel(rb_ref, pos_ref, x_ref, u_ref, o_ref, dk_acc, dv_acc, kg_ref, vg_ref):
    parts, _, tokens, _ = x_ref.shape
    per_part = tokens // BLOCK
    length = parts * tokens
    count = length // BLOCK
    factor = 1.0 / math.sqrt(HD)

    def rows(ref, which, block):
        if isinstance(block, int):
            offset = (block % per_part) * BLOCK
        else:
            offset = pl.multiple_of((block % per_part) * BLOCK, BLOCK)
        return ref.at[block // per_part, which, pl.ds(offset, BLOCK), :]

    def upstream_rows(block):
        offset = pos_ref[block // per_part] * tokens + (block % per_part) * BLOCK
        return u_ref[pl.ds(pl.multiple_of(offset, BLOCK), BLOCK), :]

    def softmax_grads(qb, ub, keys, values, mask):
        scores = _nt(qb, keys) * factor
        if mask is not None:
            scores = jnp.where(mask, -1e30, scores)
        top = jnp.max(scores, axis=1, keepdims=True)
        expo = jnp.exp(scores - top)
        weights = expo * (1.0 / jnp.sum(expo, axis=1, keepdims=True))
        rounded = weights.astype(jnp.bfloat16)
        attended = _nn(rounded, values)
        row = jnp.sum(ub.astype(jnp.float32) * attended, axis=1, keepdims=True)
        grad_probs = _nt(ub, values)
        grad_scores = (weights * (grad_probs - row) * factor).astype(jnp.bfloat16)
        query_grad = _nn(grad_scores, keys)
        key_grad = _tn(grad_scores, qb)
        value_grad = _tn(rounded, ub)
        return query_grad, key_grad, value_grad

    keys_all = x_ref[:, 1, :, :].reshape(length, HD)
    values_all = x_ref[:, 2, :, :].reshape(length, HD)
    last = count - 1
    qb = jnp.concatenate([rows(x_ref, 0, 0)[...], rows(x_ref, 0, last)[...]], axis=0)
    ub = jnp.concatenate([upstream_rows(0), upstream_rows(last)], axis=0)
    query_grad, key_grad, value_grad = softmax_grads(qb, ub, keys_all, values_all, None)
    query_grad = query_grad.astype(jnp.bfloat16)
    rows(o_ref, 0, 0)[...] = query_grad[:BLOCK]
    rows(o_ref, 0, last)[...] = query_grad[BLOCK:]
    dk_acc[...] = key_grad
    dv_acc[...] = value_grad

    columns = lax.broadcasted_iota(jnp.int32, (BLOCK, SLOTS * BLOCK), 1) // BLOCK

    def mid_step(m, carry):
        base = (m - 1) * RAND
        lower = jnp.where(m - 1 >= 1, m - 1, m)
        upper = jnp.where(m + 1 <= count - 2, m + 1, m)
        ids = [0, count - 1, lower, m, upper] + [rb_ref[base + r] for r in range(RAND)]
        for slot, block in enumerate(ids):
            kg_ref[slot * BLOCK:(slot + 1) * BLOCK, :] = rows(x_ref, 1, block)[...]
            vg_ref[slot * BLOCK:(slot + 1) * BLOCK, :] = rows(x_ref, 2, block)[...]
        start = pl.multiple_of(m * BLOCK, BLOCK)
        qb = rows(x_ref, 0, m)[...]
        ub = upstream_rows(m)
        mask = ((columns == 2) & (m == 1)) | ((columns == 4) & (m == count - 2))
        query_grad, key_grad, value_grad = softmax_grads(qb, ub, kg_ref[...], vg_ref[...], mask)
        rows(o_ref, 0, m)[...] = query_grad.astype(jnp.bfloat16)
        for slot, block in enumerate(ids):
            row = pl.multiple_of(block * BLOCK, BLOCK)
            dk_acc[pl.ds(row, BLOCK), :] += key_grad[slot * BLOCK:(slot + 1) * BLOCK, :]
            dv_acc[pl.ds(row, BLOCK), :] += value_grad[slot * BLOCK:(slot + 1) * BLOCK, :]
        return carry

    lax.fori_loop(1, count - 1, mid_step, 0, unroll=7)
    o_ref[:, 1, :, :] = dk_acc[...].reshape(parts, tokens, HD).astype(jnp.bfloat16)
    o_ref[:, 2, :, :] = dv_acc[...].reshape(parts, tokens, HD).astype(jnp.bfloat16)


def attention_grads(stacked, upstream, head, positions, random_ids):
    parts, _, _, tokens, _ = stacked.shape
    length = parts * tokens
    count = length // BLOCK
    source = pl.BlockSpec((parts, 3, None, tokens, HD), lambda h, rb, ps: (0, 0, head, 0, 0))
    whole = pl.BlockSpec((parts, 3, tokens, HD), lambda h, rb, ps: (0, 0, 0, 0))
    spec = pl.BlockSpec((length, HD), lambda h, rb, ps: (0, head))
    out = jax.ShapeDtypeStruct((parts, 3, tokens, HD), jnp.bfloat16)
    pairs = 2 * BLOCK * length + (count - 2) * BLOCK * SLOTS * BLOCK
    cost = pl.CostEstimate(
        flops=12 * pairs * HD, transcendentals=pairs, bytes_accessed=14 * length * HD
    )
    return pl.pallas_call(
        _attention_kernel,
        out_shape=out,
        grid_spec=pltpu.PrefetchScalarGridSpec(
            num_scalar_prefetch=2,
            grid=(1,),
            in_specs=[source, spec],
            out_specs=whole,
            scratch_shapes=[
                pltpu.VMEM((length, HD), jnp.float32),
                pltpu.VMEM((length, HD), jnp.float32),
                pltpu.VMEM((SLOTS * BLOCK, HD), jnp.bfloat16),
                pltpu.VMEM((SLOTS * BLOCK, HD), jnp.bfloat16),
            ],
        ),
        compiler_params=pltpu.CompilerParams(dimension_semantics=("arbitrary",)),
        cost_estimate=cost,
    )(random_ids.reshape(-1), positions, stacked, upstream)


def _assemble_kernel(*refs, first_head):
    pieces, outs = refs[:-3], refs[-3:]
    parts = pieces[0].shape[0]
    for c, piece in enumerate(pieces):
        for source in range(parts):
            start = (c * parts + source) * HD
            for g, out in enumerate(outs):
                out[0, :, start:start + HD] = piece[source, g]


def assemble(pieces, tokens, width):
    out = jax.ShapeDtypeStruct((1, tokens, width), jnp.bfloat16)
    span = pieces[0].shape[0] * HD
    early = len(pieces) - 1
    whole = pl.BlockSpec(memory_space=pltpu.VMEM)
    head_spec = pl.BlockSpec((1, tokens, early * span), lambda i: (0, 0, 0))
    partial = pl.pallas_call(
        functools.partial(_assemble_kernel, first_head=0),
        out_shape=(out, out, out),
        grid=(1,),
        in_specs=[whole] * early,
        out_specs=(head_spec, head_spec, head_spec),
    )(*pieces[:early])
    last_spec = pl.BlockSpec((1, tokens, span), lambda i: (0, 0, early))
    return pl.pallas_call(
        _assemble_last_kernel,
        out_shape=(out, out, out),
        grid=(1,),
        in_specs=[whole, last_spec, last_spec, last_spec],
        out_specs=(last_spec, last_spec, last_spec),
        input_output_aliases={1: 0, 2: 1, 3: 2},
    )(pieces[early], *partial)


def _assemble_last_kernel(piece, _first, _second, _third, *outs):
    parts = piece.shape[0]
    for source in range(parts):
        for g, out in enumerate(outs):
            out[0, :, source * HD:(source + 1) * HD] = piece[source, g]


def body(queries, key_rows, value_rows, cotangent, out_weight, random_blocks):
    dp = lax.axis_size("dp")
    ctx = lax.axis_size("context")
    local = (queries[0], key_rows[0], value_rows[0])
    local_cotangent = cotangent[0]
    tokens, width = local[0].shape
    total_heads = width // HD
    local_heads = total_heads // ctx
    rows_per_device = out_weight.shape[0]
    strided = rows_per_device == HD and local_heads == dp and ctx % 2 == 0

    if strided:
        me = lax.axis_index("dp")
        got = [out_weight] + [
            lax.ppermute(out_weight, "dp", [(a, (a + s) % dp) for a in range(dp)])
            for s in range(1, dp)
        ]
        order = (me - jnp.arange(dp)) % dp
        spread = jnp.stack(got)
        head_weight = jnp.concatenate(
            [lax.dynamic_index_in_dim(spread, order[c], 0, keepdims=False) for c in range(dp)]
        )
        j = lax.axis_index("context")
        shifts = list(range(0, ctx, 2))
        mine = jnp.stack([local_cotangent] + [
            lax.ppermute(local_cotangent, "context", [(a, (a + s) % ctx) for a in range(ctx)])
            for s in shifts[1:]
        ])
        other = lax.ppermute(mine, "context", [(a, a ^ 1) for a in range(ctx)])
        gathered = jnp.concatenate([mine, other]).reshape(ctx * tokens, -1)
        upstream = lax.dot_general(
            gathered, head_weight, (((1,), (1,)), ((), ())),
            preferred_element_type=jnp.float32,
        ).astype(jnp.bfloat16)
        source = jnp.arange(ctx)
        same = source % 2 == j % 2
        position = jnp.where(
            same, ((j - source) % ctx) // 2, ctx // 2 + (((j ^ 1) - source) % ctx) // 2
        )
        positions = position.astype(jnp.int32)

        def chunk(array):
            return array.reshape(tokens, dp, ctx, HD).transpose(2, 1, 0, 3)
    else:
        upstream = lax.dot_general(
            local_cotangent,
            lax.all_gather(out_weight, ("dp", "context"), axis=0, tiled=True),
            (((1,), (1,)), ((), ())),
            preferred_element_type=jnp.float32,
        ).astype(jnp.bfloat16)
        local = local + (upstream,)
        positions = jnp.arange(ctx, dtype=jnp.int32)

        def chunk(array):
            return array.reshape(tokens, ctx, local_heads, HD).transpose(1, 2, 0, 3)

    stacked = jnp.stack([chunk(array) for array in local], axis=1)
    moved = lax.all_to_all(stacked, "context", split_axis=0, concat_axis=0, tiled=True)
    if not strided:
        head_upstream = moved[:, 3].transpose(1, 0, 2, 3).reshape(local_heads, tokens * ctx, HD)
        moved = moved[:, :3]
    pieces = []
    for c in range(local_heads):
        if strided:
            grads = attention_grads(moved, upstream, c, positions, random_blocks[0])
        else:
            grads = attention_grads(moved, head_upstream[c], 0, positions, random_blocks[0])
        back = lax.all_to_all(grads, "context", split_axis=0, concat_axis=0, tiled=True)
        pieces.append(back if strided else back.transpose(1, 2, 0, 3))

    if strided:
        return assemble(pieces, tokens, width)
    outs = []
    for g in range(3):
        joined = jnp.stack([piece[g] for piece in pieces], axis=1 if strided else 2)
        outs.append(joined.reshape(1, tokens, width))
    return tuple(outs)


def solution(mesh):
    return jax.shard_map(
        body,
        mesh=mesh,
        in_specs=(
            P("dp", "context", None),
            P("dp", "context", None),
            P("dp", "context", None),
            P("dp", "context", None),
            P(("dp", "context"), None),
            P("dp", None, None),
        ),
        out_specs=(P("dp", "context", None), P("dp", "context", None), P("dp", "context", None)),
        check_vma=False,
    )
```

```python
import functools
import math

import jax
import jax.numpy as jnp
from jax import lax
from jax.experimental import pallas as pl
from jax.experimental.pallas import tpu as pltpu
from jax.sharding import PartitionSpec as P

HD = 128
BLOCK = 64
RAND = 3
SLOTS = 5 + RAND


def _nt(a, b):
    return lax.dot_general(a, b, (((1,), (1,)), ((), ())), preferred_element_type=jnp.float32)


def _tn(a, b):
    return lax.dot_general(a, b, (((0,), (0,)), ((), ())), preferred_element_type=jnp.float32)


def _nn(a, b):
    return lax.dot_general(a, b, (((1,), (0,)), ((), ())), preferred_element_type=jnp.float32)


def _attention_kernel(rb_ref, pos_ref, x_ref, u_ref, o_ref, dk_acc, dv_acc, kg_ref, vg_ref):
    parts, _, tokens, _ = x_ref.shape
    per_part = tokens // BLOCK
    length = parts * tokens
    count = length // BLOCK
    factor = 1.0 / math.sqrt(HD)

    def rows(ref, which, block):
        if isinstance(block, int):
            offset = (block % per_part) * BLOCK
        else:
            offset = pl.multiple_of((block % per_part) * BLOCK, BLOCK)
        return ref.at[block // per_part, which, pl.ds(offset, BLOCK), :]

    def upstream_rows(block):
        offset = pos_ref[block // per_part] * tokens + (block % per_part) * BLOCK
        return u_ref[pl.ds(pl.multiple_of(offset, BLOCK), BLOCK), :]

    def softmax_grads(qb, ub, keys, values, mask):
        scores = _nt(qb, keys) * factor
        if mask is not None:
            scores = jnp.where(mask, -1e30, scores)
        top = jnp.max(scores, axis=1, keepdims=True)
        expo = jnp.exp(scores - top)
        weights = expo * (1.0 / jnp.sum(expo, axis=1, keepdims=True))
        rounded = weights.astype(jnp.bfloat16)
        attended = _nn(rounded, values)
        row = jnp.sum(ub.astype(jnp.float32) * attended, axis=1, keepdims=True)
        grad_probs = _nt(ub, values)
        grad_scores = (weights * (grad_probs - row) * factor).astype(jnp.bfloat16)
        query_grad = _nn(grad_scores, keys)
        key_grad = _tn(grad_scores, qb)
        value_grad = _tn(rounded, ub)
        return query_grad, key_grad, value_grad

    keys_all = x_ref[:, 1, :, :].reshape(length, HD)
    values_all = x_ref[:, 2, :, :].reshape(length, HD)
    last = count - 1
    qb = jnp.concatenate([rows(x_ref, 0, 0)[...], rows(x_ref, 0, last)[...]], axis=0)
    ub = jnp.concatenate([upstream_rows(0), upstream_rows(last)], axis=0)
    query_grad, key_grad, value_grad = softmax_grads(qb, ub, keys_all, values_all, None)
    query_grad = query_grad.astype(jnp.bfloat16)
    rows(o_ref, 0, 0)[...] = query_grad[:BLOCK]
    rows(o_ref, 0, last)[...] = query_grad[BLOCK:]
    dk_acc[...] = key_grad
    dv_acc[...] = value_grad

    columns = lax.broadcasted_iota(jnp.int32, (BLOCK, SLOTS * BLOCK), 1) // BLOCK

    def mid_step(m, carry):
        base = (m - 1) * RAND
        lower = jnp.where(m - 1 >= 1, m - 1, m)
        upper = jnp.where(m + 1 <= count - 2, m + 1, m)
        ids = [0, count - 1, lower, m, upper] + [rb_ref[base + r] for r in range(RAND)]
        for slot, block in enumerate(ids):
            kg_ref[slot * BLOCK:(slot + 1) * BLOCK, :] = rows(x_ref, 1, block)[...]
            vg_ref[slot * BLOCK:(slot + 1) * BLOCK, :] = rows(x_ref, 2, block)[...]
        start = pl.multiple_of(m * BLOCK, BLOCK)
        qb = rows(x_ref, 0, m)[...]
        ub = upstream_rows(m)
        mask = ((columns == 2) & (m == 1)) | ((columns == 4) & (m == count - 2))
        query_grad, key_grad, value_grad = softmax_grads(qb, ub, kg_ref[...], vg_ref[...], mask)
        rows(o_ref, 0, m)[...] = query_grad.astype(jnp.bfloat16)
        for slot, block in enumerate(ids):
            row = pl.multiple_of(block * BLOCK, BLOCK)
            dk_acc[pl.ds(row, BLOCK), :] += key_grad[slot * BLOCK:(slot + 1) * BLOCK, :]
            dv_acc[pl.ds(row, BLOCK), :] += value_grad[slot * BLOCK:(slot + 1) * BLOCK, :]
        return carry

    lax.fori_loop(1, count - 1, mid_step, 0, unroll=14)
    o_ref[:, 1, :, :] = dk_acc[...].reshape(parts, tokens, HD).astype(jnp.bfloat16)
    o_ref[:, 2, :, :] = dv_acc[...].reshape(parts, tokens, HD).astype(jnp.bfloat16)


def attention_grads(stacked, upstream, head, positions, random_ids):
    parts, _, _, tokens, _ = stacked.shape
    length = parts * tokens
    count = length // BLOCK
    source = pl.BlockSpec((parts, 3, None, tokens, HD), lambda h, rb, ps: (0, 0, head, 0, 0))
    whole = pl.BlockSpec((parts, 3, tokens, HD), lambda h, rb, ps: (0, 0, 0, 0))
    spec = pl.BlockSpec((length, HD), lambda h, rb, ps: (0, head))
    out = jax.ShapeDtypeStruct((parts, 3, tokens, HD), jnp.bfloat16)
    pairs = 2 * BLOCK * length + (count - 2) * BLOCK * SLOTS * BLOCK
    cost = pl.CostEstimate(
        flops=12 * pairs * HD, transcendentals=pairs, bytes_accessed=14 * length * HD
    )
    return pl.pallas_call(
        _attention_kernel,
        out_shape=out,
        grid_spec=pltpu.PrefetchScalarGridSpec(
            num_scalar_prefetch=2,
            grid=(1,),
            in_specs=[source, spec],
            out_specs=whole,
            scratch_shapes=[
                pltpu.VMEM((length, HD), jnp.float32),
                pltpu.VMEM((length, HD), jnp.float32),
                pltpu.VMEM((SLOTS * BLOCK, HD), jnp.bfloat16),
                pltpu.VMEM((SLOTS * BLOCK, HD), jnp.bfloat16),
            ],
        ),
        compiler_params=pltpu.CompilerParams(dimension_semantics=("arbitrary",)),
        cost_estimate=cost,
    )(random_ids.reshape(-1), positions, stacked, upstream)


def _assemble_kernel(*refs, first_head):
    pieces, outs = refs[:-3], refs[-3:]
    parts = pieces[0].shape[0]
    for c, piece in enumerate(pieces):
        for source in range(parts):
            start = (c * parts + source) * HD
            for g, out in enumerate(outs):
                out[0, :, start:start + HD] = piece[source, g]


def assemble(pieces, tokens, width):
    out = jax.ShapeDtypeStruct((1, tokens, width), jnp.bfloat16)
    span = pieces[0].shape[0] * HD
    early = len(pieces) - 1
    whole = pl.BlockSpec(memory_space=pltpu.VMEM)
    head_spec = pl.BlockSpec((1, tokens, early * span), lambda i: (0, 0, 0))
    partial = pl.pallas_call(
        functools.partial(_assemble_kernel, first_head=0),
        out_shape=(out, out, out),
        grid=(1,),
        in_specs=[whole] * early,
        out_specs=(head_spec, head_spec, head_spec),
    )(*pieces[:early])
    last_spec = pl.BlockSpec((1, tokens, span), lambda i: (0, 0, early))
    return pl.pallas_call(
        _assemble_last_kernel,
        out_shape=(out, out, out),
        grid=(1,),
        in_specs=[whole, last_spec, last_spec, last_spec],
        out_specs=(last_spec, last_spec, last_spec),
        input_output_aliases={1: 0, 2: 1, 3: 2},
    )(pieces[early], *partial)


def _assemble_last_kernel(piece, _first, _second, _third, *outs):
    parts = piece.shape[0]
    for source in range(parts):
        for g, out in enumerate(outs):
            out[0, :, source * HD:(source + 1) * HD] = piece[source, g]


def body(queries, key_rows, value_rows, cotangent, out_weight, random_blocks):
    dp = lax.axis_size("dp")
    ctx = lax.axis_size("context")
    local = (queries[0], key_rows[0], value_rows[0])
    local_cotangent = cotangent[0]
    tokens, width = local[0].shape
    total_heads = width // HD
    local_heads = total_heads // ctx
    rows_per_device = out_weight.shape[0]
    strided = rows_per_device == HD and local_heads == dp and ctx % 2 == 0

    if strided:
        me = lax.axis_index("dp")
        got = [out_weight] + [
            lax.ppermute(out_weight, "dp", [(a, (a + s) % dp) for a in range(dp)])
            for s in range(1, dp)
        ]
        order = (me - jnp.arange(dp)) % dp
        spread = jnp.stack(got)
        head_weight = jnp.concatenate(
            [lax.dynamic_index_in_dim(spread, order[c], 0, keepdims=False) for c in range(dp)]
        )
        j = lax.axis_index("context")
        shifts = list(range(0, ctx, 2))
        mine = jnp.stack([local_cotangent] + [
            lax.ppermute(local_cotangent, "context", [(a, (a + s) % ctx) for a in range(ctx)])
            for s in shifts[1:]
        ])
        other = lax.ppermute(mine, "context", [(a, a ^ 1) for a in range(ctx)])
        gathered = jnp.concatenate([mine, other]).reshape(ctx * tokens, -1)
        upstream = lax.dot_general(
            gathered, head_weight, (((1,), (1,)), ((), ())),
            preferred_element_type=jnp.float32,
        ).astype(jnp.bfloat16)
        source = jnp.arange(ctx)
        same = source % 2 == j % 2
        position = jnp.where(
            same, ((j - source) % ctx) // 2, ctx // 2 + (((j ^ 1) - source) % ctx) // 2
        )
        positions = position.astype(jnp.int32)

        def chunk(array):
            return array.reshape(tokens, dp, ctx, HD).transpose(2, 1, 0, 3)
    else:
        upstream = lax.dot_general(
            local_cotangent,
            lax.all_gather(out_weight, ("dp", "context"), axis=0, tiled=True),
            (((1,), (1,)), ((), ())),
            preferred_element_type=jnp.float32,
        ).astype(jnp.bfloat16)
        local = local + (upstream,)
        positions = jnp.arange(ctx, dtype=jnp.int32)

        def chunk(array):
            return array.reshape(tokens, ctx, local_heads, HD).transpose(1, 2, 0, 3)

    stacked = jnp.stack([chunk(array) for array in local], axis=1)
    moved = lax.all_to_all(stacked, "context", split_axis=0, concat_axis=0, tiled=True)
    if not strided:
        head_upstream = moved[:, 3].transpose(1, 0, 2, 3).reshape(local_heads, tokens * ctx, HD)
        moved = moved[:, :3]
    pieces = []
    for c in range(local_heads):
        if strided:
            grads = attention_grads(moved, upstream, c, positions, random_blocks[0])
        else:
            grads = attention_grads(moved, head_upstream[c], 0, positions, random_blocks[0])
        back = lax.all_to_all(grads, "context", split_axis=0, concat_axis=0, tiled=True)
        pieces.append(back if strided else back.transpose(1, 2, 0, 3))

    if strided:
        return assemble(pieces, tokens, width)
    outs = []
    for g in range(3):
        joined = jnp.stack([piece[g] for piece in pieces], axis=1 if strided else 2)
        outs.append(joined.reshape(1, tokens, width))
    return tuple(outs)


def solution(mesh):
    return jax.shard_map(
        body,
        mesh=mesh,
        in_specs=(
            P("dp", "context", None),
            P("dp", "context", None),
            P("dp", "context", None),
            P("dp", "context", None),
            P(("dp", "context"), None),
            P("dp", None, None),
        ),
        out_specs=(P("dp", "context", None), P("dp", "context", None), P("dp", "context", None)),
        check_vma=False,
    )
```

```python
import functools
import math

import jax
import jax.numpy as jnp
from jax import lax
from jax.experimental import pallas as pl
from jax.experimental.pallas import tpu as pltpu
from jax.sharding import PartitionSpec as P

HD = 128
BLOCK = 64
RAND = 3
SLOTS = 5 + RAND


def _nt(a, b):
    return lax.dot_general(a, b, (((1,), (1,)), ((), ())), preferred_element_type=jnp.float32)


def _tn(a, b):
    return lax.dot_general(a, b, (((0,), (0,)), ((), ())), preferred_element_type=jnp.float32)


def _nn(a, b):
    return lax.dot_general(a, b, (((1,), (0,)), ((), ())), preferred_element_type=jnp.float32)


def _attention_kernel(rb_ref, pos_ref, x_ref, u_ref, o_ref, dk_acc, dv_acc, kg_ref, vg_ref):
    parts, _, tokens, _ = x_ref.shape
    per_part = tokens // BLOCK
    length = parts * tokens
    count = length // BLOCK
    factor = 1.0 / math.sqrt(HD)

    def rows(ref, which, block):
        if isinstance(block, int):
            offset = (block % per_part) * BLOCK
        else:
            offset = pl.multiple_of((block % per_part) * BLOCK, BLOCK)
        return ref.at[block // per_part, which, pl.ds(offset, BLOCK), :]

    def upstream_rows(block):
        offset = pos_ref[block // per_part] * tokens + (block % per_part) * BLOCK
        return u_ref[pl.ds(pl.multiple_of(offset, BLOCK), BLOCK), :]

    def softmax_grads(qb, ub, keys, values, mask):
        scores = _nt(qb, keys) * factor
        if mask is not None:
            scores = jnp.where(mask, -1e30, scores)
        top = jnp.max(scores, axis=1, keepdims=True)
        expo = jnp.exp(scores - top)
        weights = expo * (1.0 / jnp.sum(expo, axis=1, keepdims=True))
        rounded = weights.astype(jnp.bfloat16)
        attended = _nn(rounded, values)
        row = jnp.sum(ub.astype(jnp.float32) * attended, axis=1, keepdims=True)
        grad_probs = _nt(ub, values)
        grad_scores = (weights * (grad_probs - row) * factor).astype(jnp.bfloat16)
        query_grad = _nn(grad_scores, keys)
        key_grad = _tn(grad_scores, qb)
        value_grad = _tn(rounded, ub)
        return query_grad, key_grad, value_grad

    keys_all = x_ref[:, 1, :, :].reshape(length, HD)
    values_all = x_ref[:, 2, :, :].reshape(length, HD)
    last = count - 1
    qb = jnp.concatenate([rows(x_ref, 0, 0)[...], rows(x_ref, 0, last)[...]], axis=0)
    ub = jnp.concatenate([upstream_rows(0), upstream_rows(last)], axis=0)
    query_grad, key_grad, value_grad = softmax_grads(qb, ub, keys_all, values_all, None)
    query_grad = query_grad.astype(jnp.bfloat16)
    rows(o_ref, 0, 0)[...] = query_grad[:BLOCK]
    rows(o_ref, 0, last)[...] = query_grad[BLOCK:]
    dk_acc[...] = key_grad
    dv_acc[...] = value_grad

    columns = lax.broadcasted_iota(jnp.int32, (BLOCK, SLOTS * BLOCK), 1) // BLOCK
    for slot, block in enumerate((0, last)):
        kg_ref[slot * BLOCK:(slot + 1) * BLOCK, :] = rows(x_ref, 1, block)[...]
        vg_ref[slot * BLOCK:(slot + 1) * BLOCK, :] = rows(x_ref, 2, block)[...]

    def mid_step(m, carry):
        base = (m - 1) * RAND
        lower = jnp.where(m - 1 >= 1, m - 1, m)
        upper = jnp.where(m + 1 <= count - 2, m + 1, m)
        ids = [0, count - 1, lower, m, upper] + [rb_ref[base + r] for r in range(RAND)]
        for slot, block in enumerate(ids[2:], start=2):
            kg_ref[slot * BLOCK:(slot + 1) * BLOCK, :] = rows(x_ref, 1, block)[...]
            vg_ref[slot * BLOCK:(slot + 1) * BLOCK, :] = rows(x_ref, 2, block)[...]
        start = pl.multiple_of(m * BLOCK, BLOCK)
        qb = rows(x_ref, 0, m)[...]
        ub = upstream_rows(m)
        mask = ((columns == 2) & (m == 1)) | ((columns == 4) & (m == count - 2))
        query_grad, key_grad, value_grad = softmax_grads(qb, ub, kg_ref[...], vg_ref[...], mask)
        rows(o_ref, 0, m)[...] = query_grad.astype(jnp.bfloat16)
        for slot, block in enumerate(ids):
            row = pl.multiple_of(block * BLOCK, BLOCK)
            dk_acc[pl.ds(row, BLOCK), :] += key_grad[slot * BLOCK:(slot + 1) * BLOCK, :]
            dv_acc[pl.ds(row, BLOCK), :] += value_grad[slot * BLOCK:(slot + 1) * BLOCK, :]
        return carry

    lax.fori_loop(1, count - 1, mid_step, 0, unroll=14)
    o_ref[:, 1, :, :] = dk_acc[...].reshape(parts, tokens, HD).astype(jnp.bfloat16)
    o_ref[:, 2, :, :] = dv_acc[...].reshape(parts, tokens, HD).astype(jnp.bfloat16)


def attention_grads(stacked, upstream, head, positions, random_ids):
    parts, _, _, tokens, _ = stacked.shape
    length = parts * tokens
    count = length // BLOCK
    source = pl.BlockSpec((parts, 3, None, tokens, HD), lambda h, rb, ps: (0, 0, head, 0, 0))
    whole = pl.BlockSpec((parts, 3, tokens, HD), lambda h, rb, ps: (0, 0, 0, 0))
    spec = pl.BlockSpec((length, HD), lambda h, rb, ps: (0, head))
    out = jax.ShapeDtypeStruct((parts, 3, tokens, HD), jnp.bfloat16)
    pairs = 2 * BLOCK * length + (count - 2) * BLOCK * SLOTS * BLOCK
    cost = pl.CostEstimate(
        flops=12 * pairs * HD, transcendentals=pairs, bytes_accessed=14 * length * HD
    )
    return pl.pallas_call(
        _attention_kernel,
        out_shape=out,
        grid_spec=pltpu.PrefetchScalarGridSpec(
            num_scalar_prefetch=2,
            grid=(1,),
            in_specs=[source, spec],
            out_specs=whole,
            scratch_shapes=[
                pltpu.VMEM((length, HD), jnp.float32),
                pltpu.VMEM((length, HD), jnp.float32),
                pltpu.VMEM((SLOTS * BLOCK, HD), jnp.bfloat16),
                pltpu.VMEM((SLOTS * BLOCK, HD), jnp.bfloat16),
            ],
        ),
        compiler_params=pltpu.CompilerParams(dimension_semantics=("arbitrary",)),
        cost_estimate=cost,
    )(random_ids.reshape(-1), positions, stacked, upstream)


def _assemble_kernel(*refs, first_head):
    pieces, outs = refs[:-3], refs[-3:]
    parts = pieces[0].shape[0]
    for c, piece in enumerate(pieces):
        for source in range(parts):
            start = (c * parts + source) * HD
            for g, out in enumerate(outs):
                out[0, :, start:start + HD] = piece[source, g]


def assemble(pieces, tokens, width):
    out = jax.ShapeDtypeStruct((1, tokens, width), jnp.bfloat16)
    span = pieces[0].shape[0] * HD
    early = len(pieces) - 1
    whole = pl.BlockSpec(memory_space=pltpu.VMEM)
    head_spec = pl.BlockSpec((1, tokens, early * span), lambda i: (0, 0, 0))
    partial = pl.pallas_call(
        functools.partial(_assemble_kernel, first_head=0),
        out_shape=(out, out, out),
        grid=(1,),
        in_specs=[whole] * early,
        out_specs=(head_spec, head_spec, head_spec),
    )(*pieces[:early])
    last_spec = pl.BlockSpec((1, tokens, span), lambda i: (0, 0, early))
    return pl.pallas_call(
        _assemble_last_kernel,
        out_shape=(out, out, out),
        grid=(1,),
        in_specs=[whole] + [pl.BlockSpec(memory_space=pl.ANY)] * 3,
        out_specs=(last_spec, last_spec, last_spec),
        input_output_aliases={1: 0, 2: 1, 3: 2},
    )(pieces[early], *partial)


def _assemble_last_kernel(piece, _first, _second, _third, *outs):
    parts = piece.shape[0]
    for source in range(parts):
        for g, out in enumerate(outs):
            out[0, :, source * HD:(source + 1) * HD] = piece[source, g]


def body(queries, key_rows, value_rows, cotangent, out_weight, random_blocks):
    dp = lax.axis_size("dp")
    ctx = lax.axis_size("context")
    local = (queries[0], key_rows[0], value_rows[0])
    local_cotangent = cotangent[0]
    tokens, width = local[0].shape
    total_heads = width // HD
    local_heads = total_heads // ctx
    rows_per_device = out_weight.shape[0]
    strided = rows_per_device == HD and local_heads == dp and ctx % 2 == 0

    if strided:
        me = lax.axis_index("dp")
        got = [out_weight] + [
            lax.ppermute(out_weight, "dp", [(a, (a + s) % dp) for a in range(dp)])
            for s in range(1, dp)
        ]
        order = (me - jnp.arange(dp)) % dp
        spread = jnp.stack(got)
        head_weight = jnp.concatenate(
            [lax.dynamic_index_in_dim(spread, order[c], 0, keepdims=False) for c in range(dp)]
        )
        j = lax.axis_index("context")
        shifts = list(range(0, ctx, 2))
        mine = jnp.stack([local_cotangent] + [
            lax.ppermute(local_cotangent, "context", [(a, (a + s) % ctx) for a in range(ctx)])
            for s in shifts[1:]
        ])
        other = lax.ppermute(mine, "context", [(a, a ^ 1) for a in range(ctx)])
        gathered = jnp.concatenate([mine, other]).reshape(ctx * tokens, -1)
        upstream = lax.dot_general(
            gathered, head_weight, (((1,), (1,)), ((), ())),
            preferred_element_type=jnp.float32,
        ).astype(jnp.bfloat16)
        source = jnp.arange(ctx)
        same = source % 2 == j % 2
        position = jnp.where(
            same, ((j - source) % ctx) // 2, ctx // 2 + (((j ^ 1) - source) % ctx) // 2
        )
        positions = position.astype(jnp.int32)

        def chunk(array):
            return array.reshape(tokens, dp, ctx, HD).transpose(2, 1, 0, 3)
    else:
        upstream = lax.dot_general(
            local_cotangent,
            lax.all_gather(out_weight, ("dp", "context"), axis=0, tiled=True),
            (((1,), (1,)), ((), ())),
            preferred_element_type=jnp.float32,
        ).astype(jnp.bfloat16)
        local = local + (upstream,)
        positions = jnp.arange(ctx, dtype=jnp.int32)

        def chunk(array):
            return array.reshape(tokens, ctx, local_heads, HD).transpose(1, 2, 0, 3)

    stacked = jnp.stack([chunk(array) for array in local], axis=1)
    moved = lax.all_to_all(stacked, "context", split_axis=0, concat_axis=0, tiled=True)
    if not strided:
        head_upstream = moved[:, 3].transpose(1, 0, 2, 3).reshape(local_heads, tokens * ctx, HD)
        moved = moved[:, :3]
    pieces = []
    for c in range(local_heads):
        if strided:
            grads = attention_grads(moved, upstream, c, positions, random_blocks[0])
        else:
            grads = attention_grads(moved, head_upstream[c], 0, positions, random_blocks[0])
        back = lax.all_to_all(grads, "context", split_axis=0, concat_axis=0, tiled=True)
        pieces.append(back if strided else back.transpose(1, 2, 0, 3))

    if strided:
        return assemble(pieces, tokens, width)
    outs = []
    for g in range(3):
        joined = jnp.stack([piece[g] for piece in pieces], axis=1 if strided else 2)
        outs.append(joined.reshape(1, tokens, width))
    return tuple(outs)


def solution(mesh):
    return jax.shard_map(
        body,
        mesh=mesh,
        in_specs=(
            P("dp", "context", None),
            P("dp", "context", None),
            P("dp", "context", None),
            P("dp", "context", None),
            P(("dp", "context"), None),
            P("dp", None, None),
        ),
        out_specs=(P("dp", "context", None), P("dp", "context", None), P("dp", "context", None)),
        check_vma=False,
    )
```
